32 devices in a mesh: row: 4 (over z), col: 8 (over y, x, core).
Axes of the slice: x: 2, y: 2, z: 4, core: 2. Of those that a mesh axis runs over, the one named last changes fastest.
Arguments:
- positions: float32 [3, 4, 8, 64], P(None, 'row', 'col'), may hold values from 0 to 32, as said below
- species: int32 [4, 8, 64], P('row', 'col'), may hold values from 0 to 3
- descriptors: float32 [128, 4, 8, 64], P(None, 'row', 'col'), may hold values from -6 to 6
- readout: float32 [4, 128], replicated, may hold values from -0.5 to 0.5
- hardness: float32 [4], replicated, may hold values from 1 to 4
- widths: float32 [4], replicated, may hold values from 0.5 to 1.5
Outputs:
- charges: float32 [4, 8, 64], P('row', 'col')
- forces: float32 [3, 4, 8, 64], P(None, 'row', 'col')
The draws below stay inside these ranges and needn't reach their ends.
Inputs may be any that keep to these rules, and one draw needn't show every extreme that they name: `positions`: the atoms of brick (b, c) lie in [4 b, 4 b + 4) x [4 c, 4 c + 4) x [0, 4); no two atoms are closer than 0.4.
All inputs are finite; a program needn't handle non-finite values.
Results may differ from the reference program's by a relative error of at most 0.0003.
Values sent between devices are 32-bit elements; how exact they have to be, the bound alone decides.
No kernel may reach another device: no remote copies, remote signals or barrier semaphores. Data moves between devices by JAX's collectives and lax.ppermute only.
A program may use at most 64 MiB of HBM per device.

```python
import math
import jax
import jax.numpy as jnp
from jax import lax

A_DEV = 64
FEAT = 128
ITERS = 3
NSPEC = 4
BX = 4
BY = 8


def draw_positions(key, part):
    sites = jnp.arange(A_DEV, dtype=jnp.int32)
    cell_x = (sites % 4).astype(jnp.float32)
    cell_y = (sites // 4 % 4).astype(jnp.float32)
    cell_z = (sites // 16).astype(jnp.float32)
    brick_x = jnp.arange(BX, dtype=jnp.int32).astype(jnp.float32) * 4.0
    brick_y = jnp.arange(BY, dtype=jnp.int32).astype(jnp.float32) * 4.0
    zeros_grid = jnp.zeros((BX, BY, A_DEV), jnp.float32)
    base_x = zeros_grid + brick_x[:, None, None] + cell_x[None, None, :]
    base_y = zeros_grid + brick_y[None, :, None] + cell_y[None, None, :]
    base_z = zeros_grid + cell_z[None, None, :]
    lattice = jnp.stack([base_x, base_y, base_z]) + 0.5
    jitter = jax.random.uniform(key, (3, BX, BY, A_DEV), jnp.float32, -0.3, 0.3)
    return lattice + jitter


def set_ends(array, key, least, top_value):
    shape = array.shape
    spot = [jax.random.randint(jax.random.fold_in(key, axis), (), 0, shape[axis]) for axis in range(len(shape))]
    array = array.at[tuple(spot)].set(least)
    longest = shape.index(max(shape))
    spot[longest] = (spot[longest] + 1) % shape[longest]
    return array.at[tuple(spot)].set(top_value)


def levels(key, extent, shards, low, high):
    loudness = 1.0
    for axis_at, shards_of in shards:
        heights = jax.random.uniform(jax.random.fold_in(jax.random.fold_in(key, 6), axis_at), (shards_of,), jnp.float32, low / len(shards), high / len(shards))
        loudness = loudness * jnp.repeat(jnp.exp(heights), extent[axis_at] // shards_of).reshape((-1,) + (1,) * (len(extent) - 1 - axis_at))
    return loudness


def gaussian(own_key, dims, width, limit, cuts=(), kind=jnp.bfloat16):
    level = levels(own_key, dims, cuts, -0.22, 0.18) if cuts else 1.0
    array = jax.random.normal(own_key, dims, jnp.float32) * width * level
    return jnp.minimum(jnp.maximum(array, -limit), limit).astype(kind)


def setup_inputs(seed: int = 0) -> dict:
    key_list = jax.random.split(jax.random.key(seed), 7)
    positions = draw_positions(jax.random.fold_in(key_list[6], 71), 0)
    species = set_ends(jax.random.randint(key_list[1], (BX, BY, A_DEV), 0, NSPEC), jax.random.fold_in(key_list[1], 1), 0, NSPEC - 1).astype(jnp.int32)
    descriptors = gaussian(key_list[2], (FEAT, BX, BY, A_DEV), 1.0, 6.0, ((1, 4), (2, 8)), jnp.float32)
    readout = gaussian(key_list[3], (NSPEC, FEAT), FEAT ** -0.5, 0.5, (), jnp.float32)
    hardness = jnp.clip(jnp.exp(jax.random.uniform(key_list[4], (NSPEC,), jnp.float32, math.log(1.0), math.log(4.0))), 1.0, 4.0)
    widths = jnp.clip(jnp.exp(jax.random.uniform(key_list[5], (NSPEC,), jnp.float32, math.log(0.5), math.log(1.5))), 0.5, 1.5)
    return {"positions": positions, "species": species, "descriptors": descriptors, "readout": readout, "hardness": hardness, "widths": widths}


ROOT_PI = 1.7724538509055159
TWO_ROOT = 1.1283791670955126

def screened(row_geometry, col_geometry, self_pair):
    squared = jnp.zeros(self_pair.shape, row_geometry.dtype)
    for axis_id in range(3):
        separation = row_geometry[axis_id][:, None] - col_geometry[axis_id][None, :]
        squared = squared + separation * separation
    squared = jnp.where(self_pair, 1.0, squared)
    inverse = lax.rsqrt(squared)
    screening = lax.rsqrt(2.0 * (row_geometry[3][:, None] + col_geometry[3][None, :]))
    return jnp.where(self_pair, 0.0, lax.erf(screening * squared * inverse) * inverse)

def pulling(row_geometry, col_geometry, self_pair, col_charges):
    separations = []
    squared = jnp.zeros(self_pair.shape, row_geometry.dtype)
    for axis_id in range(3):
        separation = row_geometry[axis_id][:, None] - col_geometry[axis_id][None, :]
        separations.append(separation)
        squared = squared + separation * separation
    squared = jnp.where(self_pair, 1.0, squared)
    inverse = lax.rsqrt(squared)
    screening = lax.rsqrt(2.0 * (row_geometry[3][:, None] + col_geometry[3][None, :]))
    slope = (lax.erf(screening * squared * inverse) * inverse - TWO_ROOT * screening * jnp.exp(-screening * screening * squared)) * inverse * inverse
    slope = jnp.where(self_pair, 0.0, slope) * col_charges[None, :]
    return jnp.stack([lax.optimization_barrier(jnp.sum(slope * separations[0], 1)), lax.optimization_barrier(jnp.sum(slope * separations[1], 1)), lax.optimization_barrier(jnp.sum(slope * separations[2], 1))])

def reference(positions, species, descriptors, readout, hardness, widths):
    atom_count = species.size
    coords = positions.reshape(3, atom_count)
    kind_range = jnp.arange(hardness.shape[0], dtype=jnp.int32)
    onehot = (kind_range[:, None] == species.reshape(1, atom_count)).astype(jnp.float32)
    hard_atom = lax.optimization_barrier(jnp.sum(onehot * hardness[:, None], 0))
    width_atom = lax.optimization_barrier(jnp.sum(onehot * widths[:, None], 0))
    features = descriptors.reshape(descriptors.shape[0], atom_count)
    atom_weights = jnp.zeros(features.shape, jnp.float32)
    for kind in range(hardness.shape[0]):
        atom_weights = atom_weights + onehot[kind][None, :] * readout[kind][:, None]
    negativity = lax.optimization_barrier(jnp.sum(features * atom_weights, 0))
    self_term = hard_atom + 1.0 / (width_atom * ROOT_PI)
    geometry = jnp.concatenate([coords, (width_atom * width_atom)[None, :]], 0)
    block_rows = 512
    block_count = atom_count // block_rows
    col_index = jnp.arange(atom_count, dtype=jnp.int32)

    def sweep(block_fn, operand, rows_out):

        def one_block(block):
            first_row = block * block_rows
            row_geometry = lax.dynamic_slice_in_dim(geometry, first_row, block_rows, 1)
            row_index = first_row + jnp.arange(block_rows, dtype=jnp.int32)
            return block_fn(row_geometry, geometry, row_index[:, None] == col_index[None, :], operand)
        blocks = lax.map(one_block, jnp.arange(block_count, dtype=jnp.int32))
        return jnp.moveaxis(blocks, 0, 1).reshape(rows_out, atom_count)

    def apply_kernel(row_geometry, col_geometry, self_pair, vectors):
        kernel = screened(row_geometry, col_geometry, self_pair)
        return lax.optimization_barrier(jnp.sum(kernel[None, :, :] * vectors[:, None, :], 2))

    def operate(vectors):
        return sweep(apply_kernel, vectors, 2) + self_term[None, :] * vectors
    rhs = jnp.stack([-negativity, jnp.ones((atom_count,), jnp.float32)])
    solution = jnp.zeros_like(rhs)
    resid = rhs
    direction = rhs
    norm_now = lax.optimization_barrier(jnp.sum(resid * resid, 1))
    for iteration in range(ITERS):
        image = operate(direction)
        step_size = norm_now / lax.optimization_barrier(jnp.sum(direction * image, 1))
        solution = solution + step_size[:, None] * direction
        resid = resid - step_size[:, None] * image
        norm_next = lax.optimization_barrier(jnp.sum(resid * resid, 1))
        direction = resid + (norm_next / norm_now)[:, None] * direction
        norm_now = norm_next
    totals = lax.optimization_barrier(jnp.sum(solution, 1))
    lagrange = totals[0] / totals[1]
    charges = solution[0] - lagrange * solution[1]
    field_sums = sweep(pulling, charges, 3)
    forces = charges[None, :] * field_sums
    return (charges.reshape(species.shape), forces.reshape(positions.shape))
```

```python
import jax
import jax.numpy as jnp
from jax import lax
from jax.sharding import PartitionSpec as P

ITERS = 3


ROOT_PI = 1.7724538509055159
TWO_ROOT = 1.1283791670955126

PAIR_LIMIT = 16 * 1024 * 1024


def screened(row_geometry, col_geometry, self_pair):
    squared = jnp.zeros(self_pair.shape, row_geometry.dtype)
    for axis_id in range(3):
        separation = row_geometry[axis_id][:, None] - col_geometry[axis_id][None, :]
        squared = squared + separation * separation
    squared = jnp.where(self_pair, 1.0, squared)
    inverse = lax.rsqrt(squared)
    screening = lax.rsqrt(2.0 * (row_geometry[3][:, None] + col_geometry[3][None, :]))
    off = lax.erf(screening * squared * inverse) * inverse
    return jnp.where(self_pair, row_geometry[5][:, None], off)


def pulling(row_geometry, col_geometry, self_pair, col_charges):
    separations = []
    squared = jnp.zeros(self_pair.shape, row_geometry.dtype)
    for axis_id in range(3):
        separation = row_geometry[axis_id][:, None] - col_geometry[axis_id][None, :]
        separations.append(separation)
        squared = squared + separation * separation
    squared = jnp.where(self_pair, 1.0, squared)
    inverse = lax.rsqrt(squared)
    screening = lax.rsqrt(2.0 * (row_geometry[3][:, None] + col_geometry[3][None, :]))
    slope = (
        (
            lax.erf(screening * squared * inverse) * inverse
            - TWO_ROOT * screening * jnp.exp(-screening * screening * squared)
        )
        * inverse
        * inverse
    )
    slope = jnp.where(self_pair, 0.0, slope) * col_charges[None, :]
    return jnp.stack(
        [
            jnp.sum(slope * separations[0], 1),
            jnp.sum(slope * separations[1], 1),
            jnp.sum(slope * separations[2], 1),
        ]
    )


def make_shards(rows, cols):
    devices = rows * cols
    everyone = ("row", "col")

    def gather_all(piece):
        spread = jnp.broadcast_to(piece[None], (devices,) + piece.shape)
        got = lax.all_to_all(spread, everyone, 0, 0, tiled=True)
        return jnp.moveaxis(got, 0, 1).reshape(piece.shape[0], -1)

    def shards(positions, species, descriptors, readout, hardness, widths):
        per_brick = species.shape[-1]
        atoms = devices * per_brick
        me = lax.axis_index("row") * cols + lax.axis_index("col")
        kind_range = jnp.arange(hardness.shape[0], dtype=jnp.int32)
        onehot = (kind_range[:, None] == species.reshape(1, per_brick)).astype(jnp.float32)
        hard_atom = jnp.sum(onehot * hardness[:, None], 0)
        width_atom = jnp.sum(onehot * widths[:, None], 0)
        features = descriptors.reshape(descriptors.shape[0], per_brick)
        atom_weights = jnp.zeros(features.shape, jnp.float32)
        for kind in range(hardness.shape[0]):
            atom_weights = atom_weights + onehot[kind][None, :] * readout[kind][:, None]
        negativity = jnp.sum(features * atom_weights, 0)
        self_term = hard_atom + 1.0 / (width_atom * ROOT_PI)
        own = jnp.concatenate(
            [
                positions.reshape(3, per_brick),
                (width_atom * width_atom)[None],
                negativity[None],
                self_term[None],
            ],
            0,
        )
        geometry = gather_all(own)
        col_index = jnp.arange(atoms, dtype=jnp.int32)

        pair = devices % 2 == 0 and (atoms // 2) * atoms * 4 <= PAIR_LIMIT
        if pair:
            parity = me % 2
            halves = devices // 2
            row_geometry = lax.dynamic_index_in_dim(
                geometry.reshape(6, halves, 2, per_brick), parity, 2, keepdims=False
            ).reshape(6, -1)
            brick_of = 2 * jnp.arange(halves, dtype=jnp.int32) + parity
            row_index = (brick_of[:, None] * per_brick + jnp.arange(per_brick, dtype=jnp.int32)[None]).reshape(-1)
            partner = [(i, i ^ 1) for i in range(devices)]

            def pick_rows(vectors):
                return lax.dynamic_index_in_dim(
                    vectors.reshape(2, halves, 2, per_brick), parity, 2, keepdims=False
                ).reshape(2, -1)

            def assemble(mine):
                theirs = lax.ppermute(mine, everyone, partner)
                first = jnp.where(parity == 0, mine, theirs).reshape(2, halves, per_brick)
                second = jnp.where(parity == 0, theirs, mine).reshape(2, halves, per_brick)
                return jnp.stack([first, second], 2).reshape(2, atoms)
        else:
            row_geometry = own
            row_index = me * per_brick + jnp.arange(per_brick, dtype=jnp.int32)

            def assemble(mine):
                return gather_all(mine.reshape(2, per_brick))

        matrix = screened(row_geometry, geometry, row_index[:, None] == col_index[None, :])

        def operate(vectors):
            return assemble(jnp.sum(matrix[None, :, :] * vectors[:, None, :], 2))

        rhs = jnp.stack([-geometry[4], jnp.ones((atoms,), jnp.float32)])
        solution = jnp.zeros_like(rhs)
        resid = rhs
        direction = rhs
        norm_now = jnp.sum(resid * resid, 1)
        for iteration in range(ITERS):
            image = operate(direction)
            step_size = norm_now / jnp.sum(direction * image, 1)
            solution = solution + step_size[:, None] * direction
            if iteration + 1 < ITERS:
                resid = resid - step_size[:, None] * image
                norm_next = jnp.sum(resid * resid, 1)
                direction = resid + (norm_next / norm_now)[:, None] * direction
                norm_now = norm_next
        totals = jnp.sum(solution, 1)
        lagrange = totals[0] / totals[1]
        charges = solution[0] - lagrange * solution[1]
        own_index = me * per_brick + jnp.arange(per_brick, dtype=jnp.int32)
        own_charges = lax.dynamic_slice_in_dim(charges, me * per_brick, per_brick, 0)
        field = pulling(own, geometry, own_index[:, None] == col_index[None, :], charges)
        forces = (own_charges[None, :] * field).reshape(3, 1, 1, per_brick)
        return (own_charges.reshape(1, 1, per_brick), forces)

    return shards


def solution(mesh):
    in_specs = (
        P(None, "row", "col", None),
        P("row", "col", None),
        P(None, "row", "col", None),
        P(),
        P(),
        P(),
    )
    out_specs = (P("row", "col", None), P(None, "row", "col", None))
    shards = make_shards(mesh.shape["row"], mesh.shape["col"])
    return jax.shard_map(shards, mesh=mesh, in_specs=in_specs, out_specs=out_specs, check_vma=False)
```

```python
import jax
import jax.numpy as jnp
from jax import lax
from jax.sharding import PartitionSpec as P
from jax.experimental import pallas as pl
from jax.experimental.pallas import tpu as pltpu

ITERS = 3


ROOT_PI = 1.7724538509055159
TWO_ROOT = 1.1283791670955126

PAIR_LIMIT = 16 * 1024 * 1024


def screened(row_geometry, col_geometry, self_pair):
    squared = jnp.zeros(self_pair.shape, row_geometry.dtype)
    for axis_id in range(3):
        separation = row_geometry[axis_id][:, None] - col_geometry[axis_id][None, :]
        squared = squared + separation * separation
    squared = jnp.where(self_pair, 1.0, squared)
    inverse = lax.rsqrt(squared)
    screening = lax.rsqrt(2.0 * (row_geometry[3][:, None] + col_geometry[3][None, :]))
    off = lax.erf(screening * squared * inverse) * inverse
    return jnp.where(self_pair, row_geometry[5][:, None], off)


def pulling(row_geometry, col_geometry, self_pair, col_charges):
    separations = []
    squared = jnp.zeros(self_pair.shape, row_geometry.dtype)
    for axis_id in range(3):
        separation = row_geometry[axis_id][:, None] - col_geometry[axis_id][None, :]
        separations.append(separation)
        squared = squared + separation * separation
    squared = jnp.where(self_pair, 1.0, squared)
    inverse = lax.rsqrt(squared)
    screening = lax.rsqrt(2.0 * (row_geometry[3][:, None] + col_geometry[3][None, :]))
    slope = (
        (
            lax.erf(screening * squared * inverse) * inverse
            - TWO_ROOT * screening * jnp.exp(-screening * screening * squared)
        )
        * inverse
        * inverse
    )
    slope = jnp.where(self_pair, 0.0, slope) * col_charges[None, :]
    return jnp.stack(
        [
            jnp.sum(slope * separations[0], 1),
            jnp.sum(slope * separations[1], 1),
            jnp.sum(slope * separations[2], 1),
        ]
    )


MATRIX_ROWS = 32
STREAM_ROWS = 128


def matrix_kernel(rows_ref, cols_ref, vec_ref, matrix_ref, image_ref):
    rows = rows_ref[...]
    cols = cols_ref[...]
    squared = jnp.zeros((rows.shape[0], cols.shape[1]), jnp.float32)
    for axis_id in range(3):
        separation = rows[:, axis_id : axis_id + 1] - cols[axis_id : axis_id + 1, :]
        squared = squared + separation * separation
    self_pair = rows[:, 5:6] == cols[5:6, :]
    squared = jnp.where(self_pair, 1.0, squared)
    inverse = lax.rsqrt(squared)
    screening = lax.rsqrt(2.0 * (rows[:, 3:4] + cols[3:4, :]))
    off = lax.erf(screening * squared * inverse) * inverse
    matrix = jnp.where(self_pair, rows[:, 4:5], off)
    matrix_ref[...] = matrix
    vec = vec_ref[...]
    image_ref[...] = jnp.concatenate(
        [
            jnp.sum(matrix * vec[0:1, :], 1, keepdims=True),
            jnp.sum(matrix * vec[1:2, :], 1, keepdims=True),
        ],
        1,
    )


def stream_kernel(matrix_ref, vec_ref, image_ref):
    matrix = matrix_ref[...]
    vec = vec_ref[...]
    image_ref[...] = jnp.concatenate(
        [
            jnp.sum(matrix * vec[0:1, :], 1, keepdims=True),
            jnp.sum(matrix * vec[1:2, :], 1, keepdims=True),
        ],
        1,
    )


def build_matrix(rows_t, cols, vec):
    count, width = rows_t.shape[0], cols.shape[1]
    return pl.pallas_call(
        matrix_kernel,
        grid=(count // MATRIX_ROWS,),
        in_specs=[
            pl.BlockSpec((MATRIX_ROWS, 8), lambda i: (i, 0)),
            pl.BlockSpec((8, width), lambda i: (0, 0)),
            pl.BlockSpec((2, width), lambda i: (0, 0)),
        ],
        out_specs=[
            pl.BlockSpec((MATRIX_ROWS, width), lambda i: (i, 0)),
            pl.BlockSpec((MATRIX_ROWS, 2), lambda i: (i, 0)),
        ],
        out_shape=[
            jax.ShapeDtypeStruct((count, width), jnp.float32),
            jax.ShapeDtypeStruct((count, 2), jnp.float32),
        ],
    )(rows_t, cols, vec)


def stream_matrix(matrix, vec):
    count, width = matrix.shape
    return pl.pallas_call(
        stream_kernel,
        grid=(count // STREAM_ROWS,),
        in_specs=[
            pl.BlockSpec((STREAM_ROWS, width), lambda i: (i, 0)),
            pl.BlockSpec((2, width), lambda i: (0, 0)),
        ],
        out_specs=pl.BlockSpec((STREAM_ROWS, 2), lambda i: (i, 0)),
        out_shape=jax.ShapeDtypeStruct((count, 2), jnp.float32),
    )(matrix, vec)


def make_shards(rows, cols):
    devices = rows * cols
    everyone = ("row", "col")

    def gather_all(piece):
        spread = jnp.broadcast_to(piece[None], (devices,) + piece.shape)
        got = lax.all_to_all(spread, everyone, 0, 0, tiled=True)
        return jnp.moveaxis(got, 0, 1).reshape(piece.shape[0], -1)

    def shards(positions, species, descriptors, readout, hardness, widths):
        per_brick = species.shape[-1]
        atoms = devices * per_brick
        me = lax.axis_index("row") * cols + lax.axis_index("col")
        kind_range = jnp.arange(hardness.shape[0], dtype=jnp.int32)
        onehot = (kind_range[:, None] == species.reshape(1, per_brick)).astype(jnp.float32)
        hard_atom = jnp.sum(onehot * hardness[:, None], 0)
        width_atom = jnp.sum(onehot * widths[:, None], 0)
        features = descriptors.reshape(descriptors.shape[0], per_brick)
        atom_weights = jnp.zeros(features.shape, jnp.float32)
        for kind in range(hardness.shape[0]):
            atom_weights = atom_weights + onehot[kind][None, :] * readout[kind][:, None]
        negativity = jnp.sum(features * atom_weights, 0)
        self_term = hard_atom + 1.0 / (width_atom * ROOT_PI)
        own = jnp.concatenate(
            [
                positions.reshape(3, per_brick),
                (width_atom * width_atom)[None],
                negativity[None],
                self_term[None],
            ],
            0,
        )
        geometry = gather_all(own)
        col_index = jnp.arange(atoms, dtype=jnp.int32)

        pair = devices % 2 == 0 and (atoms // 2) * atoms * 4 <= PAIR_LIMIT
        if pair:
            parity = me % 2
            halves = devices // 2
            row_geometry = lax.dynamic_index_in_dim(
                geometry.reshape(6, halves, 2, per_brick), parity, 2, keepdims=False
            ).reshape(6, -1)
            brick_of = 2 * jnp.arange(halves, dtype=jnp.int32) + parity
            row_index = (brick_of[:, None] * per_brick + jnp.arange(per_brick, dtype=jnp.int32)[None]).reshape(-1)
            partner = [(i, i ^ 1) for i in range(devices)]

            def pick_rows(vectors):
                return lax.dynamic_index_in_dim(
                    vectors.reshape(2, halves, 2, per_brick), parity, 2, keepdims=False
                ).reshape(2, -1)

            def assemble(mine):
                theirs = lax.ppermute(mine, everyone, partner)
                first = jnp.where(parity == 0, mine, theirs).reshape(2, halves, per_brick)
                second = jnp.where(parity == 0, theirs, mine).reshape(2, halves, per_brick)
                return jnp.stack([first, second], 2).reshape(2, atoms)
        else:
            row_geometry = own
            row_index = me * per_brick + jnp.arange(per_brick, dtype=jnp.int32)

            def assemble(mine):
                return gather_all(mine.reshape(2, per_brick))

        rhs = jnp.stack([-geometry[4], jnp.ones((atoms,), jnp.float32)])
        if pair:
            index_row = row_index.astype(jnp.float32)[None]
            rows_t = jnp.concatenate(
                [row_geometry[:4], row_geometry[5:6], index_row, jnp.zeros((2, row_index.shape[0]), jnp.float32)], 0
            ).T
            cols_8 = jnp.concatenate(
                [geometry[:4], jnp.zeros((1, atoms), jnp.float32), col_index.astype(jnp.float32)[None],
                 jnp.zeros((2, atoms), jnp.float32)], 0
            )
            matrix, first_image = build_matrix(rows_t, cols_8, rhs)
            images = [first_image]

            def operate(vectors):
                if images:
                    return assemble(images.pop().T)
                return assemble(stream_matrix(matrix, vectors).T)
        else:
            matrix = screened(row_geometry, geometry, row_index[:, None] == col_index[None, :])

            def operate(vectors):
                return assemble(jnp.sum(matrix[None, :, :] * vectors[:, None, :], 2))

        solution = jnp.zeros_like(rhs)
        resid = rhs
        direction = rhs
        norm_now = jnp.sum(resid * resid, 1)
        for iteration in range(ITERS):
            image = operate(direction)
            step_size = norm_now / jnp.sum(direction * image, 1)
            solution = solution + step_size[:, None] * direction
            if iteration + 1 < ITERS:
                resid = resid - step_size[:, None] * image
                norm_next = jnp.sum(resid * resid, 1)
                direction = resid + (norm_next / norm_now)[:, None] * direction
                norm_now = norm_next
        totals = jnp.sum(solution, 1)
        lagrange = totals[0] / totals[1]
        charges = solution[0] - lagrange * solution[1]
        own_index = me * per_brick + jnp.arange(per_brick, dtype=jnp.int32)
        own_charges = lax.dynamic_slice_in_dim(charges, me * per_brick, per_brick, 0)
        field = pulling(own, geometry, own_index[:, None] == col_index[None, :], charges)
        forces = (own_charges[None, :] * field).reshape(3, 1, 1, per_brick)
        return (own_charges.reshape(1, 1, per_brick), forces)

    return shards


def solution(mesh):
    in_specs = (
        P(None, "row", "col", None),
        P("row", "col", None),
        P(None, "row", "col", None),
        P(),
        P(),
        P(),
    )
    out_specs = (P("row", "col", None), P(None, "row", "col", None))
    shards = make_shards(mesh.shape["row"], mesh.shape["col"])
    return jax.shard_map(shards, mesh=mesh, in_specs=in_specs, out_specs=out_specs, check_vma=False)
```

```python
import jax
import jax.numpy as jnp
from jax import lax
from jax.sharding import PartitionSpec as P

ITERS = 3


ROOT_PI = 1.7724538509055159
TWO_ROOT = 1.1283791670955126

PAIR_LIMIT = 16 * 1024 * 1024
CHUNKS = 4


def screened(row_geometry, col_geometry, self_pair):
    squared = jnp.zeros(self_pair.shape, row_geometry.dtype)
    for axis_id in range(3):
        separation = row_geometry[axis_id][:, None] - col_geometry[axis_id][None, :]
        squared = squared + separation * separation
    squared = jnp.where(self_pair, 1.0, squared)
    inverse = lax.rsqrt(squared)
    screening = lax.rsqrt(2.0 * (row_geometry[3][:, None] + col_geometry[3][None, :]))
    off = lax.erf(screening * squared * inverse) * inverse
    return jnp.where(self_pair, row_geometry[5][:, None], off)


def pulling(row_geometry, col_geometry, self_pair, col_charges):
    separations = []
    squared = jnp.zeros(self_pair.shape, row_geometry.dtype)
    for axis_id in range(3):
        separation = row_geometry[axis_id][:, None] - col_geometry[axis_id][None, :]
        separations.append(separation)
        squared = squared + separation * separation
    squared = jnp.where(self_pair, 1.0, squared)
    inverse = lax.rsqrt(squared)
    screening = lax.rsqrt(2.0 * (row_geometry[3][:, None] + col_geometry[3][None, :]))
    slope = (
        (
            lax.erf(screening * squared * inverse) * inverse
            - TWO_ROOT * screening * jnp.exp(-screening * screening * squared)
        )
        * inverse
        * inverse
    )
    slope = jnp.where(self_pair, 0.0, slope) * col_charges[None, :]
    return jnp.stack(
        [
            jnp.sum(slope * separations[0], 1),
            jnp.sum(slope * separations[1], 1),
            jnp.sum(slope * separations[2], 1),
        ]
    )


def make_shards(rows, cols):
    devices = rows * cols
    everyone = ("row", "col")

    def gather_all(piece):
        spread = jnp.broadcast_to(piece[None], (devices,) + piece.shape)
        got = lax.all_to_all(spread, everyone, 0, 0, tiled=True)
        return jnp.moveaxis(got, 0, 1).reshape(piece.shape[0], -1)

    def shards(positions, species, descriptors, readout, hardness, widths):
        per_brick = species.shape[-1]
        atoms = devices * per_brick
        me = lax.axis_index("row") * cols + lax.axis_index("col")
        kind_range = jnp.arange(hardness.shape[0], dtype=jnp.int32)
        onehot = (kind_range[:, None] == species.reshape(1, per_brick)).astype(jnp.float32)
        hard_atom = jnp.sum(onehot * hardness[:, None], 0)
        width_atom = jnp.sum(onehot * widths[:, None], 0)
        features = descriptors.reshape(descriptors.shape[0], per_brick)
        atom_weights = jnp.zeros(features.shape, jnp.float32)
        for kind in range(hardness.shape[0]):
            atom_weights = atom_weights + onehot[kind][None, :] * readout[kind][:, None]
        negativity = jnp.sum(features * atom_weights, 0)
        self_term = hard_atom + 1.0 / (width_atom * ROOT_PI)
        own = jnp.concatenate(
            [
                positions.reshape(3, per_brick),
                (width_atom * width_atom)[None],
                negativity[None],
                self_term[None],
            ],
            0,
        )
        geometry = gather_all(own)
        col_index = jnp.arange(atoms, dtype=jnp.int32)

        pair = devices % 2 == 0 and (atoms // 2) * atoms * 4 <= PAIR_LIMIT
        if pair:
            parity = me % 2
            halves = devices // 2
            row_geometry = lax.dynamic_index_in_dim(
                geometry.reshape(6, halves, 2, per_brick), parity, 2, keepdims=False
            ).reshape(6, -1)
            brick_of = 2 * jnp.arange(halves, dtype=jnp.int32) + parity
            row_index = (brick_of[:, None] * per_brick + jnp.arange(per_brick, dtype=jnp.int32)[None]).reshape(-1)
            partner = [(i, i ^ 1) for i in range(devices)]

            def pick_rows(vectors):
                return lax.dynamic_index_in_dim(
                    vectors.reshape(2, halves, 2, per_brick), parity, 2, keepdims=False
                ).reshape(2, -1)

            def assemble(mine):
                theirs = lax.ppermute(mine, everyone, partner)
                first = jnp.where(parity == 0, mine, theirs).reshape(2, halves, per_brick)
                second = jnp.where(parity == 0, theirs, mine).reshape(2, halves, per_brick)
                return jnp.stack([first, second], 2).reshape(2, atoms)
        else:
            row_geometry = own
            row_index = me * per_brick + jnp.arange(per_brick, dtype=jnp.int32)

            def assemble(mine):
                return gather_all(mine.reshape(2, per_brick))

        chunks = CHUNKS if pair and atoms % CHUNKS == 0 else 1
        width = atoms // chunks
        matrices = [
            screened(
                row_geometry,
                geometry[:, c * width : (c + 1) * width],
                row_index[:, None] == col_index[None, c * width : (c + 1) * width],
            )
            for c in range(chunks)
        ]

        def operate(vectors):
            total = 0.0
            for c, matrix in enumerate(matrices):
                part = vectors[:, c * width : (c + 1) * width]
                total = total + jnp.sum(matrix[None, :, :] * part[:, None, :], 2)
            return assemble(total)

        rhs = jnp.stack([-geometry[4], jnp.ones((atoms,), jnp.float32)])
        solution = jnp.zeros_like(rhs)
        resid = rhs
        direction = rhs
        norm_now = jnp.sum(resid * resid, 1)
        for iteration in range(ITERS):
            image = operate(direction)
            step_size = norm_now / jnp.sum(direction * image, 1)
            solution = solution + step_size[:, None] * direction
            if iteration + 1 < ITERS:
                resid = resid - step_size[:, None] * image
                norm_next = jnp.sum(resid * resid, 1)
                direction = resid + (norm_next / norm_now)[:, None] * direction
                norm_now = norm_next
        totals = jnp.sum(solution, 1)
        lagrange = totals[0] / totals[1]
        charges = solution[0] - lagrange * solution[1]
        own_index = me * per_brick + jnp.arange(per_brick, dtype=jnp.int32)
        own_charges = lax.dynamic_slice_in_dim(charges, me * per_brick, per_brick, 0)
        field = pulling(own, geometry, own_index[:, None] == col_index[None, :], charges)
        forces = (own_charges[None, :] * field).reshape(3, 1, 1, per_brick)
        return (own_charges.reshape(1, 1, per_brick), forces)

    return shards


def solution(mesh):
    in_specs = (
        P(None, "row", "col", None),
        P("row", "col", None),
        P(None, "row", "col", None),
        P(),
        P(),
        P(),
    )
    out_specs = (P("row", "col", None), P(None, "row", "col", None))
    shards = make_shards(mesh.shape["row"], mesh.shape["col"])
    return jax.shard_map(shards, mesh=mesh, in_specs=in_specs, out_specs=out_specs, check_vma=False)
```

```python
import jax
import jax.numpy as jnp
from jax import lax
from jax.sharding import PartitionSpec as P

ITERS = 3


ROOT_PI = 1.7724538509055159
TWO_ROOT = 1.1283791670955126

PAIR_LIMIT = 16 * 1024 * 1024
BLOCKS = (
    ((0, 0), (1, 1), (0, 1), (0, 2), (1, 2)),
    ((2, 2), (3, 3), (2, 3), (0, 3), (1, 3)),
)


def screened(row_geometry, col_geometry, self_pair):
    squared = jnp.zeros(self_pair.shape, row_geometry.dtype)
    for axis_id in range(3):
        separation = row_geometry[axis_id][:, None] - col_geometry[axis_id][None, :]
        squared = squared + separation * separation
    squared = jnp.where(self_pair, 1.0, squared)
    inverse = lax.rsqrt(squared)
    screening = lax.rsqrt(2.0 * (row_geometry[3][:, None] + col_geometry[3][None, :]))
    off = lax.erf(screening * squared * inverse) * inverse
    return jnp.where(self_pair, row_geometry[5][:, None], off)


def pulling(row_geometry, col_geometry, self_pair, col_charges):
    separations = []
    squared = jnp.zeros(self_pair.shape, row_geometry.dtype)
    for axis_id in range(3):
        separation = row_geometry[axis_id][:, None] - col_geometry[axis_id][None, :]
        separations.append(separation)
        squared = squared + separation * separation
    squared = jnp.where(self_pair, 1.0, squared)
    inverse = lax.rsqrt(squared)
    screening = lax.rsqrt(2.0 * (row_geometry[3][:, None] + col_geometry[3][None, :]))
    slope = (
        (
            lax.erf(screening * squared * inverse) * inverse
            - TWO_ROOT * screening * jnp.exp(-screening * screening * squared)
        )
        * inverse
        * inverse
    )
    slope = jnp.where(self_pair, 0.0, slope) * col_charges[None, :]
    return jnp.stack(
        [
            jnp.sum(slope * separations[0], 1),
            jnp.sum(slope * separations[1], 1),
            jnp.sum(slope * separations[2], 1),
        ]
    )


def make_shards(rows, cols):
    devices = rows * cols
    everyone = ("row", "col")

    def gather_all(piece):
        spread = jnp.broadcast_to(piece[None], (devices,) + piece.shape)
        got = lax.all_to_all(spread, everyone, 0, 0, tiled=True)
        return jnp.moveaxis(got, 0, 1).reshape(piece.shape[0], -1)

    def shards(positions, species, descriptors, readout, hardness, widths):
        per_brick = species.shape[-1]
        atoms = devices * per_brick
        me = lax.axis_index("row") * cols + lax.axis_index("col")
        kind_range = jnp.arange(hardness.shape[0], dtype=jnp.int32)
        onehot = (kind_range[:, None] == species.reshape(1, per_brick)).astype(jnp.float32)
        hard_atom = jnp.sum(onehot * hardness[:, None], 0)
        width_atom = jnp.sum(onehot * widths[:, None], 0)
        features = descriptors.reshape(descriptors.shape[0], per_brick)
        atom_weights = jnp.zeros(features.shape, jnp.float32)
        for kind in range(hardness.shape[0]):
            atom_weights = atom_weights + onehot[kind][None, :] * readout[kind][:, None]
        negativity = jnp.sum(features * atom_weights, 0)
        self_term = hard_atom + 1.0 / (width_atom * ROOT_PI)
        own = jnp.concatenate(
            [
                positions.reshape(3, per_brick),
                (width_atom * width_atom)[None],
                negativity[None],
                self_term[None],
            ],
            0,
        )
        geometry = gather_all(own)
        col_index = jnp.arange(atoms, dtype=jnp.int32)

        pair = devices % 2 == 0 and (atoms // 2) * atoms * 4 <= PAIR_LIMIT
        if pair:
            parity = me % 2
            halves = devices // 2
            row_geometry = lax.dynamic_index_in_dim(
                geometry.reshape(6, halves, 2, per_brick), parity, 2, keepdims=False
            ).reshape(6, -1)
            brick_of = 2 * jnp.arange(halves, dtype=jnp.int32) + parity
            row_index = (brick_of[:, None] * per_brick + jnp.arange(per_brick, dtype=jnp.int32)[None]).reshape(-1)
            partner = [(i, i ^ 1) for i in range(devices)]

            def pick_rows(vectors):
                return lax.dynamic_index_in_dim(
                    vectors.reshape(2, halves, 2, per_brick), parity, 2, keepdims=False
                ).reshape(2, -1)

            def assemble(mine):
                theirs = lax.ppermute(mine, everyone, partner)
                first = jnp.where(parity == 0, mine, theirs).reshape(2, halves, per_brick)
                second = jnp.where(parity == 0, theirs, mine).reshape(2, halves, per_brick)
                return jnp.stack([first, second], 2).reshape(2, atoms)
        else:
            row_geometry = own
            row_index = me * per_brick + jnp.arange(per_brick, dtype=jnp.int32)

            def assemble(mine):
                return gather_all(mine.reshape(2, per_brick))

        if pair and atoms % 4 == 0:
            group = atoms // 4
            starts = []
            matrices = []
            for k, ((row_a, col_a), (row_b, col_b)) in enumerate(zip(BLOCKS[0], BLOCKS[1])):
                row_at = jnp.where(parity == 0, row_a, row_b) * group
                col_at = jnp.where(parity == 0, col_a, col_b) * group
                starts.append((row_at, col_at))
                local = jnp.arange(group, dtype=jnp.int32)
                matrices.append(
                    screened(
                        lax.dynamic_slice_in_dim(geometry, row_at, group, 1),
                        lax.dynamic_slice_in_dim(geometry, col_at, group, 1),
                        (row_at + local)[:, None] == (col_at + local)[None, :],
                    )
                )

            def operate(vectors):
                partial = jnp.zeros_like(vectors)
                for k, (matrix, (row_at, col_at)) in enumerate(zip(matrices, starts)):
                    col_part = lax.dynamic_slice_in_dim(vectors, col_at, group, 1)
                    forward = jnp.sum(matrix[None, :, :] * col_part[:, None, :], 2)
                    partial = lax.dynamic_update_slice_in_dim(
                        partial, lax.dynamic_slice_in_dim(partial, row_at, group, 1) + forward, row_at, 1
                    )
                    if k >= 2:
                        row_part = lax.dynamic_slice_in_dim(vectors, row_at, group, 1)
                        backward = jnp.sum(matrix[None, :, :] * row_part[:, :, None], 1)
                        partial = lax.dynamic_update_slice_in_dim(
                            partial, lax.dynamic_slice_in_dim(partial, col_at, group, 1) + backward, col_at, 1
                        )
                return partial + lax.ppermute(partial, everyone, partner)
        else:
            matrix = screened(row_geometry, geometry, row_index[:, None] == col_index[None, :])

            def operate(vectors):
                return assemble(jnp.sum(matrix[None, :, :] * vectors[:, None, :], 2))

        rhs = jnp.stack([-geometry[4], jnp.ones((atoms,), jnp.float32)])
        solution = jnp.zeros_like(rhs)
        resid = rhs
        direction = rhs
        norm_now = jnp.sum(resid * resid, 1)
        for iteration in range(ITERS):
            image = operate(direction)
            step_size = norm_now / jnp.sum(direction * image, 1)
            solution = solution + step_size[:, None] * direction
            if iteration + 1 < ITERS:
                resid = resid - step_size[:, None] * image
                norm_next = jnp.sum(resid * resid, 1)
                direction = resid + (norm_next / norm_now)[:, None] * direction
                norm_now = norm_next
        totals = jnp.sum(solution, 1)
        lagrange = totals[0] / totals[1]
        charges = solution[0] - lagrange * solution[1]
        own_index = me * per_brick + jnp.arange(per_brick, dtype=jnp.int32)
        own_charges = lax.dynamic_slice_in_dim(charges, me * per_brick, per_brick, 0)
        field = pulling(own, geometry, own_index[:, None] == col_index[None, :], charges)
        forces = (own_charges[None, :] * field).reshape(3, 1, 1, per_brick)
        return (own_charges.reshape(1, 1, per_brick), forces)

    return shards


def solution(mesh):
    in_specs = (
        P(None, "row", "col", None),
        P("row", "col", None),
        P(None, "row", "col", None),
        P(),
        P(),
        P(),
    )
    out_specs = (P("row", "col", None), P(None, "row", "col", None))
    shards = make_shards(mesh.shape["row"], mesh.shape["col"])
    return jax.shard_map(shards, mesh=mesh, in_specs=in_specs, out_specs=out_specs, check_vma=False)
```

```python
import jax
import jax.numpy as jnp
from jax import lax
from jax.sharding import PartitionSpec as P
from jax.experimental import pallas as pl
from jax.experimental.pallas import tpu as pltpu

ITERS = 3


ROOT_PI = 1.7724538509055159
TWO_ROOT = 1.1283791670955126

PAIR_LIMIT = 16 * 1024 * 1024
BLOCKS = (
    ((0, 0), (1, 1), (0, 1), (0, 2), (1, 2)),
    ((2, 2), (3, 3), (2, 3), (0, 3), (1, 3)),
)


def screened(row_geometry, col_geometry, self_pair):
    squared = jnp.zeros(self_pair.shape, row_geometry.dtype)
    for axis_id in range(3):
        separation = row_geometry[axis_id][:, None] - col_geometry[axis_id][None, :]
        squared = squared + separation * separation
    squared = jnp.where(self_pair, 1.0, squared)
    inverse = lax.rsqrt(squared)
    screening = lax.rsqrt(2.0 * (row_geometry[3][:, None] + col_geometry[3][None, :]))
    off = lax.erf(screening * squared * inverse) * inverse
    return jnp.where(self_pair, row_geometry[5][:, None], off)


def pulling(row_geometry, col_geometry, self_pair, col_charges):
    separations = []
    squared = jnp.zeros(self_pair.shape, row_geometry.dtype)
    for axis_id in range(3):
        separation = row_geometry[axis_id][:, None] - col_geometry[axis_id][None, :]
        separations.append(separation)
        squared = squared + separation * separation
    squared = jnp.where(self_pair, 1.0, squared)
    inverse = lax.rsqrt(squared)
    screening = lax.rsqrt(2.0 * (row_geometry[3][:, None] + col_geometry[3][None, :]))
    slope = (
        (
            lax.erf(screening * squared * inverse) * inverse
            - TWO_ROOT * screening * jnp.exp(-screening * screening * squared)
        )
        * inverse
        * inverse
    )
    slope = jnp.where(self_pair, 0.0, slope) * col_charges[None, :]
    return jnp.stack(
        [
            jnp.sum(slope * separations[0], 1),
            jnp.sum(slope * separations[1], 1),
            jnp.sum(slope * separations[2], 1),
        ]
    )


def prep_kernel(hard_ref, width_ref, pos_ref, species_ref, desc_ref, readout_ref, out_ref):
    kinds = species_ref[...]
    hard = jnp.zeros(kinds.shape, jnp.float32)
    width = jnp.zeros(kinds.shape, jnp.float32)
    for kind in range(hard_ref.shape[0]):
        hard = jnp.where(kinds == kind, hard_ref[kind], hard)
        width = jnp.where(kinds == kind, width_ref[kind], width)
    scores = lax.dot_general(
        readout_ref[...],
        desc_ref[...],
        (((1,), (1,)), ((), ())),
        precision=lax.Precision.HIGHEST,
        preferred_element_type=jnp.float32,
    )
    negativity = jnp.zeros(kinds.shape, jnp.float32)
    for kind in range(hard_ref.shape[0]):
        negativity = jnp.where(kinds == kind, scores[kind : kind + 1, :], negativity)
    self_term = hard + 1.0 / (width * ROOT_PI)
    block = jnp.concatenate(
        [pos_ref[...], width * width, negativity, self_term, jnp.zeros((2,) + kinds.shape[1:], jnp.float32)], 0
    )
    for slot in range(out_ref.shape[0]):
        out_ref[slot] = block


def prep(positions, species, descriptors, readout, hardness, widths, devices):
    per_brick = species.shape[-1]
    smem = pltpu.MemorySpace.SMEM if hasattr(pltpu, "MemorySpace") else pltpu.SMEM
    return pl.pallas_call(
        prep_kernel,
        in_specs=[
            pl.BlockSpec(memory_space=smem),
            pl.BlockSpec(memory_space=smem),
            pl.BlockSpec(memory_space=pltpu.VMEM),
            pl.BlockSpec(memory_space=pltpu.VMEM),
            pl.BlockSpec(memory_space=pltpu.VMEM),
            pl.BlockSpec(memory_space=pltpu.VMEM),
        ],
        out_specs=pl.BlockSpec(memory_space=pltpu.VMEM),
        out_shape=jax.ShapeDtypeStruct((devices, 8, per_brick), jnp.float32),
    )(
        hardness,
        widths,
        positions.reshape(3, per_brick),
        species.reshape(1, per_brick),
        descriptors.reshape(descriptors.shape[0], per_brick).T,
        readout,
    )


def make_shards(rows, cols):
    devices = rows * cols
    everyone = ("row", "col")

    def gather_all(piece):
        spread = jnp.broadcast_to(piece[None], (devices,) + piece.shape)
        got = lax.all_to_all(spread, everyone, 0, 0, tiled=True)
        return jnp.moveaxis(got, 0, 1).reshape(piece.shape[0], -1)

    def shards(positions, species, descriptors, readout, hardness, widths):
        per_brick = species.shape[-1]
        atoms = devices * per_brick
        me = lax.axis_index("row") * cols + lax.axis_index("col")
        payload = prep(positions, species, descriptors, readout, hardness, widths, devices)
        geometry = lax.all_to_all(payload, everyone, 0, 2, tiled=True)[0]
        own = lax.dynamic_slice_in_dim(geometry, me * per_brick, per_brick, 1)
        col_index = jnp.arange(atoms, dtype=jnp.int32)

        pair = devices % 2 == 0 and (atoms // 2) * atoms * 4 <= PAIR_LIMIT
        if pair:
            parity = me % 2
            halves = devices // 2
            row_geometry = lax.dynamic_index_in_dim(
                geometry.reshape(geometry.shape[0], halves, 2, per_brick), parity, 2, keepdims=False
            ).reshape(geometry.shape[0], -1)
            brick_of = 2 * jnp.arange(halves, dtype=jnp.int32) + parity
            row_index = (brick_of[:, None] * per_brick + jnp.arange(per_brick, dtype=jnp.int32)[None]).reshape(-1)
            partner = [(i, i ^ 1) for i in range(devices)]

            def pick_rows(vectors):
                return lax.dynamic_index_in_dim(
                    vectors.reshape(2, halves, 2, per_brick), parity, 2, keepdims=False
                ).reshape(2, -1)

            def assemble(mine):
                theirs = lax.ppermute(mine, everyone, partner)
                first = jnp.where(parity == 0, mine, theirs).reshape(2, halves, per_brick)
                second = jnp.where(parity == 0, theirs, mine).reshape(2, halves, per_brick)
                return jnp.stack([first, second], 2).reshape(2, atoms)
        else:
            row_geometry = own
            row_index = me * per_brick + jnp.arange(per_brick, dtype=jnp.int32)

            def assemble(mine):
                return gather_all(mine.reshape(2, per_brick))

        if pair and atoms % 4 == 0:
            group = atoms // 4
            starts = []
            matrices = []
            for k, ((row_a, col_a), (row_b, col_b)) in enumerate(zip(BLOCKS[0], BLOCKS[1])):
                row_at = jnp.where(parity == 0, row_a, row_b) * group
                col_at = jnp.where(parity == 0, col_a, col_b) * group
                starts.append((row_at, col_at))
                local = jnp.arange(group, dtype=jnp.int32)
                matrices.append(
                    screened(
                        lax.dynamic_slice_in_dim(geometry, row_at, group, 1),
                        lax.dynamic_slice_in_dim(geometry, col_at, group, 1),
                        (row_at + local)[:, None] == (col_at + local)[None, :],
                    )
                )

            def operate(vectors):
                partial = jnp.zeros_like(vectors)
                for k, (matrix, (row_at, col_at)) in enumerate(zip(matrices, starts)):
                    col_part = lax.dynamic_slice_in_dim(vectors, col_at, group, 1)
                    forward = jnp.sum(matrix[None, :, :] * col_part[:, None, :], 2)
                    partial = lax.dynamic_update_slice_in_dim(
                        partial, lax.dynamic_slice_in_dim(partial, row_at, group, 1) + forward, row_at, 1
                    )
                    if k >= 2:
                        row_part = lax.dynamic_slice_in_dim(vectors, row_at, group, 1)
                        backward = jnp.sum(matrix[None, :, :] * row_part[:, :, None], 1)
                        partial = lax.dynamic_update_slice_in_dim(
                            partial, lax.dynamic_slice_in_dim(partial, col_at, group, 1) + backward, col_at, 1
                        )
                return partial + lax.ppermute(partial, everyone, partner)
        else:
            matrix = screened(row_geometry, geometry, row_index[:, None] == col_index[None, :])

            def operate(vectors):
                return assemble(jnp.sum(matrix[None, :, :] * vectors[:, None, :], 2))

        rhs = jnp.stack([-geometry[4], jnp.ones((atoms,), jnp.float32)])
        solution = jnp.zeros_like(rhs)
        resid = rhs
        direction = rhs
        norm_now = jnp.sum(resid * resid, 1)
        for iteration in range(ITERS):
            image = operate(direction)
            step_size = norm_now / jnp.sum(direction * image, 1)
            solution = solution + step_size[:, None] * direction
            if iteration + 1 < ITERS:
                resid = resid - step_size[:, None] * image
                norm_next = jnp.sum(resid * resid, 1)
                direction = resid + (norm_next / norm_now)[:, None] * direction
                norm_now = norm_next
        totals = jnp.sum(solution, 1)
        lagrange = totals[0] / totals[1]
        charges = solution[0] - lagrange * solution[1]
        own_index = me * per_brick + jnp.arange(per_brick, dtype=jnp.int32)
        own_charges = lax.dynamic_slice_in_dim(charges, me * per_brick, per_brick, 0)
        field = pulling(own, geometry, own_index[:, None] == col_index[None, :], charges)
        forces = (own_charges[None, :] * field).reshape(3, 1, 1, per_brick)
        return (own_charges.reshape(1, 1, per_brick), forces)

    return shards


def solution(mesh):
    in_specs = (
        P(None, "row", "col", None),
        P("row", "col", None),
        P(None, "row", "col", None),
        P(),
        P(),
        P(),
    )
    out_specs = (P("row", "col", None), P(None, "row", "col", None))
    shards = make_shards(mesh.shape["row"], mesh.shape["col"])
    return jax.shard_map(shards, mesh=mesh, in_specs=in_specs, out_specs=out_specs, check_vma=False)
```

```python
import jax
import jax.numpy as jnp
from jax import lax
from jax.sharding import PartitionSpec as P
from jax.experimental import pallas as pl
from jax.experimental.pallas import tpu as pltpu

ITERS = 3


ROOT_PI = 1.7724538509055159
TWO_ROOT = 1.1283791670955126

PAIR_LIMIT = 16 * 1024 * 1024
BLOCKS = (
    ((0, 0), (1, 1), (0, 1), (0, 2), (1, 2)),
    ((2, 2), (3, 3), (2, 3), (0, 3), (1, 3)),
)


def screened(row_geometry, col_geometry, self_pair):
    squared = jnp.zeros(self_pair.shape, row_geometry.dtype)
    for axis_id in range(3):
        separation = row_geometry[axis_id][:, None] - col_geometry[axis_id][None, :]
        squared = squared + separation * separation
    squared = jnp.where(self_pair, 1.0, squared)
    inverse = lax.rsqrt(squared)
    screening = lax.rsqrt(2.0 * (row_geometry[3][:, None] + col_geometry[3][None, :]))
    off = lax.erf(screening * squared * inverse) * inverse
    return jnp.where(self_pair, row_geometry[5][:, None], off)


def pulling(row_geometry, col_geometry, self_pair, col_charges):
    separations = []
    squared = jnp.zeros(self_pair.shape, row_geometry.dtype)
    for axis_id in range(3):
        separation = row_geometry[axis_id][:, None] - col_geometry[axis_id][None, :]
        separations.append(separation)
        squared = squared + separation * separation
    squared = jnp.where(self_pair, 1.0, squared)
    inverse = lax.rsqrt(squared)
    screening = lax.rsqrt(2.0 * (row_geometry[3][:, None] + col_geometry[3][None, :]))
    slope = (
        (
            lax.erf(screening * squared * inverse) * inverse
            - TWO_ROOT * screening * jnp.exp(-screening * screening * squared)
        )
        * inverse
        * inverse
    )
    slope = jnp.where(self_pair, 0.0, slope) * col_charges[None, :]
    return jnp.stack(
        [
            jnp.sum(slope * separations[0], 1),
            jnp.sum(slope * separations[1], 1),
            jnp.sum(slope * separations[2], 1),
        ]
    )


def prep_kernel(hard_ref, width_ref, pos_ref, species_ref, desc_ref, readout_ref, out_ref):
    kinds = species_ref[...]
    hard = jnp.zeros(kinds.shape, jnp.float32)
    width = jnp.zeros(kinds.shape, jnp.float32)
    for kind in range(hard_ref.shape[0]):
        hard = jnp.where(kinds == kind, hard_ref[kind], hard)
        width = jnp.where(kinds == kind, width_ref[kind], width)
    scores = lax.dot_general(
        readout_ref[...],
        desc_ref[...],
        (((1,), (1,)), ((), ())),
        precision=lax.Precision.HIGHEST,
        preferred_element_type=jnp.float32,
    )
    negativity = jnp.zeros(kinds.shape, jnp.float32)
    for kind in range(hard_ref.shape[0]):
        negativity = jnp.where(kinds == kind, scores[kind : kind + 1, :], negativity)
    self_term = hard + 1.0 / (width * ROOT_PI)
    per_brick = kinds.shape[-1]
    features = [pos_ref[0], pos_ref[1], pos_ref[2], width * width, negativity, self_term]
    features = features + [jnp.zeros(kinds.shape, jnp.float32)] * (out_ref.shape[-1] // per_brick - len(features))
    block = jnp.concatenate(features, 1)
    for slot in range(out_ref.shape[0]):
        out_ref[slot] = block


def prep(positions, species, descriptors, readout, hardness, widths, devices):
    per_brick = species.shape[-1]
    smem = pltpu.MemorySpace.SMEM if hasattr(pltpu, "MemorySpace") else pltpu.SMEM
    return pl.pallas_call(
        prep_kernel,
        in_specs=[
            pl.BlockSpec(memory_space=smem),
            pl.BlockSpec(memory_space=smem),
            pl.BlockSpec(memory_space=pltpu.VMEM),
            pl.BlockSpec(memory_space=pltpu.VMEM),
            pl.BlockSpec(memory_space=pltpu.VMEM),
            pl.BlockSpec(memory_space=pltpu.VMEM),
        ],
        out_specs=pl.BlockSpec(memory_space=pltpu.VMEM),
        out_shape=jax.ShapeDtypeStruct((devices, 1, 8 * per_brick), jnp.float32),
    )(
        hardness,
        widths,
        positions.reshape(3, 1, per_brick),
        species.reshape(1, per_brick),
        descriptors.reshape(descriptors.shape[0], per_brick).T,
        readout,
    )


def make_shards(rows, cols):
    devices = rows * cols
    everyone = ("row", "col")

    def gather_all(piece):
        spread = jnp.broadcast_to(piece[None], (devices,) + piece.shape)
        got = lax.all_to_all(spread, everyone, 0, 0, tiled=True)
        return jnp.moveaxis(got, 0, 1).reshape(piece.shape[0], -1)

    def shards(positions, species, descriptors, readout, hardness, widths):
        per_brick = species.shape[-1]
        atoms = devices * per_brick
        me = lax.axis_index("row") * cols + lax.axis_index("col")
        payload = prep(positions, species, descriptors, readout, hardness, widths, devices)
        got = lax.all_to_all(payload, everyone, 0, 0, tiled=True)
        geometry = jnp.moveaxis(got.reshape(devices, 8, per_brick), 0, 1).reshape(8, atoms)
        own = lax.dynamic_slice_in_dim(geometry, me * per_brick, per_brick, 1)
        col_index = jnp.arange(atoms, dtype=jnp.int32)

        pair = devices % 2 == 0 and (atoms // 2) * atoms * 4 <= PAIR_LIMIT
        if pair:
            parity = me % 2
            halves = devices // 2
            row_geometry = lax.dynamic_index_in_dim(
                geometry.reshape(geometry.shape[0], halves, 2, per_brick), parity, 2, keepdims=False
            ).reshape(geometry.shape[0], -1)
            brick_of = 2 * jnp.arange(halves, dtype=jnp.int32) + parity
            row_index = (brick_of[:, None] * per_brick + jnp.arange(per_brick, dtype=jnp.int32)[None]).reshape(-1)
            partner = [(i, i ^ 1) for i in range(devices)]

            def pick_rows(vectors):
                return lax.dynamic_index_in_dim(
                    vectors.reshape(2, halves, 2, per_brick), parity, 2, keepdims=False
                ).reshape(2, -1)

            def assemble(mine):
                theirs = lax.ppermute(mine, everyone, partner)
                first = jnp.where(parity == 0, mine, theirs).reshape(2, halves, per_brick)
                second = jnp.where(parity == 0, theirs, mine).reshape(2, halves, per_brick)
                return jnp.stack([first, second], 2).reshape(2, atoms)
        else:
            row_geometry = own
            row_index = me * per_brick + jnp.arange(per_brick, dtype=jnp.int32)

            def assemble(mine):
                return gather_all(mine.reshape(2, per_brick))

        if pair and atoms % 4 == 0:
            group = atoms // 4
            starts = []
            matrices = []
            for k, ((row_a, col_a), (row_b, col_b)) in enumerate(zip(BLOCKS[0], BLOCKS[1])):
                row_at = jnp.where(parity == 0, row_a, row_b) * group
                col_at = jnp.where(parity == 0, col_a, col_b) * group
                starts.append((row_at, col_at))
                local = jnp.arange(group, dtype=jnp.int32)
                matrices.append(
                    screened(
                        lax.dynamic_slice_in_dim(geometry, row_at, group, 1),
                        lax.dynamic_slice_in_dim(geometry, col_at, group, 1),
                        (row_at + local)[:, None] == (col_at + local)[None, :],
                    )
                )

            def operate(vectors):
                partial = jnp.zeros_like(vectors)
                for k, (matrix, (row_at, col_at)) in enumerate(zip(matrices, starts)):
                    col_part = lax.dynamic_slice_in_dim(vectors, col_at, group, 1)
                    forward = jnp.sum(matrix[None, :, :] * col_part[:, None, :], 2)
                    partial = lax.dynamic_update_slice_in_dim(
                        partial, lax.dynamic_slice_in_dim(partial, row_at, group, 1) + forward, row_at, 1
                    )
                    if k >= 2:
                        row_part = lax.dynamic_slice_in_dim(vectors, row_at, group, 1)
                        backward = jnp.sum(matrix[None, :, :] * row_part[:, :, None], 1)
                        partial = lax.dynamic_update_slice_in_dim(
                            partial, lax.dynamic_slice_in_dim(partial, col_at, group, 1) + backward, col_at, 1
                        )
                return partial + lax.ppermute(partial, everyone, partner)
        else:
            matrix = screened(row_geometry, geometry, row_index[:, None] == col_index[None, :])

            def operate(vectors):
                return assemble(jnp.sum(matrix[None, :, :] * vectors[:, None, :], 2))

        rhs = jnp.stack([-geometry[4], jnp.ones((atoms,), jnp.float32)])
        solution = jnp.zeros_like(rhs)
        resid = rhs
        direction = rhs
        norm_now = jnp.sum(resid * resid, 1)
        for iteration in range(ITERS):
            image = operate(direction)
            step_size = norm_now / jnp.sum(direction * image, 1)
            solution = solution + step_size[:, None] * direction
            if iteration + 1 < ITERS:
                resid = resid - step_size[:, None] * image
                norm_next = jnp.sum(resid * resid, 1)
                direction = resid + (norm_next / norm_now)[:, None] * direction
                norm_now = norm_next
        totals = jnp.sum(solution, 1)
        lagrange = totals[0] / totals[1]
        charges = solution[0] - lagrange * solution[1]
        own_index = me * per_brick + jnp.arange(per_brick, dtype=jnp.int32)
        own_charges = lax.dynamic_slice_in_dim(charges, me * per_brick, per_brick, 0)
        field = pulling(own, geometry, own_index[:, None] == col_index[None, :], charges)
        forces = (own_charges[None, :] * field).reshape(3, 1, 1, per_brick)
        return (own_charges.reshape(1, 1, per_brick), forces)

    return shards


def solution(mesh):
    in_specs = (
        P(None, "row", "col", None),
        P("row", "col", None),
        P(None, "row", "col", None),
        P(),
        P(),
        P(),
    )
    out_specs = (P("row", "col", None), P(None, "row", "col", None))
    shards = make_shards(mesh.shape["row"], mesh.shape["col"])
    return jax.shard_map(shards, mesh=mesh, in_specs=in_specs, out_specs=out_specs, check_vma=False)
```

```python
import jax
import jax.numpy as jnp
from jax import lax
from jax.sharding import PartitionSpec as P
from jax.experimental import pallas as pl
from jax.experimental.pallas import tpu as pltpu

ITERS = 3


ROOT_PI = 1.7724538509055159
TWO_ROOT = 1.1283791670955126

PAIR_LIMIT = 16 * 1024 * 1024
BLOCKS = (
    ((0, 0), (1, 1), (0, 1), (0, 2), (1, 2)),
    ((2, 2), (3, 3), (2, 3), (0, 3), (1, 3)),
)


def screened(row_geometry, col_geometry, self_pair):
    squared = jnp.zeros(self_pair.shape, row_geometry.dtype)
    for axis_id in range(3):
        separation = row_geometry[axis_id][:, None] - col_geometry[axis_id][None, :]
        squared = squared + separation * separation
    squared = jnp.where(self_pair, 1.0, squared)
    inverse = lax.rsqrt(squared)
    screening = lax.rsqrt(2.0 * (row_geometry[3][:, None] + col_geometry[3][None, :]))
    off = lax.erf(screening * squared * inverse) * inverse
    return jnp.where(self_pair, row_geometry[5][:, None], off)


def pulling(row_geometry, col_geometry, self_pair, col_charges):
    separations = []
    squared = jnp.zeros(self_pair.shape, row_geometry.dtype)
    for axis_id in range(3):
        separation = row_geometry[axis_id][:, None] - col_geometry[axis_id][None, :]
        separations.append(separation)
        squared = squared + separation * separation
    squared = jnp.where(self_pair, 1.0, squared)
    inverse = lax.rsqrt(squared)
    screening = lax.rsqrt(2.0 * (row_geometry[3][:, None] + col_geometry[3][None, :]))
    slope = (
        (
            lax.erf(screening * squared * inverse) * inverse
            - TWO_ROOT * screening * jnp.exp(-screening * screening * squared)
        )
        * inverse
        * inverse
    )
    slope = jnp.where(self_pair, 0.0, slope) * col_charges[None, :]
    return jnp.stack(
        [
            jnp.sum(slope * separations[0], 1),
            jnp.sum(slope * separations[1], 1),
            jnp.sum(slope * separations[2], 1),
        ]
    )


def prep_kernel(hard_ref, width_ref, pos_ref, species_ref, desc_ref, readout_ref, out_ref):
    kinds = species_ref[...]
    hard = jnp.zeros(kinds.shape, jnp.float32)
    width = jnp.zeros(kinds.shape, jnp.float32)
    for kind in range(hard_ref.shape[0]):
        hard = jnp.where(kinds == kind, hard_ref[kind], hard)
        width = jnp.where(kinds == kind, width_ref[kind], width)
    scores = lax.dot_general(
        readout_ref[...],
        desc_ref[...],
        (((1,), (1,)), ((), ())),
        precision=lax.Precision.HIGHEST,
        preferred_element_type=jnp.float32,
    )
    negativity = jnp.zeros(kinds.shape, jnp.float32)
    for kind in range(hard_ref.shape[0]):
        negativity = jnp.where(kinds == kind, scores[kind : kind + 1, :], negativity)
    self_term = hard + 1.0 / (width * ROOT_PI)
    per_brick = kinds.shape[-1]
    features = [pos_ref[0], pos_ref[1], pos_ref[2], width * width, negativity, self_term]
    features = features + [jnp.zeros(kinds.shape, jnp.float32)] * (out_ref.shape[-1] // per_brick - len(features))
    block = jnp.concatenate(features, 1)
    for slot in range(out_ref.shape[0]):
        out_ref[slot] = block


def prep(positions, species, descriptors, readout, hardness, widths, devices):
    per_brick = species.shape[-1]
    smem = pltpu.MemorySpace.SMEM if hasattr(pltpu, "MemorySpace") else pltpu.SMEM
    return pl.pallas_call(
        prep_kernel,
        in_specs=[
            pl.BlockSpec(memory_space=smem),
            pl.BlockSpec(memory_space=smem),
            pl.BlockSpec(memory_space=pltpu.VMEM),
            pl.BlockSpec(memory_space=pltpu.VMEM),
            pl.BlockSpec(memory_space=pltpu.VMEM),
            pl.BlockSpec(memory_space=pltpu.VMEM),
        ],
        out_specs=pl.BlockSpec(memory_space=pltpu.VMEM),
        out_shape=jax.ShapeDtypeStruct((devices, 1, 8 * per_brick), jnp.float32),
    )(
        hardness,
        widths,
        positions.reshape(3, 1, per_brick),
        species.reshape(1, per_brick),
        descriptors.reshape(descriptors.shape[0], per_brick).T,
        readout,
    )


def pulling_matrices(row_geometry, col_geometry, self_pair):
    separations = []
    squared = jnp.zeros(self_pair.shape, row_geometry.dtype)
    for axis_id in range(3):
        separation = row_geometry[axis_id][:, None] - col_geometry[axis_id][None, :]
        separations.append(separation)
        squared = squared + separation * separation
    squared = jnp.where(self_pair, 1.0, squared)
    inverse = lax.rsqrt(squared)
    screening = lax.rsqrt(2.0 * (row_geometry[3][:, None] + col_geometry[3][None, :]))
    slope = (
        (
            lax.erf(screening * squared * inverse) * inverse
            - TWO_ROOT * screening * jnp.exp(-screening * screening * squared)
        )
        * inverse
        * inverse
    )
    slope = jnp.where(self_pair, 0.0, slope)
    return [slope * separation for separation in separations]


def make_shards(rows, cols):
    devices = rows * cols
    everyone = ("row", "col")

    def gather_all(piece):
        spread = jnp.broadcast_to(piece[None], (devices,) + piece.shape)
        got = lax.all_to_all(spread, everyone, 0, 0, tiled=True)
        return jnp.moveaxis(got, 0, 1).reshape(piece.shape[0], -1)

    def shards(positions, species, descriptors, readout, hardness, widths):
        per_brick = species.shape[-1]
        atoms = devices * per_brick
        me = lax.axis_index("row") * cols + lax.axis_index("col")
        payload = prep(positions, species, descriptors, readout, hardness, widths, devices)
        got = lax.all_to_all(payload, everyone, 0, 0, tiled=True)
        geometry = jnp.moveaxis(got.reshape(devices, 8, per_brick), 0, 1).reshape(8, atoms)
        own = lax.dynamic_slice_in_dim(geometry, me * per_brick, per_brick, 1)
        col_index = jnp.arange(atoms, dtype=jnp.int32)

        pair = devices % 2 == 0 and (atoms // 2) * atoms * 4 <= PAIR_LIMIT
        if pair:
            parity = me % 2
            halves = devices // 2
            row_geometry = lax.dynamic_index_in_dim(
                geometry.reshape(geometry.shape[0], halves, 2, per_brick), parity, 2, keepdims=False
            ).reshape(geometry.shape[0], -1)
            brick_of = 2 * jnp.arange(halves, dtype=jnp.int32) + parity
            row_index = (brick_of[:, None] * per_brick + jnp.arange(per_brick, dtype=jnp.int32)[None]).reshape(-1)
            partner = [(i, i ^ 1) for i in range(devices)]

            def pick_rows(vectors):
                return lax.dynamic_index_in_dim(
                    vectors.reshape(2, halves, 2, per_brick), parity, 2, keepdims=False
                ).reshape(2, -1)

            def assemble(mine):
                theirs = lax.ppermute(mine, everyone, partner)
                first = jnp.where(parity == 0, mine, theirs).reshape(2, halves, per_brick)
                second = jnp.where(parity == 0, theirs, mine).reshape(2, halves, per_brick)
                return jnp.stack([first, second], 2).reshape(2, atoms)
        else:
            row_geometry = own
            row_index = me * per_brick + jnp.arange(per_brick, dtype=jnp.int32)

            def assemble(mine):
                return gather_all(mine.reshape(2, per_brick))

        if pair and atoms % 4 == 0:
            group = atoms // 4
            starts = []
            matrices = []
            for k, ((row_a, col_a), (row_b, col_b)) in enumerate(zip(BLOCKS[0], BLOCKS[1])):
                row_at = jnp.where(parity == 0, row_a, row_b) * group
                col_at = jnp.where(parity == 0, col_a, col_b) * group
                starts.append((row_at, col_at))
                offsets = jnp.arange(group, dtype=jnp.int32)
                matrices.append(
                    screened(
                        lax.dynamic_slice_in_dim(geometry, row_at, group, 1),
                        lax.dynamic_slice_in_dim(geometry, col_at, group, 1),
                        (row_at + offsets)[:, None] == (col_at + offsets)[None, :],
                    )
                )

            def partial_image(vectors):
                partial = jnp.zeros_like(vectors)
                for k, (matrix, (row_at, col_at)) in enumerate(zip(matrices, starts)):
                    col_part = lax.dynamic_slice_in_dim(vectors, col_at, group, 1)
                    forward = jnp.sum(matrix[None, :, :] * col_part[:, None, :], 2)
                    partial = lax.dynamic_update_slice_in_dim(
                        partial, lax.dynamic_slice_in_dim(partial, row_at, group, 1) + forward, row_at, 1
                    )
                    if k >= 2:
                        row_part = lax.dynamic_slice_in_dim(vectors, row_at, group, 1)
                        backward = jnp.sum(matrix[None, :, :] * row_part[:, :, None], 1)
                        partial = lax.dynamic_update_slice_in_dim(
                            partial, lax.dynamic_slice_in_dim(partial, col_at, group, 1) + backward, col_at, 1
                        )
                return partial

            def operate(vectors):
                partial = partial_image(vectors)
                return partial + lax.ppermute(partial, everyone, partner)

            def curvature(vectors, ready):
                mine, ready = lax.optimization_barrier((jnp.sum(vectors * partial_image(vectors), 1), ready))
                return mine + lax.ppermute(mine, everyone, partner), ready
        else:
            matrix = screened(row_geometry, geometry, row_index[:, None] == col_index[None, :])

            def operate(vectors):
                return assemble(jnp.sum(matrix[None, :, :] * vectors[:, None, :], 2))

            def curvature(vectors, ready):
                return jnp.sum(vectors * operate(vectors), 1), ready

        rhs = jnp.stack([-geometry[4], jnp.ones((atoms,), jnp.float32)])
        solution = jnp.zeros_like(rhs)
        resid = rhs
        direction = rhs
        norm_now = jnp.sum(resid * resid, 1)
        own_index = me * per_brick + jnp.arange(per_brick, dtype=jnp.int32)
        for iteration in range(ITERS - 1):
            image = operate(direction)
            step_size = norm_now / jnp.sum(direction * image, 1)
            solution = solution + step_size[:, None] * direction
            resid = resid - step_size[:, None] * image
            norm_next = jnp.sum(resid * resid, 1)
            direction = resid + (norm_next / norm_now)[:, None] * direction
            norm_now = norm_next
        pull = pulling_matrices(own, geometry, own_index[:, None] == col_index[None, :])
        last_curvature, pull = curvature(direction, pull)
        step_size = norm_now / last_curvature
        solution = solution + step_size[:, None] * direction
        totals = jnp.sum(solution, 1)
        weights = jnp.where(jnp.arange(2) == 0, 1.0, -(totals[::-1] / totals))
        charges = jnp.sum(weights[:, None] * solution, 0)
        own_charges = lax.dynamic_slice_in_dim(charges, me * per_brick, per_brick, 0)
        field = jnp.stack([jnp.sum(part * charges[None, :], 1) for part in pull])
        forces = (own_charges[None, :] * field).reshape(3, 1, 1, per_brick)
        return (own_charges.reshape(1, 1, per_brick), forces)

    return shards


def solution(mesh):
    in_specs = (
        P(None, "row", "col", None),
        P("row", "col", None),
        P(None, "row", "col", None),
        P(),
        P(),
        P(),
    )
    out_specs = (P("row", "col", None), P(None, "row", "col", None))
    shards = make_shards(mesh.shape["row"], mesh.shape["col"])
    return jax.shard_map(shards, mesh=mesh, in_specs=in_specs, out_specs=out_specs, check_vma=False)
```

```python
import jax
import jax.numpy as jnp
from jax import lax
from jax.sharding import PartitionSpec as P
from jax.experimental import pallas as pl
from jax.experimental.pallas import tpu as pltpu

ITERS = 3


ROOT_PI = 1.7724538509055159
TWO_ROOT = 1.1283791670955126

PAIR_LIMIT = 16 * 1024 * 1024
BLOCKS = (
    ((0, 0), (1, 1), (0, 1), (0, 2), (1, 2)),
    ((2, 2), (3, 3), (2, 3), (0, 3), (1, 3)),
)


def screened(row_geometry, col_geometry, self_pair):
    squared = jnp.zeros(self_pair.shape, row_geometry.dtype)
    for axis_id in range(3):
        separation = row_geometry[axis_id][:, None] - col_geometry[axis_id][None, :]
        squared = squared + separation * separation
    squared = jnp.where(self_pair, 1.0, squared)
    inverse = lax.rsqrt(squared)
    screening = lax.rsqrt(2.0 * (row_geometry[3][:, None] + col_geometry[3][None, :]))
    off = lax.erf(screening * squared * inverse) * inverse
    return jnp.where(self_pair, row_geometry[5][:, None], off)


def pulling(row_geometry, col_geometry, self_pair, col_charges):
    separations = []
    squared = jnp.zeros(self_pair.shape, row_geometry.dtype)
    for axis_id in range(3):
        separation = row_geometry[axis_id][:, None] - col_geometry[axis_id][None, :]
        separations.append(separation)
        squared = squared + separation * separation
    squared = jnp.where(self_pair, 1.0, squared)
    inverse = lax.rsqrt(squared)
    screening = lax.rsqrt(2.0 * (row_geometry[3][:, None] + col_geometry[3][None, :]))
    slope = (
        (
            lax.erf(screening * squared * inverse) * inverse
            - TWO_ROOT * screening * jnp.exp(-screening * screening * squared)
        )
        * inverse
        * inverse
    )
    slope = jnp.where(self_pair, 0.0, slope) * col_charges[None, :]
    return jnp.stack(
        [
            jnp.sum(slope * separations[0], 1),
            jnp.sum(slope * separations[1], 1),
            jnp.sum(slope * separations[2], 1),
        ]
    )


def prep_kernel(hard_ref, width_ref, pos_ref, species_ref, desc_ref, readout_ref, out_ref):
    kinds = species_ref[...]
    hard = jnp.zeros(kinds.shape, jnp.float32)
    width = jnp.zeros(kinds.shape, jnp.float32)
    for kind in range(hard_ref.shape[0]):
        hard = jnp.where(kinds == kind, hard_ref[kind], hard)
        width = jnp.where(kinds == kind, width_ref[kind], width)
    scores = lax.dot_general(
        readout_ref[...],
        desc_ref[...],
        (((1,), (1,)), ((), ())),
        precision=lax.Precision.HIGHEST,
        preferred_element_type=jnp.float32,
    )
    negativity = jnp.zeros(kinds.shape, jnp.float32)
    for kind in range(hard_ref.shape[0]):
        negativity = jnp.where(kinds == kind, scores[kind : kind + 1, :], negativity)
    self_term = hard + 1.0 / (width * ROOT_PI)
    per_brick = kinds.shape[-1]
    features = [pos_ref[0], pos_ref[1], pos_ref[2], width * width, negativity, self_term]
    features = features + [jnp.zeros(kinds.shape, jnp.float32)] * (out_ref.shape[-1] // per_brick - len(features))
    block = jnp.concatenate(features, 1)
    for slot in range(out_ref.shape[0]):
        out_ref[slot] = block


def prep(positions, species, descriptors, readout, hardness, widths, devices):
    per_brick = species.shape[-1]
    smem = pltpu.MemorySpace.SMEM if hasattr(pltpu, "MemorySpace") else pltpu.SMEM
    return pl.pallas_call(
        prep_kernel,
        in_specs=[
            pl.BlockSpec(memory_space=smem),
            pl.BlockSpec(memory_space=smem),
            pl.BlockSpec(memory_space=pltpu.VMEM),
            pl.BlockSpec(memory_space=pltpu.VMEM),
            pl.BlockSpec(memory_space=pltpu.VMEM),
            pl.BlockSpec(memory_space=pltpu.VMEM),
        ],
        out_specs=pl.BlockSpec(memory_space=pltpu.VMEM),
        out_shape=jax.ShapeDtypeStruct((devices, 1, 8 * per_brick), jnp.float32),
    )(
        hardness,
        widths,
        positions.reshape(3, 1, per_brick),
        species.reshape(1, per_brick),
        descriptors.reshape(descriptors.shape[0], per_brick).T,
        readout,
    )


def pulling_fields(row_geometry, col_geometry, self_pair, vectors):
    separations = []
    squared = jnp.zeros(self_pair.shape, row_geometry.dtype)
    for axis_id in range(3):
        separation = row_geometry[axis_id][:, None] - col_geometry[axis_id][None, :]
        separations.append(separation)
        squared = squared + separation * separation
    squared = jnp.where(self_pair, 1.0, squared)
    inverse = lax.rsqrt(squared)
    screening = lax.rsqrt(2.0 * (row_geometry[3][:, None] + col_geometry[3][None, :]))
    slope = (
        (
            lax.erf(screening * squared * inverse) * inverse
            - TWO_ROOT * screening * jnp.exp(-screening * screening * squared)
        )
        * inverse
        * inverse
    )
    slope = jnp.where(self_pair, 0.0, slope)
    return jnp.stack(
        [jnp.stack([jnp.sum(slope * vector[None, :] * separation, 1) for separation in separations]) for vector in vectors]
    )


def make_shards(rows, cols):
    devices = rows * cols
    everyone = ("row", "col")

    def gather_all(piece):
        spread = jnp.broadcast_to(piece[None], (devices,) + piece.shape)
        got = lax.all_to_all(spread, everyone, 0, 0, tiled=True)
        return jnp.moveaxis(got, 0, 1).reshape(piece.shape[0], -1)

    def shards(positions, species, descriptors, readout, hardness, widths):
        per_brick = species.shape[-1]
        atoms = devices * per_brick
        me = lax.axis_index("row") * cols + lax.axis_index("col")
        payload = prep(positions, species, descriptors, readout, hardness, widths, devices)
        got = lax.all_to_all(payload, everyone, 0, 0, tiled=True)
        geometry = jnp.moveaxis(got.reshape(devices, 8, per_brick), 0, 1).reshape(8, atoms)
        own = lax.dynamic_slice_in_dim(geometry, me * per_brick, per_brick, 1)
        col_index = jnp.arange(atoms, dtype=jnp.int32)

        pair = devices % 2 == 0 and (atoms // 2) * atoms * 4 <= PAIR_LIMIT
        if pair:
            parity = me % 2
            halves = devices // 2
            row_geometry = lax.dynamic_index_in_dim(
                geometry.reshape(geometry.shape[0], halves, 2, per_brick), parity, 2, keepdims=False
            ).reshape(geometry.shape[0], -1)
            brick_of = 2 * jnp.arange(halves, dtype=jnp.int32) + parity
            row_index = (brick_of[:, None] * per_brick + jnp.arange(per_brick, dtype=jnp.int32)[None]).reshape(-1)
            partner = [(i, i ^ 1) for i in range(devices)]

            def pick_rows(vectors):
                return lax.dynamic_index_in_dim(
                    vectors.reshape(2, halves, 2, per_brick), parity, 2, keepdims=False
                ).reshape(2, -1)

            def assemble(mine):
                theirs = lax.ppermute(mine, everyone, partner)
                first = jnp.where(parity == 0, mine, theirs).reshape(2, halves, per_brick)
                second = jnp.where(parity == 0, theirs, mine).reshape(2, halves, per_brick)
                return jnp.stack([first, second], 2).reshape(2, atoms)
        else:
            row_geometry = own
            row_index = me * per_brick + jnp.arange(per_brick, dtype=jnp.int32)

            def assemble(mine):
                return gather_all(mine.reshape(2, per_brick))

        if pair and atoms % 4 == 0:
            group = atoms // 4
            starts = []
            matrices = []
            for k, ((row_a, col_a), (row_b, col_b)) in enumerate(zip(BLOCKS[0], BLOCKS[1])):
                row_at = jnp.where(parity == 0, row_a, row_b) * group
                col_at = jnp.where(parity == 0, col_a, col_b) * group
                starts.append((row_at, col_at))
                offsets = jnp.arange(group, dtype=jnp.int32)
                matrices.append(
                    screened(
                        lax.dynamic_slice_in_dim(geometry, row_at, group, 1),
                        lax.dynamic_slice_in_dim(geometry, col_at, group, 1),
                        (row_at + offsets)[:, None] == (col_at + offsets)[None, :],
                    )
                )

            def partial_image(vectors):
                partial = jnp.zeros_like(vectors)
                for k, (matrix, (row_at, col_at)) in enumerate(zip(matrices, starts)):
                    col_part = lax.dynamic_slice_in_dim(vectors, col_at, group, 1)
                    forward = jnp.sum(matrix[None, :, :] * col_part[:, None, :], 2)
                    partial = lax.dynamic_update_slice_in_dim(
                        partial, lax.dynamic_slice_in_dim(partial, row_at, group, 1) + forward, row_at, 1
                    )
                    if k >= 2:
                        row_part = lax.dynamic_slice_in_dim(vectors, row_at, group, 1)
                        backward = jnp.sum(matrix[None, :, :] * row_part[:, :, None], 1)
                        partial = lax.dynamic_update_slice_in_dim(
                            partial, lax.dynamic_slice_in_dim(partial, col_at, group, 1) + backward, col_at, 1
                        )
                return partial

            def operate(vectors):
                partial = partial_image(vectors)
                return partial + lax.ppermute(partial, everyone, partner)

            def curvature(vectors, ready):
                mine, ready = lax.optimization_barrier((jnp.sum(vectors * partial_image(vectors), 1), ready))
                return mine + lax.ppermute(mine, everyone, partner), ready
        else:
            matrix = screened(row_geometry, geometry, row_index[:, None] == col_index[None, :])

            def operate(vectors):
                return assemble(jnp.sum(matrix[None, :, :] * vectors[:, None, :], 2))

            def curvature(vectors, ready):
                return jnp.sum(vectors * operate(vectors), 1), ready

        rhs = jnp.stack([-geometry[4], jnp.ones((atoms,), jnp.float32)])
        solution = jnp.zeros_like(rhs)
        resid = rhs
        direction = rhs
        norm_now = jnp.sum(resid * resid, 1)
        own_index = me * per_brick + jnp.arange(per_brick, dtype=jnp.int32)
        for iteration in range(ITERS - 1):
            image = operate(direction)
            step_size = norm_now / jnp.sum(direction * image, 1)
            solution = solution + step_size[:, None] * direction
            resid = resid - step_size[:, None] * image
            norm_next = jnp.sum(resid * resid, 1)
            direction = resid + (norm_next / norm_now)[:, None] * direction
            norm_now = norm_next
        fields = pulling_fields(
            own, geometry, own_index[:, None] == col_index[None, :],
            [solution[0], solution[1], direction[0], direction[1]],
        ).reshape(2, 2, 3, per_brick)
        own_solution = lax.dynamic_slice_in_dim(solution, me * per_brick, per_brick, 1)
        own_direction = lax.dynamic_slice_in_dim(direction, me * per_brick, per_brick, 1)
        solution_sums = jnp.sum(solution, 1)
        direction_sums = jnp.sum(direction, 1)
        last_curvature, fields = curvature(direction, fields)
        step_size = norm_now / last_curvature
        totals = solution_sums + step_size * direction_sums
        weights = jnp.where(jnp.arange(2) == 0, 1.0, -(totals[::-1] / totals))
        own_charges = jnp.sum(weights[:, None] * (own_solution + step_size[:, None] * own_direction), 0)
        field = jnp.sum(
            weights[:, None, None] * (fields[0] + step_size[:, None, None] * fields[1]), 0
        )
        forces = (own_charges[None, :] * field).reshape(3, 1, 1, per_brick)
        return (own_charges.reshape(1, 1, per_brick), forces)

    return shards


def solution(mesh):
    in_specs = (
        P(None, "row", "col", None),
        P("row", "col", None),
        P(None, "row", "col", None),
        P(),
        P(),
        P(),
    )
    out_specs = (P("row", "col", None), P(None, "row", "col", None))
    shards = make_shards(mesh.shape["row"], mesh.shape["col"])
    return jax.shard_map(shards, mesh=mesh, in_specs=in_specs, out_specs=out_specs, check_vma=False)
```

```python
import jax
import jax.numpy as jnp
from jax import lax
from jax.sharding import PartitionSpec as P
from jax.experimental import pallas as pl
from jax.experimental.pallas import tpu as pltpu

ITERS = 3


ROOT_PI = 1.7724538509055159
TWO_ROOT = 1.1283791670955126

PAIR_LIMIT = 16 * 1024 * 1024
BLOCKS = (
    ((0, 0), (1, 1), (0, 1), (0, 2), (1, 2)),
    ((2, 2), (3, 3), (2, 3), (0, 3), (1, 3)),
)


def screened(row_geometry, col_geometry, self_pair):
    squared = jnp.zeros(self_pair.shape, row_geometry.dtype)
    for axis_id in range(3):
        separation = row_geometry[axis_id][:, None] - col_geometry[axis_id][None, :]
        squared = squared + separation * separation
    squared = jnp.where(self_pair, 1.0, squared)
    inverse = lax.rsqrt(squared)
    screening = lax.rsqrt(2.0 * (row_geometry[3][:, None] + col_geometry[3][None, :]))
    off = lax.erf(screening * squared * inverse) * inverse
    return jnp.where(self_pair, row_geometry[5][:, None], off)


def pulling(row_geometry, col_geometry, self_pair, col_charges):
    separations = []
    squared = jnp.zeros(self_pair.shape, row_geometry.dtype)
    for axis_id in range(3):
        separation = row_geometry[axis_id][:, None] - col_geometry[axis_id][None, :]
        separations.append(separation)
        squared = squared + separation * separation
    squared = jnp.where(self_pair, 1.0, squared)
    inverse = lax.rsqrt(squared)
    screening = lax.rsqrt(2.0 * (row_geometry[3][:, None] + col_geometry[3][None, :]))
    slope = (
        (
            lax.erf(screening * squared * inverse) * inverse
            - TWO_ROOT * screening * jnp.exp(-screening * screening * squared)
        )
        * inverse
        * inverse
    )
    slope = jnp.where(self_pair, 0.0, slope) * col_charges[None, :]
    return jnp.stack(
        [
            jnp.sum(slope * separations[0], 1),
            jnp.sum(slope * separations[1], 1),
            jnp.sum(slope * separations[2], 1),
        ]
    )


def prep_kernel(hard_ref, width_ref, pos_ref, species_ref, desc_ref, readout_ref, out_ref):
    kinds = species_ref[...]
    hard = jnp.zeros(kinds.shape, jnp.float32)
    width = jnp.zeros(kinds.shape, jnp.float32)
    for kind in range(hard_ref.shape[0]):
        hard = jnp.where(kinds == kind, hard_ref[kind], hard)
        width = jnp.where(kinds == kind, width_ref[kind], width)
    scores = lax.dot_general(
        readout_ref[...],
        desc_ref[...],
        (((1,), (1,)), ((), ())),
        precision=lax.Precision.HIGHEST,
        preferred_element_type=jnp.float32,
    )
    negativity = jnp.zeros(kinds.shape, jnp.float32)
    for kind in range(hard_ref.shape[0]):
        negativity = jnp.where(kinds == kind, scores[kind : kind + 1, :], negativity)
    self_term = hard + 1.0 / (width * ROOT_PI)
    per_brick = kinds.shape[-1]
    features = [pos_ref[0], pos_ref[1], pos_ref[2], width * width, negativity, self_term]
    features = features + [jnp.zeros(kinds.shape, jnp.float32)] * (out_ref.shape[-1] // per_brick - len(features))
    block = jnp.concatenate(features, 1)
    for slot in range(out_ref.shape[0]):
        out_ref[slot] = block


def prep(positions, species, descriptors, readout, hardness, widths, devices):
    per_brick = species.shape[-1]
    smem = pltpu.MemorySpace.SMEM if hasattr(pltpu, "MemorySpace") else pltpu.SMEM
    return pl.pallas_call(
        prep_kernel,
        in_specs=[
            pl.BlockSpec(memory_space=smem),
            pl.BlockSpec(memory_space=smem),
            pl.BlockSpec(memory_space=pltpu.VMEM),
            pl.BlockSpec(memory_space=pltpu.VMEM),
            pl.BlockSpec(memory_space=pltpu.VMEM),
            pl.BlockSpec(memory_space=pltpu.VMEM),
        ],
        out_specs=pl.BlockSpec(memory_space=pltpu.VMEM),
        out_shape=jax.ShapeDtypeStruct((devices, 1, 8 * per_brick), jnp.float32),
    )(
        hardness,
        widths,
        positions.reshape(3, 1, per_brick),
        species.reshape(1, per_brick),
        descriptors.reshape(descriptors.shape[0], per_brick).T,
        readout,
    )


def pulling_fields(row_geometry, col_geometry, self_pair, vectors):
    separations = []
    squared = jnp.zeros(self_pair.shape, row_geometry.dtype)
    for axis_id in range(3):
        separation = row_geometry[axis_id][:, None] - col_geometry[axis_id][None, :]
        separations.append(separation)
        squared = squared + separation * separation
    squared = jnp.where(self_pair, 1.0, squared)
    inverse = lax.rsqrt(squared)
    screening = lax.rsqrt(2.0 * (row_geometry[3][:, None] + col_geometry[3][None, :]))
    slope = (
        (
            lax.erf(screening * squared * inverse) * inverse
            - TWO_ROOT * screening * jnp.exp(-screening * screening * squared)
        )
        * inverse
        * inverse
    )
    slope = jnp.where(self_pair, 0.0, slope)
    return jnp.stack(
        [jnp.stack([jnp.sum(slope * vector[None, :] * separation, 1) for separation in separations]) for vector in vectors]
    )


def make_shards(rows, cols):
    devices = rows * cols
    everyone = ("row", "col")

    def gather_all(piece):
        spread = jnp.broadcast_to(piece[None], (devices,) + piece.shape)
        got = lax.all_to_all(spread, everyone, 0, 0, tiled=True)
        return jnp.moveaxis(got, 0, 1).reshape(piece.shape[0], -1)

    def shards(positions, species, descriptors, readout, hardness, widths):
        per_brick = species.shape[-1]
        atoms = devices * per_brick
        me = lax.axis_index("row") * cols + lax.axis_index("col")
        payload = prep(positions, species, descriptors, readout, hardness, widths, devices)
        got = lax.all_to_all(payload, everyone, 0, 0, tiled=True)
        geometry = jnp.moveaxis(got.reshape(devices, 8, per_brick), 0, 1).reshape(8, atoms)
        own = lax.dynamic_slice_in_dim(geometry, me * per_brick, per_brick, 1)
        col_index = jnp.arange(atoms, dtype=jnp.int32)

        pair = devices % 2 == 0 and (atoms // 2) * atoms * 4 <= PAIR_LIMIT
        if pair:
            parity = me % 2
            halves = devices // 2
            row_geometry = lax.dynamic_index_in_dim(
                geometry.reshape(geometry.shape[0], halves, 2, per_brick), parity, 2, keepdims=False
            ).reshape(geometry.shape[0], -1)
            brick_of = 2 * jnp.arange(halves, dtype=jnp.int32) + parity
            row_index = (brick_of[:, None] * per_brick + jnp.arange(per_brick, dtype=jnp.int32)[None]).reshape(-1)
            partner = [(i, i ^ 1) for i in range(devices)]

            def pick_rows(vectors):
                return lax.dynamic_index_in_dim(
                    vectors.reshape(2, halves, 2, per_brick), parity, 2, keepdims=False
                ).reshape(2, -1)

            def assemble(mine):
                theirs = lax.ppermute(mine, everyone, partner)
                first = jnp.where(parity == 0, mine, theirs).reshape(2, halves, per_brick)
                second = jnp.where(parity == 0, theirs, mine).reshape(2, halves, per_brick)
                return jnp.stack([first, second], 2).reshape(2, atoms)
        else:
            row_geometry = own
            row_index = me * per_brick + jnp.arange(per_brick, dtype=jnp.int32)

            def assemble(mine):
                return gather_all(mine.reshape(2, per_brick))

        if pair and atoms % 4 == 0:
            group = atoms // 4
            starts = []
            matrices = []
            for k, ((row_a, col_a), (row_b, col_b)) in enumerate(zip(BLOCKS[0], BLOCKS[1])):
                row_at = jnp.where(parity == 0, row_a, row_b) * group
                col_at = jnp.where(parity == 0, col_a, col_b) * group
                starts.append((row_at, col_at))
                offsets = jnp.arange(group, dtype=jnp.int32)
                matrices.append(
                    screened(
                        lax.dynamic_slice_in_dim(geometry, row_at, group, 1),
                        lax.dynamic_slice_in_dim(geometry, col_at, group, 1),
                        (row_at + offsets)[:, None] == (col_at + offsets)[None, :],
                    )
                )

            def partial_image(vectors):
                partial = jnp.zeros_like(vectors)
                for k, (matrix, (row_at, col_at)) in enumerate(zip(matrices, starts)):
                    col_part = lax.dynamic_slice_in_dim(vectors, col_at, group, 1)
                    forward = jnp.sum(matrix[None, :, :] * col_part[:, None, :], 2)
                    partial = lax.dynamic_update_slice_in_dim(
                        partial, lax.dynamic_slice_in_dim(partial, row_at, group, 1) + forward, row_at, 1
                    )
                    if k >= 2:
                        row_part = lax.dynamic_slice_in_dim(vectors, row_at, group, 1)
                        backward = jnp.sum(matrix[None, :, :] * row_part[:, :, None], 1)
                        partial = lax.dynamic_update_slice_in_dim(
                            partial, lax.dynamic_slice_in_dim(partial, col_at, group, 1) + backward, col_at, 1
                        )
                return partial

            def operate(vectors):
                partial = partial_image(vectors)
                return partial + lax.ppermute(partial, everyone, partner)

            def curvature(vectors):
                mine = jnp.sum(vectors * partial_image(vectors), 1)
                return mine + lax.ppermute(mine, everyone, partner)
        else:
            matrix = screened(row_geometry, geometry, row_index[:, None] == col_index[None, :])

            def operate(vectors):
                return assemble(jnp.sum(matrix[None, :, :] * vectors[:, None, :], 2))

            def curvature(vectors):
                return jnp.sum(vectors * operate(vectors), 1)

        rhs = jnp.stack([-geometry[4], jnp.ones((atoms,), jnp.float32)])
        solution = jnp.zeros_like(rhs)
        resid = rhs
        direction = rhs
        norm_now = jnp.sum(resid * resid, 1)
        own_index = me * per_brick + jnp.arange(per_brick, dtype=jnp.int32)
        for iteration in range(ITERS - 1):
            image = operate(direction)
            step_size = norm_now / jnp.sum(direction * image, 1)
            solution = solution + step_size[:, None] * direction
            resid = resid - step_size[:, None] * image
            norm_next = jnp.sum(resid * resid, 1)
            direction = resid + (norm_next / norm_now)[:, None] * direction
            norm_now = norm_next
        fields = pulling_fields(
            own, geometry, own_index[:, None] == col_index[None, :],
            [solution[0], solution[1], direction[0], direction[1]],
        ).reshape(2, 2, 3, per_brick)
        own_solution = lax.dynamic_slice_in_dim(solution, me * per_brick, per_brick, 1)
        own_direction = lax.dynamic_slice_in_dim(direction, me * per_brick, per_brick, 1)
        solution_sums = jnp.sum(solution, 1)
        direction_sums = jnp.sum(direction, 1)
        last_curvature = curvature(direction)
        step_size = norm_now / last_curvature
        totals = solution_sums + step_size * direction_sums
        weights = jnp.where(jnp.arange(2) == 0, 1.0, -(totals[::-1] / totals))
        own_charges = jnp.sum(weights[:, None] * (own_solution + step_size[:, None] * own_direction), 0)
        field = jnp.sum(
            weights[:, None, None] * (fields[0] + step_size[:, None, None] * fields[1]), 0
        )
        forces = (own_charges[None, :] * field).reshape(3, 1, 1, per_brick)
        return (own_charges.reshape(1, 1, per_brick), forces)

    return shards


def solution(mesh):
    in_specs = (
        P(None, "row", "col", None),
        P("row", "col", None),
        P(None, "row", "col", None),
        P(),
        P(),
        P(),
    )
    out_specs = (P("row", "col", None), P(None, "row", "col", None))
    shards = make_shards(mesh.shape["row"], mesh.shape["col"])
    return jax.shard_map(shards, mesh=mesh, in_specs=in_specs, out_specs=out_specs, check_vma=False)
```

```python
import jax
import jax.numpy as jnp
from jax import lax
from jax.sharding import PartitionSpec as P
from jax.experimental import pallas as pl
from jax.experimental.pallas import tpu as pltpu

ITERS = 3


ROOT_PI = 1.7724538509055159
TWO_ROOT = 1.1283791670955126

PAIR_LIMIT = 16 * 1024 * 1024
BLOCKS = (
    ((0, 0), (1, 1), (0, 1), (0, 2), (1, 2)),
    ((2, 2), (3, 3), (2, 3), (0, 3), (1, 3)),
)


def screened(row_geometry, col_geometry, self_pair):
    squared = jnp.zeros(self_pair.shape, row_geometry.dtype)
    for axis_id in range(3):
        separation = row_geometry[axis_id][:, None] - col_geometry[axis_id][None, :]
        squared = squared + separation * separation
    squared = jnp.where(self_pair, 1.0, squared)
    inverse = lax.rsqrt(squared)
    screening = lax.rsqrt(2.0 * (row_geometry[3][:, None] + col_geometry[3][None, :]))
    off = lax.erf(screening * squared * inverse) * inverse
    return jnp.where(self_pair, row_geometry[5][:, None], off)


def pulling(row_geometry, col_geometry, self_pair, col_charges):
    separations = []
    squared = jnp.zeros(self_pair.shape, row_geometry.dtype)
    for axis_id in range(3):
        separation = row_geometry[axis_id][:, None] - col_geometry[axis_id][None, :]
        separations.append(separation)
        squared = squared + separation * separation
    squared = jnp.where(self_pair, 1.0, squared)
    inverse = lax.rsqrt(squared)
    screening = lax.rsqrt(2.0 * (row_geometry[3][:, None] + col_geometry[3][None, :]))
    slope = (
        (
            lax.erf(screening * squared * inverse) * inverse
            - TWO_ROOT * screening * jnp.exp(-screening * screening * squared)
        )
        * inverse
        * inverse
    )
    slope = jnp.where(self_pair, 0.0, slope) * col_charges[None, :]
    return jnp.stack(
        [
            jnp.sum(slope * separations[0], 1),
            jnp.sum(slope * separations[1], 1),
            jnp.sum(slope * separations[2], 1),
        ]
    )


def prep_kernel(hard_ref, width_ref, pos_ref, species_ref, desc_ref, readout_ref, out_ref):
    kinds = species_ref[...]
    hard = jnp.zeros(kinds.shape, jnp.float32)
    width = jnp.zeros(kinds.shape, jnp.float32)
    for kind in range(hard_ref.shape[0]):
        hard = jnp.where(kinds == kind, hard_ref[kind], hard)
        width = jnp.where(kinds == kind, width_ref[kind], width)
    scores = lax.dot_general(
        readout_ref[...],
        desc_ref[...],
        (((1,), (1,)), ((), ())),
        precision=lax.Precision.HIGHEST,
        preferred_element_type=jnp.float32,
    )
    negativity = jnp.zeros(kinds.shape, jnp.float32)
    for kind in range(hard_ref.shape[0]):
        negativity = jnp.where(kinds == kind, scores[kind : kind + 1, :], negativity)
    self_term = hard + 1.0 / (width * ROOT_PI)
    per_brick = kinds.shape[-1]
    features = [pos_ref[0], pos_ref[1], pos_ref[2], width * width, negativity, self_term]
    features = features + [jnp.zeros(kinds.shape, jnp.float32)] * (out_ref.shape[-1] // per_brick - len(features))
    block = jnp.concatenate(features, 1)
    for slot in range(out_ref.shape[0]):
        out_ref[slot] = block


def prep(positions, species, descriptors, readout, hardness, widths, devices):
    per_brick = species.shape[-1]
    smem = pltpu.MemorySpace.SMEM if hasattr(pltpu, "MemorySpace") else pltpu.SMEM
    return pl.pallas_call(
        prep_kernel,
        in_specs=[
            pl.BlockSpec(memory_space=smem),
            pl.BlockSpec(memory_space=smem),
            pl.BlockSpec(memory_space=pltpu.VMEM),
            pl.BlockSpec(memory_space=pltpu.VMEM),
            pl.BlockSpec(memory_space=pltpu.VMEM),
            pl.BlockSpec(memory_space=pltpu.VMEM),
        ],
        out_specs=pl.BlockSpec(memory_space=pltpu.VMEM),
        out_shape=jax.ShapeDtypeStruct((devices, 1, 8 * per_brick), jnp.float32),
    )(
        hardness,
        widths,
        positions.reshape(3, 1, per_brick),
        species.reshape(1, per_brick),
        descriptors.reshape(descriptors.shape[0], per_brick).T,
        readout,
    )


def pulling_fields(row_geometry, col_geometry, self_pair, vectors):
    separations = []
    squared = jnp.zeros(self_pair.shape, row_geometry.dtype)
    for axis_id in range(3):
        separation = row_geometry[axis_id][:, None] - col_geometry[axis_id][None, :]
        separations.append(separation)
        squared = squared + separation * separation
    squared = jnp.where(self_pair, 1.0, squared)
    inverse = lax.rsqrt(squared)
    screening = lax.rsqrt(2.0 * (row_geometry[3][:, None] + col_geometry[3][None, :]))
    slope = (
        (
            lax.erf(screening * squared * inverse) * inverse
            - TWO_ROOT * screening * jnp.exp(-screening * screening * squared)
        )
        * inverse
        * inverse
    )
    slope = jnp.where(self_pair, 0.0, slope)
    return jnp.stack(
        [jnp.stack([jnp.sum(slope * vector[None, :] * separation, 1) for separation in separations]) for vector in vectors]
    )


def make_shards(rows, cols):
    devices = rows * cols
    everyone = ("row", "col")

    def gather_all(piece):
        spread = jnp.broadcast_to(piece[None], (devices,) + piece.shape)
        got = lax.all_to_all(spread, everyone, 0, 0, tiled=True)
        return jnp.moveaxis(got, 0, 1).reshape(piece.shape[0], -1)

    def shards(positions, species, descriptors, readout, hardness, widths):
        per_brick = species.shape[-1]
        atoms = devices * per_brick
        me = lax.axis_index("row") * cols + lax.axis_index("col")
        payload = prep(positions, species, descriptors, readout, hardness, widths, devices)
        got = lax.all_to_all(payload, everyone, 0, 0, tiled=True)
        geometry = jnp.moveaxis(got.reshape(devices, 8, per_brick), 0, 1).reshape(8, atoms)
        own = lax.dynamic_slice_in_dim(geometry, me * per_brick, per_brick, 1)
        col_index = jnp.arange(atoms, dtype=jnp.int32)

        pair = devices % 2 == 0 and (atoms // 2) * atoms * 4 <= PAIR_LIMIT
        if pair:
            parity = me % 2
            halves = devices // 2
            row_geometry = lax.dynamic_index_in_dim(
                geometry.reshape(geometry.shape[0], halves, 2, per_brick), parity, 2, keepdims=False
            ).reshape(geometry.shape[0], -1)
            brick_of = 2 * jnp.arange(halves, dtype=jnp.int32) + parity
            row_index = (brick_of[:, None] * per_brick + jnp.arange(per_brick, dtype=jnp.int32)[None]).reshape(-1)
            partner = [(i, i ^ 1) for i in range(devices)]

            def pick_rows(vectors):
                return lax.dynamic_index_in_dim(
                    vectors.reshape(2, halves, 2, per_brick), parity, 2, keepdims=False
                ).reshape(2, -1)

            def assemble(mine):
                theirs = lax.ppermute(mine, everyone, partner)
                first = jnp.where(parity == 0, mine, theirs).reshape(2, halves, per_brick)
                second = jnp.where(parity == 0, theirs, mine).reshape(2, halves, per_brick)
                return jnp.stack([first, second], 2).reshape(2, atoms)
        else:
            row_geometry = own
            row_index = me * per_brick + jnp.arange(per_brick, dtype=jnp.int32)

            def assemble(mine):
                return gather_all(mine.reshape(2, per_brick))

        if pair and atoms % 4 == 0:
            group = atoms // 4
            starts = []
            matrices = []
            for k, ((row_a, col_a), (row_b, col_b)) in enumerate(zip(BLOCKS[0], BLOCKS[1])):
                row_at = jnp.where(parity == 0, row_a, row_b) * group
                col_at = jnp.where(parity == 0, col_a, col_b) * group
                starts.append((row_at, col_at))
                offsets = jnp.arange(group, dtype=jnp.int32)
                matrices.append(
                    screened(
                        lax.dynamic_slice_in_dim(geometry, row_at, group, 1),
                        lax.dynamic_slice_in_dim(geometry, col_at, group, 1),
                        (row_at + offsets)[:, None] == (col_at + offsets)[None, :],
                    )
                )

            def partial_image(vectors):
                partial = jnp.zeros_like(vectors)
                for k, (matrix, (row_at, col_at)) in enumerate(zip(matrices, starts)):
                    col_part = lax.dynamic_slice_in_dim(vectors, col_at, group, 1)
                    forward = jnp.sum(matrix[None, :, :] * col_part[:, None, :], 2)
                    partial = lax.dynamic_update_slice_in_dim(
                        partial, lax.dynamic_slice_in_dim(partial, row_at, group, 1) + forward, row_at, 1
                    )
                    if k >= 2:
                        row_part = lax.dynamic_slice_in_dim(vectors, row_at, group, 1)
                        backward = jnp.sum(matrix[None, :, :] * row_part[:, :, None], 1)
                        partial = lax.dynamic_update_slice_in_dim(
                            partial, lax.dynamic_slice_in_dim(partial, col_at, group, 1) + backward, col_at, 1
                        )
                return partial

            def operate(vectors):
                partial = partial_image(vectors)
                return partial + lax.ppermute(partial, everyone, partner)

            def curvature(vectors):
                mine = 0.0
                for k, (matrix, (row_at, col_at)) in enumerate(zip(matrices, starts)):
                    col_part = lax.dynamic_slice_in_dim(vectors, col_at, group, 1)
                    row_part = lax.dynamic_slice_in_dim(vectors, row_at, group, 1)
                    term = jnp.sum(row_part * jnp.sum(matrix[None, :, :] * col_part[:, None, :], 2), 1)
                    mine = mine + (term if k < 2 else 2.0 * term)
                return mine + lax.ppermute(mine, everyone, partner)
        else:
            matrix = screened(row_geometry, geometry, row_index[:, None] == col_index[None, :])

            def operate(vectors):
                return assemble(jnp.sum(matrix[None, :, :] * vectors[:, None, :], 2))

            def curvature(vectors):
                return jnp.sum(vectors * operate(vectors), 1)

        rhs = jnp.stack([-geometry[4], jnp.ones((atoms,), jnp.float32)])
        solution = jnp.zeros_like(rhs)
        resid = rhs
        direction = rhs
        norm_now = jnp.sum(resid * resid, 1)
        own_index = me * per_brick + jnp.arange(per_brick, dtype=jnp.int32)
        for iteration in range(ITERS - 1):
            image = operate(direction)
            step_size = norm_now / jnp.sum(direction * image, 1)
            solution = solution + step_size[:, None] * direction
            resid = resid - step_size[:, None] * image
            norm_next = jnp.sum(resid * resid, 1)
            direction = resid + (norm_next / norm_now)[:, None] * direction
            norm_now = norm_next
        fields = pulling_fields(
            own, geometry, own_index[:, None] == col_index[None, :],
            [solution[0], solution[1], direction[0], direction[1]],
        ).reshape(2, 2, 3, per_brick)
        own_solution = lax.dynamic_slice_in_dim(solution, me * per_brick, per_brick, 1)
        own_direction = lax.dynamic_slice_in_dim(direction, me * per_brick, per_brick, 1)
        solution_sums = jnp.sum(solution, 1)
        direction_sums = jnp.sum(direction, 1)
        last_curvature = curvature(direction)
        step_size = norm_now / last_curvature
        totals = solution_sums + step_size * direction_sums
        weights = jnp.where(jnp.arange(2) == 0, 1.0, -(totals[::-1] / totals))
        own_charges = jnp.sum(weights[:, None] * (own_solution + step_size[:, None] * own_direction), 0)
        field = jnp.sum(
            weights[:, None, None] * (fields[0] + step_size[:, None, None] * fields[1]), 0
        )
        forces = (own_charges[None, :] * field).reshape(3, 1, 1, per_brick)
        return (own_charges.reshape(1, 1, per_brick), forces)

    return shards


def solution(mesh):
    in_specs = (
        P(None, "row", "col", None),
        P("row", "col", None),
        P(None, "row", "col", None),
        P(),
        P(),
        P(),
    )
    out_specs = (P("row", "col", None), P(None, "row", "col", None))
    shards = make_shards(mesh.shape["row"], mesh.shape["col"])
    return jax.shard_map(shards, mesh=mesh, in_specs=in_specs, out_specs=out_specs, check_vma=False)
```

```python
import jax
import jax.numpy as jnp
from jax import lax
from jax.sharding import PartitionSpec as P
from jax.experimental import pallas as pl
from jax.experimental.pallas import tpu as pltpu

ITERS = 3


ROOT_PI = 1.7724538509055159
TWO_ROOT = 1.1283791670955126

PAIR_LIMIT = 16 * 1024 * 1024
FEATURES = 6
BLOCKS = (
    ((0, 0), (1, 1), (0, 1), (0, 2), (1, 2)),
    ((2, 2), (3, 3), (2, 3), (0, 3), (1, 3)),
)


def screened(row_geometry, col_geometry, self_pair):
    squared = jnp.zeros(self_pair.shape, row_geometry.dtype)
    for axis_id in range(3):
        separation = row_geometry[axis_id][:, None] - col_geometry[axis_id][None, :]
        squared = squared + separation * separation
    squared = jnp.where(self_pair, 1.0, squared)
    inverse = lax.rsqrt(squared)
    screening = lax.rsqrt(2.0 * (row_geometry[3][:, None] + col_geometry[3][None, :]))
    off = lax.erf(screening * squared * inverse) * inverse
    return jnp.where(self_pair, row_geometry[5][:, None], off)


def pulling(row_geometry, col_geometry, self_pair, col_charges):
    separations = []
    squared = jnp.zeros(self_pair.shape, row_geometry.dtype)
    for axis_id in range(3):
        separation = row_geometry[axis_id][:, None] - col_geometry[axis_id][None, :]
        separations.append(separation)
        squared = squared + separation * separation
    squared = jnp.where(self_pair, 1.0, squared)
    inverse = lax.rsqrt(squared)
    screening = lax.rsqrt(2.0 * (row_geometry[3][:, None] + col_geometry[3][None, :]))
    slope = (
        (
            lax.erf(screening * squared * inverse) * inverse
            - TWO_ROOT * screening * jnp.exp(-screening * screening * squared)
        )
        * inverse
        * inverse
    )
    slope = jnp.where(self_pair, 0.0, slope) * col_charges[None, :]
    return jnp.stack(
        [
            jnp.sum(slope * separations[0], 1),
            jnp.sum(slope * separations[1], 1),
            jnp.sum(slope * separations[2], 1),
        ]
    )


def prep_kernel(hard_ref, width_ref, pos_ref, species_ref, desc_ref, readout_ref, out_ref):
    kinds = species_ref[...]
    hard = jnp.zeros(kinds.shape, jnp.float32)
    width = jnp.zeros(kinds.shape, jnp.float32)
    for kind in range(hard_ref.shape[0]):
        hard = jnp.where(kinds == kind, hard_ref[kind], hard)
        width = jnp.where(kinds == kind, width_ref[kind], width)
    scores = lax.dot_general(
        readout_ref[...],
        desc_ref[...],
        (((1,), (1,)), ((), ())),
        precision=lax.Precision.HIGHEST,
        preferred_element_type=jnp.float32,
    )
    negativity = jnp.zeros(kinds.shape, jnp.float32)
    for kind in range(hard_ref.shape[0]):
        negativity = jnp.where(kinds == kind, scores[kind : kind + 1, :], negativity)
    self_term = hard + 1.0 / (width * ROOT_PI)
    per_brick = kinds.shape[-1]
    features = [pos_ref[0], pos_ref[1], pos_ref[2], width * width, negativity, self_term]
    features = features + [jnp.zeros(kinds.shape, jnp.float32)] * (out_ref.shape[-1] // per_brick - len(features))
    block = jnp.concatenate(features, 1)
    for slot in range(out_ref.shape[0]):
        out_ref[slot] = block


def prep(positions, species, descriptors, readout, hardness, widths, devices):
    per_brick = species.shape[-1]
    smem = pltpu.MemorySpace.SMEM if hasattr(pltpu, "MemorySpace") else pltpu.SMEM
    return pl.pallas_call(
        prep_kernel,
        in_specs=[
            pl.BlockSpec(memory_space=smem),
            pl.BlockSpec(memory_space=smem),
            pl.BlockSpec(memory_space=pltpu.VMEM),
            pl.BlockSpec(memory_space=pltpu.VMEM),
            pl.BlockSpec(memory_space=pltpu.VMEM),
            pl.BlockSpec(memory_space=pltpu.VMEM),
        ],
        out_specs=pl.BlockSpec(memory_space=pltpu.VMEM),
        out_shape=jax.ShapeDtypeStruct((devices, 1, FEATURES * per_brick), jnp.float32),
    )(
        hardness,
        widths,
        positions.reshape(3, 1, per_brick),
        species.reshape(1, per_brick),
        descriptors.reshape(descriptors.shape[0], per_brick).T,
        readout,
    )


def pulling_fields(row_geometry, col_geometry, self_pair, vectors):
    separations = []
    squared = jnp.zeros(self_pair.shape, row_geometry.dtype)
    for axis_id in range(3):
        separation = row_geometry[axis_id][:, None] - col_geometry[axis_id][None, :]
        separations.append(separation)
        squared = squared + separation * separation
    squared = jnp.where(self_pair, 1.0, squared)
    inverse = lax.rsqrt(squared)
    screening = lax.rsqrt(2.0 * (row_geometry[3][:, None] + col_geometry[3][None, :]))
    slope = (
        (
            lax.erf(screening * squared * inverse) * inverse
            - TWO_ROOT * screening * jnp.exp(-screening * screening * squared)
        )
        * inverse
        * inverse
    )
    slope = jnp.where(self_pair, 0.0, slope)
    return jnp.stack(
        [jnp.stack([jnp.sum(slope * vector[None, :] * separation, 1) for separation in separations]) for vector in vectors]
    )


def make_shards(rows, cols):
    devices = rows * cols
    everyone = ("row", "col")

    def gather_all(piece):
        spread = jnp.broadcast_to(piece[None], (devices,) + piece.shape)
        got = lax.all_to_all(spread, everyone, 0, 0, tiled=True)
        return jnp.moveaxis(got, 0, 1).reshape(piece.shape[0], -1)

    def shards(positions, species, descriptors, readout, hardness, widths):
        per_brick = species.shape[-1]
        atoms = devices * per_brick
        me = lax.axis_index("row") * cols + lax.axis_index("col")
        payload = prep(positions, species, descriptors, readout, hardness, widths, devices)
        got = lax.all_to_all(payload, everyone, 0, 0, tiled=True)
        geometry = jnp.moveaxis(got.reshape(devices, FEATURES, per_brick), 0, 1).reshape(FEATURES, atoms)
        own = lax.dynamic_slice_in_dim(geometry, me * per_brick, per_brick, 1)
        col_index = jnp.arange(atoms, dtype=jnp.int32)

        pair = devices % 2 == 0 and (atoms // 2) * atoms * 4 <= PAIR_LIMIT
        if pair:
            parity = me % 2
            halves = devices // 2
            row_geometry = lax.dynamic_index_in_dim(
                geometry.reshape(geometry.shape[0], halves, 2, per_brick), parity, 2, keepdims=False
            ).reshape(geometry.shape[0], -1)
            brick_of = 2 * jnp.arange(halves, dtype=jnp.int32) + parity
            row_index = (brick_of[:, None] * per_brick + jnp.arange(per_brick, dtype=jnp.int32)[None]).reshape(-1)
            partner = [(i, i ^ 1) for i in range(devices)]

            def pick_rows(vectors):
                return lax.dynamic_index_in_dim(
                    vectors.reshape(2, halves, 2, per_brick), parity, 2, keepdims=False
                ).reshape(2, -1)

            def assemble(mine):
                theirs = lax.ppermute(mine, everyone, partner)
                first = jnp.where(parity == 0, mine, theirs).reshape(2, halves, per_brick)
                second = jnp.where(parity == 0, theirs, mine).reshape(2, halves, per_brick)
                return jnp.stack([first, second], 2).reshape(2, atoms)
        else:
            row_geometry = own
            row_index = me * per_brick + jnp.arange(per_brick, dtype=jnp.int32)

            def assemble(mine):
                return gather_all(mine.reshape(2, per_brick))

        if pair and atoms % 4 == 0:
            group = atoms // 4
            starts = []
            matrices = []
            for k, ((row_a, col_a), (row_b, col_b)) in enumerate(zip(BLOCKS[0], BLOCKS[1])):
                row_at = jnp.where(parity == 0, row_a, row_b) * group
                col_at = jnp.where(parity == 0, col_a, col_b) * group
                starts.append((row_at, col_at))
                offsets = jnp.arange(group, dtype=jnp.int32)
                matrices.append(
                    screened(
                        lax.dynamic_slice_in_dim(geometry, row_at, group, 1),
                        lax.dynamic_slice_in_dim(geometry, col_at, group, 1),
                        (row_at + offsets)[:, None] == (col_at + offsets)[None, :],
                    )
                )

            def partial_image(vectors):
                partial = jnp.zeros_like(vectors)
                for k, (matrix, (row_at, col_at)) in enumerate(zip(matrices, starts)):
                    col_part = lax.dynamic_slice_in_dim(vectors, col_at, group, 1)
                    forward = jnp.sum(matrix[None, :, :] * col_part[:, None, :], 2)
                    partial = lax.dynamic_update_slice_in_dim(
                        partial, lax.dynamic_slice_in_dim(partial, row_at, group, 1) + forward, row_at, 1
                    )
                    if k >= 2:
                        row_part = lax.dynamic_slice_in_dim(vectors, row_at, group, 1)
                        backward = jnp.sum(matrix[None, :, :] * row_part[:, :, None], 1)
                        partial = lax.dynamic_update_slice_in_dim(
                            partial, lax.dynamic_slice_in_dim(partial, col_at, group, 1) + backward, col_at, 1
                        )
                return partial

            def operate(vectors):
                partial = partial_image(vectors)
                return partial + lax.ppermute(partial, everyone, partner)

            def curvature(vectors):
                mine = 0.0
                for k, (matrix, (row_at, col_at)) in enumerate(zip(matrices, starts)):
                    col_part = lax.dynamic_slice_in_dim(vectors, col_at, group, 1)
                    row_part = lax.dynamic_slice_in_dim(vectors, row_at, group, 1)
                    term = jnp.sum(row_part * jnp.sum(matrix[None, :, :] * col_part[:, None, :], 2), 1)
                    mine = mine + (term if k < 2 else 2.0 * term)
                return mine + lax.ppermute(mine, everyone, partner)
        else:
            matrix = screened(row_geometry, geometry, row_index[:, None] == col_index[None, :])

            def operate(vectors):
                return assemble(jnp.sum(matrix[None, :, :] * vectors[:, None, :], 2))

            def curvature(vectors):
                return jnp.sum(vectors * operate(vectors), 1)

        rhs = jnp.stack([-geometry[4], jnp.ones((atoms,), jnp.float32)])
        solution = jnp.zeros_like(rhs)
        resid = rhs
        direction = rhs
        norm_now = jnp.sum(resid * resid, 1)
        own_index = me * per_brick + jnp.arange(per_brick, dtype=jnp.int32)
        for iteration in range(ITERS - 1):
            image = operate(direction)
            step_size = norm_now / jnp.sum(direction * image, 1)
            solution = solution + step_size[:, None] * direction
            resid = resid - step_size[:, None] * image
            norm_next = jnp.sum(resid * resid, 1)
            direction = resid + (norm_next / norm_now)[:, None] * direction
            norm_now = norm_next
        fields = pulling_fields(
            own, geometry, own_index[:, None] == col_index[None, :],
            [solution[0], solution[1], direction[0], direction[1]],
        ).reshape(2, 2, 3, per_brick)
        own_solution = lax.dynamic_slice_in_dim(solution, me * per_brick, per_brick, 1)
        own_direction = lax.dynamic_slice_in_dim(direction, me * per_brick, per_brick, 1)
        solution_sums = jnp.sum(solution, 1)
        direction_sums = jnp.sum(direction, 1)
        last_curvature = curvature(direction)
        step_size = norm_now / last_curvature
        totals = solution_sums + step_size * direction_sums
        weights = jnp.where(jnp.arange(2) == 0, 1.0, -(totals[::-1] / totals))
        own_charges = jnp.sum(weights[:, None] * (own_solution + step_size[:, None] * own_direction), 0)
        field = jnp.sum(
            weights[:, None, None] * (fields[0] + step_size[:, None, None] * fields[1]), 0
        )
        forces = (own_charges[None, :] * field).reshape(3, 1, 1, per_brick)
        return (own_charges.reshape(1, 1, per_brick), forces)

    return shards


def solution(mesh):
    in_specs = (
        P(None, "row", "col", None),
        P("row", "col", None),
        P(None, "row", "col", None),
        P(),
        P(),
        P(),
    )
    out_specs = (P("row", "col", None), P(None, "row", "col", None))
    shards = make_shards(mesh.shape["row"], mesh.shape["col"])
    return jax.shard_map(shards, mesh=mesh, in_specs=in_specs, out_specs=out_specs, check_vma=False)
```

```python
import jax
import jax.numpy as jnp
from jax import lax
from jax.sharding import PartitionSpec as P
from jax.experimental import pallas as pl
from jax.experimental.pallas import tpu as pltpu

ITERS = 3


ROOT_PI = 1.7724538509055159
TWO_ROOT = 1.1283791670955126

PAIR_LIMIT = 16 * 1024 * 1024
FEATURES = 6
CURVATURE_ORDER = (2, 1, 0, 3, 4)
BLOCKS = (
    ((0, 0), (1, 1), (0, 1), (0, 2), (1, 2)),
    ((2, 2), (3, 3), (2, 3), (0, 3), (1, 3)),
)


def screened(row_geometry, col_geometry, self_pair):
    squared = jnp.zeros(self_pair.shape, row_geometry.dtype)
    for axis_id in range(3):
        separation = row_geometry[axis_id][:, None] - col_geometry[axis_id][None, :]
        squared = squared + separation * separation
    squared = jnp.where(self_pair, 1.0, squared)
    inverse = lax.rsqrt(squared)
    screening = lax.rsqrt(2.0 * (row_geometry[3][:, None] + col_geometry[3][None, :]))
    off = lax.erf(screening * squared * inverse) * inverse
    return jnp.where(self_pair, row_geometry[5][:, None], off)


def pulling(row_geometry, col_geometry, self_pair, col_charges):
    separations = []
    squared = jnp.zeros(self_pair.shape, row_geometry.dtype)
    for axis_id in range(3):
        separation = row_geometry[axis_id][:, None] - col_geometry[axis_id][None, :]
        separations.append(separation)
        squared = squared + separation * separation
    squared = jnp.where(self_pair, 1.0, squared)
    inverse = lax.rsqrt(squared)
    screening = lax.rsqrt(2.0 * (row_geometry[3][:, None] + col_geometry[3][None, :]))
    slope = (
        (
            lax.erf(screening * squared * inverse) * inverse
            - TWO_ROOT * screening * jnp.exp(-screening * screening * squared)
        )
        * inverse
        * inverse
    )
    slope = jnp.where(self_pair, 0.0, slope) * col_charges[None, :]
    return jnp.stack(
        [
            jnp.sum(slope * separations[0], 1),
            jnp.sum(slope * separations[1], 1),
            jnp.sum(slope * separations[2], 1),
        ]
    )


def prep_kernel(hard_ref, width_ref, pos_ref, species_ref, desc_ref, readout_ref, out_ref):
    kinds = species_ref[...]
    hard = jnp.zeros(kinds.shape, jnp.float32)
    width = jnp.zeros(kinds.shape, jnp.float32)
    for kind in range(hard_ref.shape[0]):
        hard = jnp.where(kinds == kind, hard_ref[kind], hard)
        width = jnp.where(kinds == kind, width_ref[kind], width)
    scores = lax.dot_general(
        readout_ref[...],
        desc_ref[...],
        (((1,), (1,)), ((), ())),
        precision=lax.Precision.HIGHEST,
        preferred_element_type=jnp.float32,
    )
    negativity = jnp.zeros(kinds.shape, jnp.float32)
    for kind in range(hard_ref.shape[0]):
        negativity = jnp.where(kinds == kind, scores[kind : kind + 1, :], negativity)
    self_term = hard + 1.0 / (width * ROOT_PI)
    per_brick = kinds.shape[-1]
    features = [pos_ref[0], pos_ref[1], pos_ref[2], width * width, negativity, self_term]
    features = features + [jnp.zeros(kinds.shape, jnp.float32)] * (out_ref.shape[-1] // per_brick - len(features))
    block = jnp.concatenate(features, 1)
    for slot in range(out_ref.shape[0]):
        out_ref[slot] = block


def prep(positions, species, descriptors, readout, hardness, widths, devices):
    per_brick = species.shape[-1]
    smem = pltpu.MemorySpace.SMEM if hasattr(pltpu, "MemorySpace") else pltpu.SMEM
    return pl.pallas_call(
        prep_kernel,
        in_specs=[
            pl.BlockSpec(memory_space=smem),
            pl.BlockSpec(memory_space=smem),
            pl.BlockSpec(memory_space=pltpu.VMEM),
            pl.BlockSpec(memory_space=pltpu.VMEM),
            pl.BlockSpec(memory_space=pltpu.VMEM),
            pl.BlockSpec(memory_space=pltpu.VMEM),
        ],
        out_specs=pl.BlockSpec(memory_space=pltpu.VMEM),
        out_shape=jax.ShapeDtypeStruct((devices, 1, FEATURES * per_brick), jnp.float32),
    )(
        hardness,
        widths,
        positions.reshape(3, 1, per_brick),
        species.reshape(1, per_brick),
        descriptors.reshape(descriptors.shape[0], per_brick).T,
        readout,
    )


def pulling_fields(row_geometry, col_geometry, self_pair, vectors):
    separations = []
    squared = jnp.zeros(self_pair.shape, row_geometry.dtype)
    for axis_id in range(3):
        separation = row_geometry[axis_id][:, None] - col_geometry[axis_id][None, :]
        separations.append(separation)
        squared = squared + separation * separation
    squared = jnp.where(self_pair, 1.0, squared)
    inverse = lax.rsqrt(squared)
    screening = lax.rsqrt(2.0 * (row_geometry[3][:, None] + col_geometry[3][None, :]))
    slope = (
        (
            lax.erf(screening * squared * inverse) * inverse
            - TWO_ROOT * screening * jnp.exp(-screening * screening * squared)
        )
        * inverse
        * inverse
    )
    slope = jnp.where(self_pair, 0.0, slope)
    return jnp.stack(
        [jnp.stack([jnp.sum(slope * vector[None, :] * separation, 1) for separation in separations]) for vector in vectors]
    )


def make_shards(rows, cols):
    devices = rows * cols
    everyone = ("row", "col")

    def gather_all(piece):
        spread = jnp.broadcast_to(piece[None], (devices,) + piece.shape)
        got = lax.all_to_all(spread, everyone, 0, 0, tiled=True)
        return jnp.moveaxis(got, 0, 1).reshape(piece.shape[0], -1)

    def shards(positions, species, descriptors, readout, hardness, widths):
        per_brick = species.shape[-1]
        atoms = devices * per_brick
        me = lax.axis_index("row") * cols + lax.axis_index("col")
        payload = prep(positions, species, descriptors, readout, hardness, widths, devices)
        got = lax.all_to_all(payload, everyone, 0, 0, tiled=True)
        geometry = jnp.moveaxis(got.reshape(devices, FEATURES, per_brick), 0, 1).reshape(FEATURES, atoms)
        own = lax.dynamic_slice_in_dim(geometry, me * per_brick, per_brick, 1)
        col_index = jnp.arange(atoms, dtype=jnp.int32)

        pair = devices % 2 == 0 and (atoms // 2) * atoms * 4 <= PAIR_LIMIT
        if pair:
            parity = me % 2
            halves = devices // 2
            row_geometry = lax.dynamic_index_in_dim(
                geometry.reshape(geometry.shape[0], halves, 2, per_brick), parity, 2, keepdims=False
            ).reshape(geometry.shape[0], -1)
            brick_of = 2 * jnp.arange(halves, dtype=jnp.int32) + parity
            row_index = (brick_of[:, None] * per_brick + jnp.arange(per_brick, dtype=jnp.int32)[None]).reshape(-1)
            partner = [(i, i ^ 1) for i in range(devices)]

            def pick_rows(vectors):
                return lax.dynamic_index_in_dim(
                    vectors.reshape(2, halves, 2, per_brick), parity, 2, keepdims=False
                ).reshape(2, -1)

            def assemble(mine):
                theirs = lax.ppermute(mine, everyone, partner)
                first = jnp.where(parity == 0, mine, theirs).reshape(2, halves, per_brick)
                second = jnp.where(parity == 0, theirs, mine).reshape(2, halves, per_brick)
                return jnp.stack([first, second], 2).reshape(2, atoms)
        else:
            row_geometry = own
            row_index = me * per_brick + jnp.arange(per_brick, dtype=jnp.int32)

            def assemble(mine):
                return gather_all(mine.reshape(2, per_brick))

        if pair and atoms % 4 == 0:
            group = atoms // 4
            starts = []
            matrices = []
            for k, ((row_a, col_a), (row_b, col_b)) in enumerate(zip(BLOCKS[0], BLOCKS[1])):
                row_at = jnp.where(parity == 0, row_a, row_b) * group
                col_at = jnp.where(parity == 0, col_a, col_b) * group
                starts.append((row_at, col_at))
                offsets = jnp.arange(group, dtype=jnp.int32)
                matrices.append(
                    screened(
                        lax.dynamic_slice_in_dim(geometry, row_at, group, 1),
                        lax.dynamic_slice_in_dim(geometry, col_at, group, 1),
                        (row_at + offsets)[:, None] == (col_at + offsets)[None, :],
                    )
                )

            def partial_image(vectors):
                partial = jnp.zeros_like(vectors)
                for k, (matrix, (row_at, col_at)) in enumerate(zip(matrices, starts)):
                    col_part = lax.dynamic_slice_in_dim(vectors, col_at, group, 1)
                    forward = jnp.sum(matrix[None, :, :] * col_part[:, None, :], 2)
                    partial = lax.dynamic_update_slice_in_dim(
                        partial, lax.dynamic_slice_in_dim(partial, row_at, group, 1) + forward, row_at, 1
                    )
                    if k >= 2:
                        row_part = lax.dynamic_slice_in_dim(vectors, row_at, group, 1)
                        backward = jnp.sum(matrix[None, :, :] * row_part[:, :, None], 1)
                        partial = lax.dynamic_update_slice_in_dim(
                            partial, lax.dynamic_slice_in_dim(partial, col_at, group, 1) + backward, col_at, 1
                        )
                return partial

            def operate(vectors):
                partial = partial_image(vectors)
                return partial + lax.ppermute(partial, everyone, partner)

            def curvature(vectors):
                mine = 0.0
                for k in CURVATURE_ORDER:
                    matrix, (row_at, col_at) = matrices[k], starts[k]
                    col_part = lax.dynamic_slice_in_dim(vectors, col_at, group, 1)
                    row_part = lax.dynamic_slice_in_dim(vectors, row_at, group, 1)
                    term = jnp.sum(row_part * jnp.sum(matrix[None, :, :] * col_part[:, None, :], 2), 1)
                    mine = mine + (term if k < 2 else 2.0 * term)
                return mine + lax.ppermute(mine, everyone, partner)
        else:
            matrix = screened(row_geometry, geometry, row_index[:, None] == col_index[None, :])

            def operate(vectors):
                return assemble(jnp.sum(matrix[None, :, :] * vectors[:, None, :], 2))

            def curvature(vectors):
                return jnp.sum(vectors * operate(vectors), 1)

        rhs = jnp.stack([-geometry[4], jnp.ones((atoms,), jnp.float32)])
        solution = jnp.zeros_like(rhs)
        resid = rhs
        direction = rhs
        norm_now = jnp.sum(resid * resid, 1)
        own_index = me * per_brick + jnp.arange(per_brick, dtype=jnp.int32)
        for iteration in range(ITERS - 1):
            image = operate(direction)
            step_size = norm_now / jnp.sum(direction * image, 1)
            solution = solution + step_size[:, None] * direction
            resid = resid - step_size[:, None] * image
            norm_next = jnp.sum(resid * resid, 1)
            direction = resid + (norm_next / norm_now)[:, None] * direction
            norm_now = norm_next
        fields = pulling_fields(
            own, geometry, own_index[:, None] == col_index[None, :],
            [solution[0], solution[1], direction[0], direction[1]],
        ).reshape(2, 2, 3, per_brick)
        own_solution = lax.dynamic_slice_in_dim(solution, me * per_brick, per_brick, 1)
        own_direction = lax.dynamic_slice_in_dim(direction, me * per_brick, per_brick, 1)
        solution_sums = jnp.sum(solution, 1)
        direction_sums = jnp.sum(direction, 1)
        last_curvature = curvature(direction)
        step_size = norm_now / last_curvature
        totals = solution_sums + step_size * direction_sums
        weights = jnp.where(jnp.arange(2) == 0, 1.0, -(totals[::-1] / totals))
        own_charges = jnp.sum(weights[:, None] * (own_solution + step_size[:, None] * own_direction), 0)
        field = jnp.sum(
            weights[:, None, None] * (fields[0] + step_size[:, None, None] * fields[1]), 0
        )
        forces = (own_charges[None, :] * field).reshape(3, 1, 1, per_brick)
        return (own_charges.reshape(1, 1, per_brick), forces)

    return shards


def solution(mesh):
    in_specs = (
        P(None, "row", "col", None),
        P("row", "col", None),
        P(None, "row", "col", None),
        P(),
        P(),
        P(),
    )
    out_specs = (P("row", "col", None), P(None, "row", "col", None))
    shards = make_shards(mesh.shape["row"], mesh.shape["col"])
    return jax.shard_map(shards, mesh=mesh, in_specs=in_specs, out_specs=out_specs, check_vma=False)
```

```python
import jax
import jax.numpy as jnp
from jax import lax
from jax.sharding import PartitionSpec as P
from jax.experimental import pallas as pl
from jax.experimental.pallas import tpu as pltpu

ITERS = 3


ROOT_PI = 1.7724538509055159
TWO_ROOT = 1.1283791670955126

PAIR_LIMIT = 16 * 1024 * 1024
FEATURES = 6
BLOCKS = (
    ((0, 0), (1, 1), (0, 1), (0, 2), (1, 2)),
    ((2, 2), (3, 3), (2, 3), (0, 3), (1, 3)),
)


def screened(row_geometry, col_geometry, self_pair):
    squared = 0.0
    for axis_id in range(3):
        separation = row_geometry[axis_id][:, None] - col_geometry[axis_id][None, :]
        squared = squared + separation * separation
    if self_pair is not None:
        squared = jnp.where(self_pair, 1.0, squared)
    inverse = lax.rsqrt(squared)
    screening = lax.rsqrt(2.0 * (row_geometry[3][:, None] + col_geometry[3][None, :]))
    off = lax.erf(screening * squared * inverse) * inverse
    if self_pair is None:
        return off
    return jnp.where(self_pair, row_geometry[5][:, None], off)


def pulling(row_geometry, col_geometry, self_pair, col_charges):
    separations = []
    squared = jnp.zeros(self_pair.shape, row_geometry.dtype)
    for axis_id in range(3):
        separation = row_geometry[axis_id][:, None] - col_geometry[axis_id][None, :]
        separations.append(separation)
        squared = squared + separation * separation
    squared = jnp.where(self_pair, 1.0, squared)
    inverse = lax.rsqrt(squared)
    screening = lax.rsqrt(2.0 * (row_geometry[3][:, None] + col_geometry[3][None, :]))
    slope = (
        (
            lax.erf(screening * squared * inverse) * inverse
            - TWO_ROOT * screening * jnp.exp(-screening * screening * squared)
        )
        * inverse
        * inverse
    )
    slope = jnp.where(self_pair, 0.0, slope) * col_charges[None, :]
    return jnp.stack(
        [
            jnp.sum(slope * separations[0], 1),
            jnp.sum(slope * separations[1], 1),
            jnp.sum(slope * separations[2], 1),
        ]
    )


def prep_kernel(hard_ref, width_ref, pos_ref, species_ref, desc_ref, readout_ref, out_ref):
    kinds = species_ref[...]
    hard = jnp.zeros(kinds.shape, jnp.float32)
    width = jnp.zeros(kinds.shape, jnp.float32)
    for kind in range(hard_ref.shape[0]):
        hard = jnp.where(kinds == kind, hard_ref[kind], hard)
        width = jnp.where(kinds == kind, width_ref[kind], width)
    scores = lax.dot_general(
        readout_ref[...],
        desc_ref[...],
        (((1,), (1,)), ((), ())),
        precision=lax.Precision.HIGHEST,
        preferred_element_type=jnp.float32,
    )
    negativity = jnp.zeros(kinds.shape, jnp.float32)
    for kind in range(hard_ref.shape[0]):
        negativity = jnp.where(kinds == kind, scores[kind : kind + 1, :], negativity)
    self_term = hard + 1.0 / (width * ROOT_PI)
    per_brick = kinds.shape[-1]
    features = [pos_ref[0], pos_ref[1], pos_ref[2], width * width, negativity, self_term]
    features = features + [jnp.zeros(kinds.shape, jnp.float32)] * (out_ref.shape[-1] // per_brick - len(features))
    block = jnp.concatenate(features, 1)
    for slot in range(out_ref.shape[0]):
        out_ref[slot] = block


def prep(positions, species, descriptors, readout, hardness, widths, devices):
    per_brick = species.shape[-1]
    smem = pltpu.MemorySpace.SMEM if hasattr(pltpu, "MemorySpace") else pltpu.SMEM
    return pl.pallas_call(
        prep_kernel,
        in_specs=[
            pl.BlockSpec(memory_space=smem),
            pl.BlockSpec(memory_space=smem),
            pl.BlockSpec(memory_space=pltpu.VMEM),
            pl.BlockSpec(memory_space=pltpu.VMEM),
            pl.BlockSpec(memory_space=pltpu.VMEM),
            pl.BlockSpec(memory_space=pltpu.VMEM),
        ],
        out_specs=pl.BlockSpec(memory_space=pltpu.VMEM),
        out_shape=jax.ShapeDtypeStruct((devices, 1, FEATURES * per_brick), jnp.float32),
    )(
        hardness,
        widths,
        positions.reshape(3, 1, per_brick),
        species.reshape(1, per_brick),
        descriptors.reshape(descriptors.shape[0], per_brick).T,
        readout,
    )


def pulling_fields(row_geometry, col_geometry, self_pair, vectors):
    separations = []
    squared = jnp.zeros(self_pair.shape, row_geometry.dtype)
    for axis_id in range(3):
        separation = row_geometry[axis_id][:, None] - col_geometry[axis_id][None, :]
        separations.append(separation)
        squared = squared + separation * separation
    squared = jnp.where(self_pair, 1.0, squared)
    inverse = lax.rsqrt(squared)
    screening = lax.rsqrt(2.0 * (row_geometry[3][:, None] + col_geometry[3][None, :]))
    slope = (
        (
            lax.erf(screening * squared * inverse) * inverse
            - TWO_ROOT * screening * jnp.exp(-screening * screening * squared)
        )
        * inverse
        * inverse
    )
    slope = jnp.where(self_pair, 0.0, slope)
    return jnp.stack(
        [jnp.stack([jnp.sum(slope * vector[None, :] * separation, 1) for separation in separations]) for vector in vectors]
    )


def make_shards(rows, cols):
    devices = rows * cols
    everyone = ("row", "col")

    def gather_all(piece):
        spread = jnp.broadcast_to(piece[None], (devices,) + piece.shape)
        got = lax.all_to_all(spread, everyone, 0, 0, tiled=True)
        return jnp.moveaxis(got, 0, 1).reshape(piece.shape[0], -1)

    def shards(positions, species, descriptors, readout, hardness, widths):
        per_brick = species.shape[-1]
        atoms = devices * per_brick
        me = lax.axis_index("row") * cols + lax.axis_index("col")
        payload = prep(positions, species, descriptors, readout, hardness, widths, devices)
        got = lax.all_to_all(payload, everyone, 0, 0, tiled=True)
        geometry = jnp.moveaxis(got.reshape(devices, FEATURES, per_brick), 0, 1).reshape(FEATURES, atoms)
        own = lax.dynamic_slice_in_dim(geometry, me * per_brick, per_brick, 1)
        col_index = jnp.arange(atoms, dtype=jnp.int32)

        pair = devices % 2 == 0 and (atoms // 2) * atoms * 4 <= PAIR_LIMIT
        if pair:
            parity = me % 2
            halves = devices // 2
            row_geometry = lax.dynamic_index_in_dim(
                geometry.reshape(geometry.shape[0], halves, 2, per_brick), parity, 2, keepdims=False
            ).reshape(geometry.shape[0], -1)
            brick_of = 2 * jnp.arange(halves, dtype=jnp.int32) + parity
            row_index = (brick_of[:, None] * per_brick + jnp.arange(per_brick, dtype=jnp.int32)[None]).reshape(-1)
            partner = [(i, i ^ 1) for i in range(devices)]

            def pick_rows(vectors):
                return lax.dynamic_index_in_dim(
                    vectors.reshape(2, halves, 2, per_brick), parity, 2, keepdims=False
                ).reshape(2, -1)

            def assemble(mine):
                theirs = lax.ppermute(mine, everyone, partner)
                first = jnp.where(parity == 0, mine, theirs).reshape(2, halves, per_brick)
                second = jnp.where(parity == 0, theirs, mine).reshape(2, halves, per_brick)
                return jnp.stack([first, second], 2).reshape(2, atoms)
        else:
            row_geometry = own
            row_index = me * per_brick + jnp.arange(per_brick, dtype=jnp.int32)

            def assemble(mine):
                return gather_all(mine.reshape(2, per_brick))

        if pair and atoms % 4 == 0:
            group = atoms // 4
            starts = []
            matrices = []
            for k, ((row_a, col_a), (row_b, col_b)) in enumerate(zip(BLOCKS[0], BLOCKS[1])):
                row_at = jnp.where(parity == 0, row_a, row_b) * group
                col_at = jnp.where(parity == 0, col_a, col_b) * group
                starts.append((row_at, col_at))
                offsets = jnp.arange(group, dtype=jnp.int32)
                matrices.append(
                    screened(
                        lax.dynamic_slice_in_dim(geometry, row_at, group, 1),
                        lax.dynamic_slice_in_dim(geometry, col_at, group, 1),
                        offsets[:, None] == offsets[None, :] if k < 2 else None,
                    )
                )

            def partial_image(vectors):
                partial = jnp.zeros_like(vectors)
                for k, (matrix, (row_at, col_at)) in enumerate(zip(matrices, starts)):
                    col_part = lax.dynamic_slice_in_dim(vectors, col_at, group, 1)
                    forward = jnp.sum(matrix[None, :, :] * col_part[:, None, :], 2)
                    partial = lax.dynamic_update_slice_in_dim(
                        partial, lax.dynamic_slice_in_dim(partial, row_at, group, 1) + forward, row_at, 1
                    )
                    if k >= 2:
                        row_part = lax.dynamic_slice_in_dim(vectors, row_at, group, 1)
                        backward = jnp.sum(matrix[None, :, :] * row_part[:, :, None], 1)
                        partial = lax.dynamic_update_slice_in_dim(
                            partial, lax.dynamic_slice_in_dim(partial, col_at, group, 1) + backward, col_at, 1
                        )
                return partial

            def operate(vectors):
                partial = partial_image(vectors)
                return partial + lax.ppermute(partial, everyone, partner)

            def curvature(vectors):
                mine = 0.0
                for k, (matrix, (row_at, col_at)) in enumerate(zip(matrices, starts)):
                    col_part = lax.dynamic_slice_in_dim(vectors, col_at, group, 1)
                    row_part = lax.dynamic_slice_in_dim(vectors, row_at, group, 1)
                    term = jnp.sum(row_part * jnp.sum(matrix[None, :, :] * col_part[:, None, :], 2), 1)
                    mine = mine + (term if k < 2 else 2.0 * term)
                return mine + lax.ppermute(mine, everyone, partner)
        else:
            matrix = screened(row_geometry, geometry, row_index[:, None] == col_index[None, :])

            def operate(vectors):
                return assemble(jnp.sum(matrix[None, :, :] * vectors[:, None, :], 2))

            def curvature(vectors):
                return jnp.sum(vectors * operate(vectors), 1)

        rhs = jnp.stack([-geometry[4], jnp.ones((atoms,), jnp.float32)])
        solution = jnp.zeros_like(rhs)
        resid = rhs
        direction = rhs
        norm_now = jnp.sum(resid * resid, 1)
        own_index = me * per_brick + jnp.arange(per_brick, dtype=jnp.int32)
        for iteration in range(ITERS - 1):
            image = operate(direction)
            step_size = norm_now / jnp.sum(direction * image, 1)
            solution = solution + step_size[:, None] * direction
            resid = resid - step_size[:, None] * image
            norm_next = jnp.sum(resid * resid, 1)
            direction = resid + (norm_next / norm_now)[:, None] * direction
            norm_now = norm_next
        fields = pulling_fields(
            own, geometry, own_index[:, None] == col_index[None, :],
            [solution[0], solution[1], direction[0], direction[1]],
        ).reshape(2, 2, 3, per_brick)
        own_solution = lax.dynamic_slice_in_dim(solution, me * per_brick, per_brick, 1)
        own_direction = lax.dynamic_slice_in_dim(direction, me * per_brick, per_brick, 1)
        solution_sums = jnp.sum(solution, 1)
        direction_sums = jnp.sum(direction, 1)
        last_curvature = curvature(direction)
        step_size = norm_now / last_curvature
        totals = solution_sums + step_size * direction_sums
        weights = jnp.where(jnp.arange(2) == 0, 1.0, -(totals[::-1] / totals))
        own_charges = jnp.sum(weights[:, None] * (own_solution + step_size[:, None] * own_direction), 0)
        field = jnp.sum(
            weights[:, None, None] * (fields[0] + step_size[:, None, None] * fields[1]), 0
        )
        forces = (own_charges[None, :] * field).reshape(3, 1, 1, per_brick)
        return (own_charges.reshape(1, 1, per_brick), forces)

    return shards


def solution(mesh):
    in_specs = (
        P(None, "row", "col", None),
        P("row", "col", None),
        P(None, "row", "col", None),
        P(),
        P(),
        P(),
    )
    out_specs = (P("row", "col", None), P(None, "row", "col", None))
    shards = make_shards(mesh.shape["row"], mesh.shape["col"])
    return jax.shard_map(shards, mesh=mesh, in_specs=in_specs, out_specs=out_specs, check_vma=False)
```

```python
import jax
import jax.numpy as jnp
from jax import lax
from jax.sharding import PartitionSpec as P
from jax.experimental import pallas as pl
from jax.experimental.pallas import tpu as pltpu

ITERS = 3


ROOT_PI = 1.7724538509055159
TWO_ROOT = 1.1283791670955126

PAIR_LIMIT = 16 * 1024 * 1024
FEATURES = 6
BLOCKS = (
    ((0, 0), (1, 1), (0, 1), (0, 2), (1, 2)),
    ((2, 2), (3, 3), (2, 3), (0, 3), (1, 3)),
)


def screened(row_geometry, col_geometry, self_pair):
    squared = 0.0
    for axis_id in range(3):
        separation = row_geometry[axis_id][:, None] - col_geometry[axis_id][None, :]
        squared = squared + separation * separation
    if self_pair is not None:
        squared = jnp.where(self_pair, 1.0, squared)
    inverse = lax.rsqrt(squared)
    screening = lax.rsqrt(row_geometry[3][:, None] + col_geometry[3][None, :])
    off = lax.erf(screening * squared * inverse) * inverse
    if self_pair is None:
        return off
    return jnp.where(self_pair, row_geometry[5][:, None], off)


def pulling(row_geometry, col_geometry, self_pair, col_charges):
    separations = []
    squared = jnp.zeros(self_pair.shape, row_geometry.dtype)
    for axis_id in range(3):
        separation = row_geometry[axis_id][:, None] - col_geometry[axis_id][None, :]
        separations.append(separation)
        squared = squared + separation * separation
    squared = jnp.where(self_pair, 1.0, squared)
    inverse = lax.rsqrt(squared)
    screening = lax.rsqrt(row_geometry[3][:, None] + col_geometry[3][None, :])
    slope = (
        (
            lax.erf(screening * squared * inverse) * inverse
            - TWO_ROOT * screening * jnp.exp(-screening * screening * squared)
        )
        * inverse
        * inverse
    )
    slope = jnp.where(self_pair, 0.0, slope) * col_charges[None, :]
    return jnp.stack(
        [
            jnp.sum(slope * separations[0], 1),
            jnp.sum(slope * separations[1], 1),
            jnp.sum(slope * separations[2], 1),
        ]
    )


def prep_kernel(hard_ref, width_ref, pos_ref, species_ref, desc_ref, readout_ref, out_ref):
    kinds = species_ref[...]
    hard = jnp.zeros(kinds.shape, jnp.float32)
    width = jnp.zeros(kinds.shape, jnp.float32)
    for kind in range(hard_ref.shape[0]):
        hard = jnp.where(kinds == kind, hard_ref[kind], hard)
        width = jnp.where(kinds == kind, width_ref[kind], width)
    scores = lax.dot_general(
        readout_ref[...],
        desc_ref[...],
        (((1,), (1,)), ((), ())),
        precision=lax.Precision.HIGHEST,
        preferred_element_type=jnp.float32,
    )
    negativity = jnp.zeros(kinds.shape, jnp.float32)
    for kind in range(hard_ref.shape[0]):
        negativity = jnp.where(kinds == kind, scores[kind : kind + 1, :], negativity)
    self_term = hard + 1.0 / (width * ROOT_PI)
    per_brick = kinds.shape[-1]
    features = [pos_ref[0], pos_ref[1], pos_ref[2], 2.0 * (width * width), negativity, self_term]
    features = features + [jnp.zeros(kinds.shape, jnp.float32)] * (out_ref.shape[-1] // per_brick - len(features))
    block = jnp.concatenate(features, 1)
    for slot in range(out_ref.shape[0]):
        out_ref[slot] = block


def prep(positions, species, descriptors, readout, hardness, widths, devices):
    per_brick = species.shape[-1]
    smem = pltpu.MemorySpace.SMEM if hasattr(pltpu, "MemorySpace") else pltpu.SMEM
    return pl.pallas_call(
        prep_kernel,
        in_specs=[
            pl.BlockSpec(memory_space=smem),
            pl.BlockSpec(memory_space=smem),
            pl.BlockSpec(memory_space=pltpu.VMEM),
            pl.BlockSpec(memory_space=pltpu.VMEM),
            pl.BlockSpec(memory_space=pltpu.VMEM),
            pl.BlockSpec(memory_space=pltpu.VMEM),
        ],
        out_specs=pl.BlockSpec(memory_space=pltpu.VMEM),
        out_shape=jax.ShapeDtypeStruct((devices, 1, FEATURES * per_brick), jnp.float32),
    )(
        hardness,
        widths,
        positions.reshape(3, 1, per_brick),
        species.reshape(1, per_brick),
        descriptors.reshape(descriptors.shape[0], per_brick).T,
        readout,
    )


def pulling_fields(row_geometry, col_geometry, self_pair, vectors):
    separations = []
    squared = jnp.zeros(self_pair.shape, row_geometry.dtype)
    for axis_id in range(3):
        separation = row_geometry[axis_id][:, None] - col_geometry[axis_id][None, :]
        separations.append(separation)
        squared = squared + separation * separation
    squared = jnp.where(self_pair, 1.0, squared)
    inverse = lax.rsqrt(squared)
    screening = lax.rsqrt(row_geometry[3][:, None] + col_geometry[3][None, :])
    slope = (
        (
            lax.erf(screening * squared * inverse) * inverse
            - TWO_ROOT * screening * jnp.exp(-screening * screening * squared)
        )
        * inverse
        * inverse
    )
    slope = jnp.where(self_pair, 0.0, slope)
    return jnp.stack(
        [jnp.stack([jnp.sum(slope * vector[None, :] * separation, 1) for separation in separations]) for vector in vectors]
    )


def make_shards(rows, cols):
    devices = rows * cols
    everyone = ("row", "col")

    def gather_all(piece):
        spread = jnp.broadcast_to(piece[None], (devices,) + piece.shape)
        got = lax.all_to_all(spread, everyone, 0, 0, tiled=True)
        return jnp.moveaxis(got, 0, 1).reshape(piece.shape[0], -1)

    def shards(positions, species, descriptors, readout, hardness, widths):
        per_brick = species.shape[-1]
        atoms = devices * per_brick
        me = lax.axis_index("row") * cols + lax.axis_index("col")
        payload = prep(positions, species, descriptors, readout, hardness, widths, devices)
        got = lax.all_to_all(payload, everyone, 0, 0, tiled=True)
        geometry = jnp.moveaxis(got.reshape(devices, FEATURES, per_brick), 0, 1).reshape(FEATURES, atoms)
        own = lax.dynamic_slice_in_dim(geometry, me * per_brick, per_brick, 1)
        col_index = jnp.arange(atoms, dtype=jnp.int32)

        pair = devices % 2 == 0 and (atoms // 2) * atoms * 4 <= PAIR_LIMIT
        if pair:
            parity = me % 2
            halves = devices // 2
            row_geometry = lax.dynamic_index_in_dim(
                geometry.reshape(geometry.shape[0], halves, 2, per_brick), parity, 2, keepdims=False
            ).reshape(geometry.shape[0], -1)
            brick_of = 2 * jnp.arange(halves, dtype=jnp.int32) + parity
            row_index = (brick_of[:, None] * per_brick + jnp.arange(per_brick, dtype=jnp.int32)[None]).reshape(-1)
            partner = [(i, i ^ 1) for i in range(devices)]

            def pick_rows(vectors):
                return lax.dynamic_index_in_dim(
                    vectors.reshape(2, halves, 2, per_brick), parity, 2, keepdims=False
                ).reshape(2, -1)

            def assemble(mine):
                theirs = lax.ppermute(mine, everyone, partner)
                first = jnp.where(parity == 0, mine, theirs).reshape(2, halves, per_brick)
                second = jnp.where(parity == 0, theirs, mine).reshape(2, halves, per_brick)
                return jnp.stack([first, second], 2).reshape(2, atoms)
        else:
            row_geometry = own
            row_index = me * per_brick + jnp.arange(per_brick, dtype=jnp.int32)

            def assemble(mine):
                return gather_all(mine.reshape(2, per_brick))

        if pair and atoms % 4 == 0:
            group = atoms // 4
            starts = []
            matrices = []
            for k, ((row_a, col_a), (row_b, col_b)) in enumerate(zip(BLOCKS[0], BLOCKS[1])):
                row_at = jnp.where(parity == 0, row_a, row_b) * group
                col_at = jnp.where(parity == 0, col_a, col_b) * group
                starts.append((row_at, col_at))
                offsets = jnp.arange(group, dtype=jnp.int32)
                matrices.append(
                    screened(
                        lax.dynamic_slice_in_dim(geometry, row_at, group, 1),
                        lax.dynamic_slice_in_dim(geometry, col_at, group, 1),
                        offsets[:, None] == offsets[None, :] if k < 2 else None,
                    )
                )

            def partial_image(vectors, second_ones=False):
                partial = jnp.zeros_like(vectors)
                for k, (matrix, (row_at, col_at)) in enumerate(zip(matrices, starts)):
                    col_part = lax.dynamic_slice_in_dim(vectors, col_at, group, 1)
                    if second_ones:
                        forward = jnp.stack([jnp.sum(matrix * col_part[0][None, :], 1), jnp.sum(matrix, 1)])
                    else:
                        forward = jnp.sum(matrix[None, :, :] * col_part[:, None, :], 2)
                    partial = lax.dynamic_update_slice_in_dim(
                        partial, lax.dynamic_slice_in_dim(partial, row_at, group, 1) + forward, row_at, 1
                    )
                    if k >= 2:
                        row_part = lax.dynamic_slice_in_dim(vectors, row_at, group, 1)
                        if second_ones:
                            backward = jnp.stack([jnp.sum(matrix * row_part[0][:, None], 0), jnp.sum(matrix, 0)])
                        else:
                            backward = jnp.sum(matrix[None, :, :] * row_part[:, :, None], 1)
                        partial = lax.dynamic_update_slice_in_dim(
                            partial, lax.dynamic_slice_in_dim(partial, col_at, group, 1) + backward, col_at, 1
                        )
                return partial

            def operate(vectors, second_ones=False):
                partial = partial_image(vectors, second_ones)
                return partial + lax.ppermute(partial, everyone, partner)

            def curvature(vectors):
                mine = 0.0
                for k, (matrix, (row_at, col_at)) in enumerate(zip(matrices, starts)):
                    col_part = lax.dynamic_slice_in_dim(vectors, col_at, group, 1)
                    row_part = lax.dynamic_slice_in_dim(vectors, row_at, group, 1)
                    term = jnp.sum(row_part * jnp.sum(matrix[None, :, :] * col_part[:, None, :], 2), 1)
                    mine = mine + (term if k < 2 else 2.0 * term)
                return mine + lax.ppermute(mine, everyone, partner)
        else:
            matrix = screened(row_geometry, geometry, row_index[:, None] == col_index[None, :])

            def operate(vectors, second_ones=False):
                return assemble(jnp.sum(matrix[None, :, :] * vectors[:, None, :], 2))

            def curvature(vectors):
                return jnp.sum(vectors * operate(vectors), 1)

        rhs = jnp.stack([-geometry[4], jnp.ones((atoms,), jnp.float32)])
        solution = jnp.zeros_like(rhs)
        resid = rhs
        direction = rhs
        norm_now = jnp.sum(resid * resid, 1)
        own_index = me * per_brick + jnp.arange(per_brick, dtype=jnp.int32)
        for iteration in range(ITERS - 1):
            image = operate(direction, second_ones=iteration == 0)
            step_size = norm_now / jnp.sum(direction * image, 1)
            solution = solution + step_size[:, None] * direction
            resid = resid - step_size[:, None] * image
            norm_next = jnp.sum(resid * resid, 1)
            direction = resid + (norm_next / norm_now)[:, None] * direction
            norm_now = norm_next
        fields = pulling_fields(
            own, geometry, own_index[:, None] == col_index[None, :],
            [solution[0], solution[1], direction[0], direction[1]],
        ).reshape(2, 2, 3, per_brick)
        own_solution = lax.dynamic_slice_in_dim(solution, me * per_brick, per_brick, 1)
        own_direction = lax.dynamic_slice_in_dim(direction, me * per_brick, per_brick, 1)
        solution_sums = jnp.sum(solution, 1)
        direction_sums = jnp.sum(direction, 1)
        last_curvature = curvature(direction)
        step_size = norm_now / last_curvature
        totals = solution_sums + step_size * direction_sums
        weights = jnp.where(jnp.arange(2) == 0, 1.0, -(totals[::-1] / totals))
        own_charges = jnp.sum(weights[:, None] * (own_solution + step_size[:, None] * own_direction), 0)
        field = jnp.sum(
            weights[:, None, None] * (fields[0] + step_size[:, None, None] * fields[1]), 0
        )
        forces = (own_charges[None, :] * field).reshape(3, 1, 1, per_brick)
        return (own_charges.reshape(1, 1, per_brick), forces)

    return shards


def solution(mesh):
    in_specs = (
        P(None, "row", "col", None),
        P("row", "col", None),
        P(None, "row", "col", None),
        P(),
        P(),
        P(),
    )
    out_specs = (P("row", "col", None), P(None, "row", "col", None))
    shards = make_shards(mesh.shape["row"], mesh.shape["col"])
    return jax.shard_map(shards, mesh=mesh, in_specs=in_specs, out_specs=out_specs, check_vma=False)
```

```python
import jax
import jax.numpy as jnp
from jax import lax
from jax.sharding import PartitionSpec as P
from jax.experimental import pallas as pl
from jax.experimental.pallas import tpu as pltpu

ITERS = 3


ROOT_PI = 1.7724538509055159
TWO_ROOT = 1.1283791670955126

PAIR_LIMIT = 16 * 1024 * 1024
FEATURES = 6
BLOCKS = (
    ((0, 0), (1, 1), (0, 1), (0, 2), (1, 2)),
    ((2, 2), (3, 3), (2, 3), (0, 3), (1, 3)),
)


def screened(row_geometry, col_geometry, self_pair):
    squared = 0.0
    for axis_id in range(3):
        separation = row_geometry[axis_id][:, None] - col_geometry[axis_id][None, :]
        squared = squared + separation * separation
    if self_pair is not None:
        squared = jnp.where(self_pair, 1.0, squared)
    inverse = lax.rsqrt(squared)
    screening = lax.rsqrt(row_geometry[3][:, None] + col_geometry[3][None, :])
    off = lax.erf(screening * squared * inverse) * inverse
    if self_pair is None:
        return off
    return jnp.where(self_pair, row_geometry[5][:, None], off)


def pulling(row_geometry, col_geometry, self_pair, col_charges):
    separations = []
    squared = jnp.zeros(self_pair.shape, row_geometry.dtype)
    for axis_id in range(3):
        separation = row_geometry[axis_id][:, None] - col_geometry[axis_id][None, :]
        separations.append(separation)
        squared = squared + separation * separation
    squared = jnp.where(self_pair, 1.0, squared)
    inverse = lax.rsqrt(squared)
    screening = lax.rsqrt(row_geometry[3][:, None] + col_geometry[3][None, :])
    slope = (
        (
            lax.erf(screening * squared * inverse) * inverse
            - TWO_ROOT * screening * jnp.exp(-screening * screening * squared)
        )
        * inverse
        * inverse
    )
    slope = jnp.where(self_pair, 0.0, slope) * col_charges[None, :]
    return jnp.stack(
        [
            jnp.sum(slope * separations[0], 1),
            jnp.sum(slope * separations[1], 1),
            jnp.sum(slope * separations[2], 1),
        ]
    )


def prep_kernel(hard_ref, width_ref, pos_ref, species_ref, desc_ref, readout_ref, out_ref):
    kinds = species_ref[...]
    hard = jnp.zeros(kinds.shape, jnp.float32)
    width = jnp.zeros(kinds.shape, jnp.float32)
    for kind in range(hard_ref.shape[0]):
        hard = jnp.where(kinds == kind, hard_ref[kind], hard)
        width = jnp.where(kinds == kind, width_ref[kind], width)
    scores = lax.dot_general(
        readout_ref[...],
        desc_ref[...],
        (((1,), (1,)), ((), ())),
        precision=lax.Precision.HIGHEST,
        preferred_element_type=jnp.float32,
    )
    negativity = jnp.zeros(kinds.shape, jnp.float32)
    for kind in range(hard_ref.shape[0]):
        negativity = jnp.where(kinds == kind, scores[kind : kind + 1, :], negativity)
    self_term = hard + 1.0 / (width * ROOT_PI)
    per_brick = kinds.shape[-1]
    features = [pos_ref[0], pos_ref[1], pos_ref[2], 2.0 * (width * width), negativity, self_term]
    features = features + [jnp.zeros(kinds.shape, jnp.float32)] * (out_ref.shape[-1] // per_brick - len(features))
    block = jnp.concatenate(features, 1)
    for slot in range(out_ref.shape[0]):
        out_ref[slot] = block


def prep(positions, species, descriptors, readout, hardness, widths, devices):
    per_brick = species.shape[-1]
    smem = pltpu.MemorySpace.SMEM if hasattr(pltpu, "MemorySpace") else pltpu.SMEM
    return pl.pallas_call(
        prep_kernel,
        in_specs=[
            pl.BlockSpec(memory_space=smem),
            pl.BlockSpec(memory_space=smem),
            pl.BlockSpec(memory_space=pltpu.VMEM),
            pl.BlockSpec(memory_space=pltpu.VMEM),
            pl.BlockSpec(memory_space=pltpu.VMEM),
            pl.BlockSpec(memory_space=pltpu.VMEM),
        ],
        out_specs=pl.BlockSpec(memory_space=pltpu.VMEM),
        out_shape=jax.ShapeDtypeStruct((devices, 1, FEATURES * per_brick), jnp.float32),
    )(
        hardness,
        widths,
        positions.reshape(3, 1, per_brick),
        species.reshape(1, per_brick),
        descriptors.reshape(descriptors.shape[0], per_brick).T,
        readout,
    )


def pulling_fields(row_geometry, col_geometry, self_pair, vectors):
    separations = []
    squared = jnp.zeros(self_pair.shape, row_geometry.dtype)
    for axis_id in range(3):
        separation = row_geometry[axis_id][:, None] - col_geometry[axis_id][None, :]
        separations.append(separation)
        squared = squared + separation * separation
    squared = jnp.where(self_pair, 1.0, squared)
    inverse = lax.rsqrt(squared)
    screening = lax.rsqrt(row_geometry[3][:, None] + col_geometry[3][None, :])
    slope = (
        (
            lax.erf(screening * squared * inverse) * inverse
            - TWO_ROOT * screening * jnp.exp(-screening * screening * squared)
        )
        * inverse
        * inverse
    )
    slope = jnp.where(self_pair, 0.0, slope)
    return jnp.stack(
        [jnp.stack([jnp.sum(slope * vector[None, :] * separation, 1) for separation in separations]) for vector in vectors]
    )


def make_shards(rows, cols):
    devices = rows * cols
    everyone = ("row", "col")

    def gather_all(piece):
        spread = jnp.broadcast_to(piece[None], (devices,) + piece.shape)
        got = lax.all_to_all(spread, everyone, 0, 0, tiled=True)
        return jnp.moveaxis(got, 0, 1).reshape(piece.shape[0], -1)

    def shards(positions, species, descriptors, readout, hardness, widths):
        per_brick = species.shape[-1]
        atoms = devices * per_brick
        me = lax.axis_index("row") * cols + lax.axis_index("col")
        payload = prep(positions, species, descriptors, readout, hardness, widths, devices)
        got = lax.all_to_all(payload, everyone, 0, 0, tiled=True)
        geometry = jnp.moveaxis(got.reshape(devices, FEATURES, per_brick), 0, 1).reshape(FEATURES, atoms)
        own = lax.dynamic_slice_in_dim(geometry, me * per_brick, per_brick, 1)
        col_index = jnp.arange(atoms, dtype=jnp.int32)

        pair = devices % 2 == 0 and (atoms // 2) * atoms * 4 <= PAIR_LIMIT
        if pair:
            parity = me % 2
            halves = devices // 2
            row_geometry = lax.dynamic_index_in_dim(
                geometry.reshape(geometry.shape[0], halves, 2, per_brick), parity, 2, keepdims=False
            ).reshape(geometry.shape[0], -1)
            brick_of = 2 * jnp.arange(halves, dtype=jnp.int32) + parity
            row_index = (brick_of[:, None] * per_brick + jnp.arange(per_brick, dtype=jnp.int32)[None]).reshape(-1)
            partner = [(i, i ^ 1) for i in range(devices)]

            def pick_rows(vectors):
                return lax.dynamic_index_in_dim(
                    vectors.reshape(2, halves, 2, per_brick), parity, 2, keepdims=False
                ).reshape(2, -1)

            def assemble(mine):
                theirs = lax.ppermute(mine, everyone, partner)
                first = jnp.where(parity == 0, mine, theirs).reshape(2, halves, per_brick)
                second = jnp.where(parity == 0, theirs, mine).reshape(2, halves, per_brick)
                return jnp.stack([first, second], 2).reshape(2, atoms)
        else:
            row_geometry = own
            row_index = me * per_brick + jnp.arange(per_brick, dtype=jnp.int32)

            def assemble(mine):
                return gather_all(mine.reshape(2, per_brick))

        if pair and atoms % 4 == 0:
            group = atoms // 4
            starts = []
            matrices = []
            for k, ((row_a, col_a), (row_b, col_b)) in enumerate(zip(BLOCKS[0], BLOCKS[1])):
                row_at = jnp.where(parity == 0, row_a, row_b) * group
                col_at = jnp.where(parity == 0, col_a, col_b) * group
                starts.append((row_at, col_at))
                offsets = jnp.arange(group, dtype=jnp.int32)
                matrices.append(
                    screened(
                        lax.dynamic_slice_in_dim(geometry, row_at, group, 1),
                        lax.dynamic_slice_in_dim(geometry, col_at, group, 1),
                        offsets[:, None] == offsets[None, :] if k < 2 else None,
                    )
                )

            def partial_image(vectors):
                partial = jnp.zeros_like(vectors)
                for k, (matrix, (row_at, col_at)) in enumerate(zip(matrices, starts)):
                    col_part = lax.dynamic_slice_in_dim(vectors, col_at, group, 1)
                    forward = jnp.sum(matrix[None, :, :] * col_part[:, None, :], 2)
                    partial = lax.dynamic_update_slice_in_dim(
                        partial, lax.dynamic_slice_in_dim(partial, row_at, group, 1) + forward, row_at, 1
                    )
                    if k >= 2:
                        row_part = lax.dynamic_slice_in_dim(vectors, row_at, group, 1)
                        backward = jnp.sum(matrix[None, :, :] * row_part[:, :, None], 1)
                        partial = lax.dynamic_update_slice_in_dim(
                            partial, lax.dynamic_slice_in_dim(partial, col_at, group, 1) + backward, col_at, 1
                        )
                return partial

            def operate(vectors):
                partial = partial_image(vectors)
                return partial + lax.ppermute(partial, everyone, partner)

            def curvature(vectors):
                mine = 0.0
                for k, (matrix, (row_at, col_at)) in enumerate(zip(matrices, starts)):
                    col_part = lax.dynamic_slice_in_dim(vectors, col_at, group, 1)
                    row_part = lax.dynamic_slice_in_dim(vectors, row_at, group, 1)
                    term = jnp.sum(row_part * jnp.sum(matrix[None, :, :] * col_part[:, None, :], 2), 1)
                    mine = mine + (term if k < 2 else 2.0 * term)
                return mine + lax.ppermute(mine, everyone, partner)
        else:
            matrix = screened(row_geometry, geometry, row_index[:, None] == col_index[None, :])

            def operate(vectors):
                return assemble(jnp.sum(matrix[None, :, :] * vectors[:, None, :], 2))

            def curvature(vectors):
                return jnp.sum(vectors * operate(vectors), 1)

        rhs = jnp.stack([-geometry[4], jnp.ones((atoms,), jnp.float32)])
        solution = jnp.zeros_like(rhs)
        resid = rhs
        direction = rhs
        norm_now = jnp.sum(resid * resid, 1)
        own_index = me * per_brick + jnp.arange(per_brick, dtype=jnp.int32)
        for iteration in range(ITERS - 1):
            image = operate(direction)
            step_size = norm_now / jnp.sum(direction * image, 1)
            solution = solution + step_size[:, None] * direction
            resid = resid - step_size[:, None] * image
            norm_next = jnp.sum(resid * resid, 1)
            direction = resid + (norm_next / norm_now)[:, None] * direction
            norm_now = norm_next
        fields = pulling_fields(
            own, geometry, own_index[:, None] == col_index[None, :],
            [solution[0], solution[1], direction[0], direction[1]],
        ).reshape(2, 2, 3, per_brick)
        own_solution = lax.dynamic_slice_in_dim(solution, me * per_brick, per_brick, 1)
        own_direction = lax.dynamic_slice_in_dim(direction, me * per_brick, per_brick, 1)
        solution_sums = jnp.sum(solution, 1)
        direction_sums = jnp.sum(direction, 1)
        last_curvature = curvature(direction)
        step_size = norm_now / last_curvature
        totals = solution_sums + step_size * direction_sums
        weights = jnp.where(jnp.arange(2) == 0, 1.0, -(totals[::-1] / totals))
        own_charges = jnp.sum(weights[:, None] * (own_solution + step_size[:, None] * own_direction), 0)
        field = jnp.sum(
            weights[:, None, None] * (fields[0] + step_size[:, None, None] * fields[1]), 0
        )
        forces = (own_charges[None, :] * field).reshape(3, 1, 1, per_brick)
        return (own_charges.reshape(1, 1, per_brick), forces)

    return shards


def solution(mesh):
    in_specs = (
        P(None, "row", "col", None),
        P("row", "col", None),
        P(None, "row", "col", None),
        P(),
        P(),
        P(),
    )
    out_specs = (P("row", "col", None), P(None, "row", "col", None))
    shards = make_shards(mesh.shape["row"], mesh.shape["col"])
    return jax.shard_map(shards, mesh=mesh, in_specs=in_specs, out_specs=out_specs, check_vma=False)
```

```python
import jax
import jax.numpy as jnp
from jax import lax
from jax.sharding import PartitionSpec as P
from jax.experimental import pallas as pl
from jax.experimental.pallas import tpu as pltpu

ITERS = 3


ROOT_PI = 1.7724538509055159
TWO_ROOT = 1.1283791670955126

PAIR_LIMIT = 16 * 1024 * 1024
FEATURES = 6
BLOCKS = (
    ((0, 0), (1, 1), (0, 1), (0, 2), (1, 2)),
    ((2, 2), (3, 3), (2, 3), (0, 3), (1, 3)),
)


def screened(row_geometry, col_geometry, self_pair):
    squared = 0.0
    for axis_id in range(3):
        separation = row_geometry[axis_id][:, None] - col_geometry[axis_id][None, :]
        squared = squared + separation * separation
    if self_pair is not None:
        squared = jnp.where(self_pair, 1.0, squared)
    inverse = lax.rsqrt(squared)
    screening = lax.rsqrt(row_geometry[3][:, None] + col_geometry[3][None, :])
    off = lax.erf(screening * squared * inverse) * inverse
    if self_pair is None:
        return off
    return jnp.where(self_pair, row_geometry[5][:, None], off)


def pulling(row_geometry, col_geometry, self_pair, col_charges):
    separations = []
    squared = jnp.zeros(self_pair.shape, row_geometry.dtype)
    for axis_id in range(3):
        separation = row_geometry[axis_id][:, None] - col_geometry[axis_id][None, :]
        separations.append(separation)
        squared = squared + separation * separation
    squared = jnp.where(self_pair, 1.0, squared)
    inverse = lax.rsqrt(squared)
    screening = lax.rsqrt(row_geometry[3][:, None] + col_geometry[3][None, :])
    slope = (
        (
            lax.erf(screening * squared * inverse) * inverse
            - TWO_ROOT * screening * jnp.exp(-screening * screening * squared)
        )
        * inverse
        * inverse
    )
    slope = jnp.where(self_pair, 0.0, slope) * col_charges[None, :]
    return jnp.stack(
        [
            jnp.sum(slope * separations[0], 1),
            jnp.sum(slope * separations[1], 1),
            jnp.sum(slope * separations[2], 1),
        ]
    )


def prep_kernel(hard_ref, width_ref, pos_ref, species_ref, desc_ref, readout_ref, out_ref):
    kinds = species_ref[...]
    hard = jnp.zeros(kinds.shape, jnp.float32)
    width = jnp.zeros(kinds.shape, jnp.float32)
    for kind in range(hard_ref.shape[0]):
        hard = jnp.where(kinds == kind, hard_ref[kind], hard)
        width = jnp.where(kinds == kind, width_ref[kind], width)
    scores = lax.dot_general(
        readout_ref[...],
        desc_ref[...],
        (((1,), (1,)), ((), ())),
        precision=lax.Precision.HIGHEST,
        preferred_element_type=jnp.float32,
    )
    negativity = jnp.zeros(kinds.shape, jnp.float32)
    for kind in range(hard_ref.shape[0]):
        negativity = jnp.where(kinds == kind, scores[kind : kind + 1, :], negativity)
    self_term = hard + 1.0 / (width * ROOT_PI)
    per_brick = kinds.shape[-1]
    features = [pos_ref[0], pos_ref[1], pos_ref[2], 2.0 * (width * width), negativity, self_term]
    features = features + [jnp.zeros(kinds.shape, jnp.float32)] * (out_ref.shape[-1] // per_brick - len(features))
    block = jnp.concatenate(features, 1)
    for slot in range(out_ref.shape[0]):
        out_ref[slot] = block


def prep(positions, species, descriptors, readout, hardness, widths, devices):
    per_brick = species.shape[-1]
    smem = pltpu.MemorySpace.SMEM if hasattr(pltpu, "MemorySpace") else pltpu.SMEM
    return pl.pallas_call(
        prep_kernel,
        in_specs=[
            pl.BlockSpec(memory_space=smem),
            pl.BlockSpec(memory_space=smem),
            pl.BlockSpec(memory_space=pltpu.VMEM),
            pl.BlockSpec(memory_space=pltpu.VMEM),
            pl.BlockSpec(memory_space=pltpu.VMEM),
            pl.BlockSpec(memory_space=pltpu.VMEM),
        ],
        out_specs=pl.BlockSpec(memory_space=pltpu.VMEM),
        out_shape=jax.ShapeDtypeStruct((devices, 1, FEATURES * per_brick), jnp.float32),
    )(
        hardness,
        widths,
        positions.reshape(3, 1, per_brick),
        species.reshape(1, per_brick),
        descriptors.reshape(descriptors.shape[0], per_brick).T,
        readout,
    )


def pulling_fields(row_geometry, col_geometry, self_pair, vectors):
    separations = []
    squared = jnp.zeros(self_pair.shape, row_geometry.dtype)
    for axis_id in range(3):
        separation = row_geometry[axis_id][:, None] - col_geometry[axis_id][None, :]
        separations.append(separation)
        squared = squared + separation * separation
    squared = jnp.where(self_pair, 1.0, squared)
    inverse = lax.rsqrt(squared)
    screening = lax.rsqrt(row_geometry[3][:, None] + col_geometry[3][None, :])
    slope = (
        (
            lax.erf(screening * squared * inverse) * inverse
            - TWO_ROOT * screening * jnp.exp(-screening * screening * squared)
        )
        * inverse
        * inverse
    )
    slope = jnp.where(self_pair, 0.0, slope)
    return jnp.stack(
        [jnp.stack([jnp.sum(slope * vector[None, :] * separation, 1) for separation in separations]) for vector in vectors]
    )


def make_shards(rows, cols):
    devices = rows * cols
    everyone = ("row", "col")

    def gather_all(piece):
        spread = jnp.broadcast_to(piece[None], (devices,) + piece.shape)
        got = lax.all_to_all(spread, everyone, 0, 0, tiled=True)
        return jnp.moveaxis(got, 0, 1).reshape(piece.shape[0], -1)

    def shards(positions, species, descriptors, readout, hardness, widths):
        per_brick = species.shape[-1]
        atoms = devices * per_brick
        me = lax.axis_index("row") * cols + lax.axis_index("col")
        payload = prep(positions, species, descriptors, readout, hardness, widths, devices)
        got = lax.all_to_all(payload, everyone, 0, 0, tiled=True)
        geometry = jnp.moveaxis(got.reshape(devices, FEATURES, per_brick), 0, 1).reshape(FEATURES, atoms)
        own = lax.dynamic_slice_in_dim(geometry, me * per_brick, per_brick, 1)
        col_index = jnp.arange(atoms, dtype=jnp.int32)

        pair = devices % 2 == 0 and (atoms // 2) * atoms * 4 <= PAIR_LIMIT
        if pair:
            parity = me % 2
            halves = devices // 2
            row_geometry = lax.dynamic_index_in_dim(
                geometry.reshape(geometry.shape[0], halves, 2, per_brick), parity, 2, keepdims=False
            ).reshape(geometry.shape[0], -1)
            brick_of = 2 * jnp.arange(halves, dtype=jnp.int32) + parity
            row_index = (brick_of[:, None] * per_brick + jnp.arange(per_brick, dtype=jnp.int32)[None]).reshape(-1)
            partner = [(i, i ^ 1) for i in range(devices)]

            def pick_rows(vectors):
                return lax.dynamic_index_in_dim(
                    vectors.reshape(2, halves, 2, per_brick), parity, 2, keepdims=False
                ).reshape(2, -1)

            def assemble(mine):
                theirs = lax.ppermute(mine, everyone, partner)
                first = jnp.where(parity == 0, mine, theirs).reshape(2, halves, per_brick)
                second = jnp.where(parity == 0, theirs, mine).reshape(2, halves, per_brick)
                return jnp.stack([first, second], 2).reshape(2, atoms)
        else:
            row_geometry = own
            row_index = me * per_brick + jnp.arange(per_brick, dtype=jnp.int32)

            def assemble(mine):
                return gather_all(mine.reshape(2, per_brick))

        if pair and atoms % 4 == 0:
            group = atoms // 4
            starts = []
            matrices = []
            for k, ((row_a, col_a), (row_b, col_b)) in enumerate(zip(BLOCKS[0], BLOCKS[1])):
                row_at = jnp.where(parity == 0, row_a, row_b) * group
                col_at = jnp.where(parity == 0, col_a, col_b) * group
                starts.append((row_at, col_at))
                offsets = jnp.arange(group, dtype=jnp.int32)
                matrices.append(
                    lax.optimization_barrier(
                        screened(
                            lax.dynamic_slice_in_dim(geometry, row_at, group, 1),
                            lax.dynamic_slice_in_dim(geometry, col_at, group, 1),
                            offsets[:, None] == offsets[None, :] if k < 2 else None,
                        )
                    )
                )

            def partial_image(vectors):
                partial = jnp.zeros_like(vectors)
                for k, (matrix, (row_at, col_at)) in enumerate(zip(matrices, starts)):
                    col_part = lax.dynamic_slice_in_dim(vectors, col_at, group, 1)
                    forward = jnp.sum(matrix[None, :, :] * col_part[:, None, :], 2)
                    partial = lax.dynamic_update_slice_in_dim(
                        partial, lax.dynamic_slice_in_dim(partial, row_at, group, 1) + forward, row_at, 1
                    )
                    if k >= 2:
                        row_part = lax.dynamic_slice_in_dim(vectors, row_at, group, 1)
                        backward = jnp.sum(matrix[None, :, :] * row_part[:, :, None], 1)
                        partial = lax.dynamic_update_slice_in_dim(
                            partial, lax.dynamic_slice_in_dim(partial, col_at, group, 1) + backward, col_at, 1
                        )
                return partial

            def operate(vectors):
                partial = partial_image(vectors)
                return partial + lax.ppermute(partial, everyone, partner)

            def curvature(vectors):
                mine = 0.0
                for k, (matrix, (row_at, col_at)) in enumerate(zip(matrices, starts)):
                    col_part = lax.dynamic_slice_in_dim(vectors, col_at, group, 1)
                    row_part = lax.dynamic_slice_in_dim(vectors, row_at, group, 1)
                    term = jnp.sum(row_part * jnp.sum(matrix[None, :, :] * col_part[:, None, :], 2), 1)
                    mine = mine + (term if k < 2 else 2.0 * term)
                return mine + lax.ppermute(mine, everyone, partner)
        else:
            matrix = screened(row_geometry, geometry, row_index[:, None] == col_index[None, :])

            def operate(vectors):
                return assemble(jnp.sum(matrix[None, :, :] * vectors[:, None, :], 2))

            def curvature(vectors):
                return jnp.sum(vectors * operate(vectors), 1)

        rhs = jnp.stack([-geometry[4], jnp.ones((atoms,), jnp.float32)])
        solution = jnp.zeros_like(rhs)
        resid = rhs
        direction = rhs
        norm_now = jnp.sum(resid * resid, 1)
        own_index = me * per_brick + jnp.arange(per_brick, dtype=jnp.int32)
        for iteration in range(ITERS - 1):
            image = operate(direction)
            step_size = norm_now / jnp.sum(direction * image, 1)
            solution = solution + step_size[:, None] * direction
            resid = resid - step_size[:, None] * image
            norm_next = jnp.sum(resid * resid, 1)
            direction = resid + (norm_next / norm_now)[:, None] * direction
            norm_now = norm_next
        fields = pulling_fields(
            own, geometry, own_index[:, None] == col_index[None, :],
            [solution[0], solution[1], direction[0], direction[1]],
        ).reshape(2, 2, 3, per_brick)
        own_solution = lax.dynamic_slice_in_dim(solution, me * per_brick, per_brick, 1)
        own_direction = lax.dynamic_slice_in_dim(direction, me * per_brick, per_brick, 1)
        solution_sums = jnp.sum(solution, 1)
        direction_sums = jnp.sum(direction, 1)
        last_curvature = curvature(direction)
        step_size = norm_now / last_curvature
        totals = solution_sums + step_size * direction_sums
        weights = jnp.where(jnp.arange(2) == 0, 1.0, -(totals[::-1] / totals))
        own_charges = jnp.sum(weights[:, None] * (own_solution + step_size[:, None] * own_direction), 0)
        field = jnp.sum(
            weights[:, None, None] * (fields[0] + step_size[:, None, None] * fields[1]), 0
        )
        forces = (own_charges[None, :] * field).reshape(3, 1, 1, per_brick)
        return (own_charges.reshape(1, 1, per_brick), forces)

    return shards


def solution(mesh):
    in_specs = (
        P(None, "row", "col", None),
        P("row", "col", None),
        P(None, "row", "col", None),
        P(),
        P(),
        P(),
    )
    out_specs = (P("row", "col", None), P(None, "row", "col", None))
    shards = make_shards(mesh.shape["row"], mesh.shape["col"])
    return jax.shard_map(shards, mesh=mesh, in_specs=in_specs, out_specs=out_specs, check_vma=False)
```

```python
import jax
import jax.numpy as jnp
from jax import lax
from jax.sharding import PartitionSpec as P
from jax.experimental import pallas as pl
from jax.experimental.pallas import tpu as pltpu

ITERS = 3


ROOT_PI = 1.7724538509055159
TWO_ROOT = 1.1283791670955126

PAIR_LIMIT = 16 * 1024 * 1024
FEATURES = 6
BLOCKS = (
    ((0, 0), (1, 1), (0, 1), (0, 2), (1, 2)),
    ((2, 2), (3, 3), (2, 3), (0, 3), (1, 3)),
)


def screened(row_geometry, col_geometry, self_pair):
    squared = 0.0
    for axis_id in range(3):
        separation = row_geometry[axis_id][:, None] - col_geometry[axis_id][None, :]
        squared = squared + separation * separation
    if self_pair is not None:
        squared = jnp.where(self_pair, 1.0, squared)
    inverse = lax.rsqrt(squared)
    screening = lax.rsqrt(row_geometry[3][:, None] + col_geometry[3][None, :])
    off = lax.erf(screening * squared * inverse) * inverse
    if self_pair is None:
        return off
    return jnp.where(self_pair, row_geometry[5][:, None], off)


def pulling(row_geometry, col_geometry, self_pair, col_charges):
    separations = []
    squared = jnp.zeros(self_pair.shape, row_geometry.dtype)
    for axis_id in range(3):
        separation = row_geometry[axis_id][:, None] - col_geometry[axis_id][None, :]
        separations.append(separation)
        squared = squared + separation * separation
    squared = jnp.where(self_pair, 1.0, squared)
    inverse = lax.rsqrt(squared)
    screening = lax.rsqrt(row_geometry[3][:, None] + col_geometry[3][None, :])
    slope = (
        (
            lax.erf(screening * squared * inverse) * inverse
            - TWO_ROOT * screening * jnp.exp(-screening * screening * squared)
        )
        * inverse
        * inverse
    )
    slope = jnp.where(self_pair, 0.0, slope) * col_charges[None, :]
    return jnp.stack(
        [
            jnp.sum(slope * separations[0], 1),
            jnp.sum(slope * separations[1], 1),
            jnp.sum(slope * separations[2], 1),
        ]
    )


def prep_kernel(hard_ref, width_ref, pos_ref, species_ref, desc_ref, readout_ref, out_ref):
    kinds = species_ref[...]
    hard_row = hard_ref[...]
    width_row = width_ref[...]
    hard = jnp.zeros(kinds.shape, jnp.float32)
    width = jnp.zeros(kinds.shape, jnp.float32)
    for kind in range(hard_ref.shape[1]):
        hard = jnp.where(kinds == kind, hard_row[:, kind : kind + 1], hard)
        width = jnp.where(kinds == kind, width_row[:, kind : kind + 1], width)
    scores = lax.dot_general(
        readout_ref[...],
        desc_ref[...],
        (((1,), (1,)), ((), ())),
        precision=lax.Precision.HIGHEST,
        preferred_element_type=jnp.float32,
    )
    negativity = jnp.zeros(kinds.shape, jnp.float32)
    for kind in range(hard_ref.shape[1]):
        negativity = jnp.where(kinds == kind, scores[kind : kind + 1, :], negativity)
    self_term = hard + 1.0 / (width * ROOT_PI)
    per_brick = kinds.shape[-1]
    features = [pos_ref[0], pos_ref[1], pos_ref[2], 2.0 * (width * width), negativity, self_term]
    features = features + [jnp.zeros(kinds.shape, jnp.float32)] * (out_ref.shape[-1] // per_brick - len(features))
    block = jnp.concatenate(features, 1)
    for slot in range(out_ref.shape[0]):
        out_ref[slot] = block


def prep(positions, species, descriptors, readout, hardness, widths, devices):
    per_brick = species.shape[-1]
    return pl.pallas_call(
        prep_kernel,
        in_specs=[
            pl.BlockSpec(memory_space=pltpu.VMEM),
            pl.BlockSpec(memory_space=pltpu.VMEM),
            pl.BlockSpec(memory_space=pltpu.VMEM),
            pl.BlockSpec(memory_space=pltpu.VMEM),
            pl.BlockSpec(memory_space=pltpu.VMEM),
            pl.BlockSpec(memory_space=pltpu.VMEM),
        ],
        out_specs=pl.BlockSpec(memory_space=pltpu.VMEM),
        out_shape=jax.ShapeDtypeStruct((devices, 1, FEATURES * per_brick), jnp.float32),
    )(
        hardness.reshape(1, -1),
        widths.reshape(1, -1),
        positions.reshape(3, 1, per_brick),
        species.reshape(1, per_brick),
        descriptors.reshape(descriptors.shape[0], per_brick).T,
        readout,
    )


def pulling_fields(row_geometry, col_geometry, self_pair, vectors):
    separations = []
    squared = jnp.zeros(self_pair.shape, row_geometry.dtype)
    for axis_id in range(3):
        separation = row_geometry[axis_id][:, None] - col_geometry[axis_id][None, :]
        separations.append(separation)
        squared = squared + separation * separation
    squared = jnp.where(self_pair, 1.0, squared)
    inverse = lax.rsqrt(squared)
    screening = lax.rsqrt(row_geometry[3][:, None] + col_geometry[3][None, :])
    slope = (
        (
            lax.erf(screening * squared * inverse) * inverse
            - TWO_ROOT * screening * jnp.exp(-screening * screening * squared)
        )
        * inverse
        * inverse
    )
    slope = jnp.where(self_pair, 0.0, slope)
    return jnp.stack(
        [jnp.stack([jnp.sum(slope * vector[None, :] * separation, 1) for separation in separations]) for vector in vectors]
    )


def make_shards(rows, cols):
    devices = rows * cols
    everyone = ("row", "col")

    def gather_all(piece):
        spread = jnp.broadcast_to(piece[None], (devices,) + piece.shape)
        got = lax.all_to_all(spread, everyone, 0, 0, tiled=True)
        return jnp.moveaxis(got, 0, 1).reshape(piece.shape[0], -1)

    def shards(positions, species, descriptors, readout, hardness, widths):
        per_brick = species.shape[-1]
        atoms = devices * per_brick
        me = lax.axis_index("row") * cols + lax.axis_index("col")
        payload = prep(positions, species, descriptors, readout, hardness, widths, devices)
        got = lax.all_to_all(payload, everyone, 0, 0, tiled=True)
        geometry = jnp.moveaxis(got.reshape(devices, FEATURES, per_brick), 0, 1).reshape(FEATURES, atoms)
        own = lax.dynamic_slice_in_dim(geometry, me * per_brick, per_brick, 1)
        col_index = jnp.arange(atoms, dtype=jnp.int32)

        pair = devices % 2 == 0 and (atoms // 2) * atoms * 4 <= PAIR_LIMIT
        if pair:
            parity = me % 2
            halves = devices // 2
            row_geometry = lax.dynamic_index_in_dim(
                geometry.reshape(geometry.shape[0], halves, 2, per_brick), parity, 2, keepdims=False
            ).reshape(geometry.shape[0], -1)
            brick_of = 2 * jnp.arange(halves, dtype=jnp.int32) + parity
            row_index = (brick_of[:, None] * per_brick + jnp.arange(per_brick, dtype=jnp.int32)[None]).reshape(-1)
            partner = [(i, i ^ 1) for i in range(devices)]

            def pick_rows(vectors):
                return lax.dynamic_index_in_dim(
                    vectors.reshape(2, halves, 2, per_brick), parity, 2, keepdims=False
                ).reshape(2, -1)

            def assemble(mine):
                theirs = lax.ppermute(mine, everyone, partner)
                first = jnp.where(parity == 0, mine, theirs).reshape(2, halves, per_brick)
                second = jnp.where(parity == 0, theirs, mine).reshape(2, halves, per_brick)
                return jnp.stack([first, second], 2).reshape(2, atoms)
        else:
            row_geometry = own
            row_index = me * per_brick + jnp.arange(per_brick, dtype=jnp.int32)

            def assemble(mine):
                return gather_all(mine.reshape(2, per_brick))

        if pair and atoms % 4 == 0:
            group = atoms // 4
            starts = []
            matrices = []
            for k, ((row_a, col_a), (row_b, col_b)) in enumerate(zip(BLOCKS[0], BLOCKS[1])):
                row_at = jnp.where(parity == 0, row_a, row_b) * group
                col_at = jnp.where(parity == 0, col_a, col_b) * group
                starts.append((row_at, col_at))
                offsets = jnp.arange(group, dtype=jnp.int32)
                matrices.append(
                    lax.optimization_barrier(
                        screened(
                            lax.dynamic_slice_in_dim(geometry, row_at, group, 1),
                            lax.dynamic_slice_in_dim(geometry, col_at, group, 1),
                            offsets[:, None] == offsets[None, :] if k < 2 else None,
                        )
                    )
                )

            def partial_image(vectors):
                partial = jnp.zeros_like(vectors)
                for k, (matrix, (row_at, col_at)) in enumerate(zip(matrices, starts)):
                    col_part = lax.dynamic_slice_in_dim(vectors, col_at, group, 1)
                    forward = jnp.sum(matrix[None, :, :] * col_part[:, None, :], 2)
                    partial = lax.dynamic_update_slice_in_dim(
                        partial, lax.dynamic_slice_in_dim(partial, row_at, group, 1) + forward, row_at, 1
                    )
                    if k >= 2:
                        row_part = lax.dynamic_slice_in_dim(vectors, row_at, group, 1)
                        backward = jnp.sum(matrix[None, :, :] * row_part[:, :, None], 1)
                        partial = lax.dynamic_update_slice_in_dim(
                            partial, lax.dynamic_slice_in_dim(partial, col_at, group, 1) + backward, col_at, 1
                        )
                return partial

            def operate(vectors):
                partial = partial_image(vectors)
                return partial + lax.ppermute(partial, everyone, partner)

            def curvature(vectors):
                mine = 0.0
                for k, (matrix, (row_at, col_at)) in enumerate(zip(matrices, starts)):
                    col_part = lax.dynamic_slice_in_dim(vectors, col_at, group, 1)
                    row_part = lax.dynamic_slice_in_dim(vectors, row_at, group, 1)
                    term = jnp.sum(row_part * jnp.sum(matrix[None, :, :] * col_part[:, None, :], 2), 1)
                    mine = mine + (term if k < 2 else 2.0 * term)
                return mine + lax.ppermute(mine, everyone, partner)
        else:
            matrix = screened(row_geometry, geometry, row_index[:, None] == col_index[None, :])

            def operate(vectors):
                return assemble(jnp.sum(matrix[None, :, :] * vectors[:, None, :], 2))

            def curvature(vectors):
                return jnp.sum(vectors * operate(vectors), 1)

        rhs = jnp.stack([-geometry[4], jnp.ones((atoms,), jnp.float32)])
        solution = jnp.zeros_like(rhs)
        resid = rhs
        direction = rhs
        norm_now = jnp.sum(resid * resid, 1)
        own_index = me * per_brick + jnp.arange(per_brick, dtype=jnp.int32)
        for iteration in range(ITERS - 1):
            image = operate(direction)
            step_size = norm_now / jnp.sum(direction * image, 1)
            solution = solution + step_size[:, None] * direction
            resid = resid - step_size[:, None] * image
            norm_next = jnp.sum(resid * resid, 1)
            direction = resid + (norm_next / norm_now)[:, None] * direction
            norm_now = norm_next
        fields = pulling_fields(
            own, geometry, own_index[:, None] == col_index[None, :],
            [solution[0], solution[1], direction[0], direction[1]],
        ).reshape(2, 2, 3, per_brick)
        own_solution = lax.dynamic_slice_in_dim(solution, me * per_brick, per_brick, 1)
        own_direction = lax.dynamic_slice_in_dim(direction, me * per_brick, per_brick, 1)
        solution_sums = jnp.sum(solution, 1)
        direction_sums = jnp.sum(direction, 1)
        last_curvature = curvature(direction)
        step_size = norm_now / last_curvature
        totals = solution_sums + step_size * direction_sums
        weights = jnp.where(jnp.arange(2) == 0, 1.0, -(totals[::-1] / totals))
        own_charges = jnp.sum(weights[:, None] * (own_solution + step_size[:, None] * own_direction), 0)
        field = jnp.sum(
            weights[:, None, None] * (fields[0] + step_size[:, None, None] * fields[1]), 0
        )
        forces = (own_charges[None, :] * field).reshape(3, 1, 1, per_brick)
        return (own_charges.reshape(1, 1, per_brick), forces)

    return shards


def solution(mesh):
    in_specs = (
        P(None, "row", "col", None),
        P("row", "col", None),
        P(None, "row", "col", None),
        P(),
        P(),
        P(),
    )
    out_specs = (P("row", "col", None), P(None, "row", "col", None))
    shards = make_shards(mesh.shape["row"], mesh.shape["col"])
    return jax.shard_map(shards, mesh=mesh, in_specs=in_specs, out_specs=out_specs, check_vma=False)
```

```python
import jax
import jax.numpy as jnp
from jax import lax
from jax.sharding import PartitionSpec as P
from jax.experimental import pallas as pl
from jax.experimental.pallas import tpu as pltpu

ITERS = 3


ROOT_PI = 1.7724538509055159
TWO_ROOT = 1.1283791670955126

PAIR_LIMIT = 16 * 1024 * 1024
FEATURES = 6
BLOCKS = (
    ((0, 0), (1, 1), (0, 1), (0, 2), (1, 2)),
    ((2, 2), (3, 3), (2, 3), (0, 3), (1, 3)),
)


def screened(row_geometry, col_geometry, self_pair):
    squared = 0.0
    for axis_id in range(3):
        separation = row_geometry[axis_id][:, None] - col_geometry[axis_id][None, :]
        squared = squared + separation * separation
    if self_pair is not None:
        squared = jnp.where(self_pair, 1.0, squared)
    inverse = lax.rsqrt(squared)
    screening = lax.rsqrt(row_geometry[3][:, None] + col_geometry[3][None, :])
    off = lax.erf(screening * squared * inverse) * inverse
    if self_pair is None:
        return off
    return jnp.where(self_pair, row_geometry[5][:, None], off)


def pulling(row_geometry, col_geometry, self_pair, col_charges):
    separations = []
    squared = jnp.zeros(self_pair.shape, row_geometry.dtype)
    for axis_id in range(3):
        separation = row_geometry[axis_id][:, None] - col_geometry[axis_id][None, :]
        separations.append(separation)
        squared = squared + separation * separation
    squared = jnp.where(self_pair, 1.0, squared)
    inverse = lax.rsqrt(squared)
    screening = lax.rsqrt(row_geometry[3][:, None] + col_geometry[3][None, :])
    slope = (
        (
            lax.erf(screening * squared * inverse) * inverse
            - TWO_ROOT * screening * jnp.exp(-screening * screening * squared)
        )
        * inverse
        * inverse
    )
    slope = jnp.where(self_pair, 0.0, slope) * col_charges[None, :]
    return jnp.stack(
        [
            jnp.sum(slope * separations[0], 1),
            jnp.sum(slope * separations[1], 1),
            jnp.sum(slope * separations[2], 1),
        ]
    )


def prep_kernel(hard_ref, width_ref, pos_ref, species_ref, desc_ref, readout_ref, out_ref):
    kinds = species_ref[...]
    hard = jnp.zeros(kinds.shape, jnp.float32)
    width = jnp.zeros(kinds.shape, jnp.float32)
    for kind in range(hard_ref.shape[0]):
        hard = jnp.where(kinds == kind, hard_ref[kind], hard)
        width = jnp.where(kinds == kind, width_ref[kind], width)
    scores = lax.dot_general(
        readout_ref[...],
        desc_ref[...],
        (((1,), (1,)), ((), ())),
        precision=lax.Precision.HIGHEST,
        preferred_element_type=jnp.float32,
    )
    negativity = jnp.zeros(kinds.shape, jnp.float32)
    for kind in range(hard_ref.shape[0]):
        negativity = jnp.where(kinds == kind, scores[kind : kind + 1, :], negativity)
    self_term = hard + 1.0 / (width * ROOT_PI)
    per_brick = kinds.shape[-1]
    features = [pos_ref[0], pos_ref[1], pos_ref[2], 2.0 * (width * width), negativity, self_term]
    features = features + [jnp.zeros(kinds.shape, jnp.float32)] * (out_ref.shape[-1] // per_brick - len(features))
    block = jnp.concatenate(features, 1)
    for slot in range(out_ref.shape[0]):
        out_ref[slot] = block


def prep(positions, species, descriptors, readout, hardness, widths, devices):
    per_brick = species.shape[-1]
    smem = pltpu.MemorySpace.SMEM if hasattr(pltpu, "MemorySpace") else pltpu.SMEM
    return pl.pallas_call(
        prep_kernel,
        in_specs=[
            pl.BlockSpec(memory_space=smem),
            pl.BlockSpec(memory_space=smem),
            pl.BlockSpec(memory_space=pltpu.VMEM),
            pl.BlockSpec(memory_space=pltpu.VMEM),
            pl.BlockSpec(memory_space=pltpu.VMEM),
            pl.BlockSpec(memory_space=pltpu.VMEM),
        ],
        out_specs=pl.BlockSpec(memory_space=pltpu.VMEM),
        out_shape=jax.ShapeDtypeStruct((devices, 1, FEATURES * per_brick), jnp.float32),
    )(
        hardness,
        widths,
        positions.reshape(3, 1, per_brick),
        species.reshape(1, per_brick),
        descriptors.reshape(descriptors.shape[0], per_brick).T,
        readout,
    )


def pulling_slope(row_geometry, col_geometry, self_pair):
    squared = jnp.zeros(self_pair.shape, row_geometry.dtype)
    for axis_id in range(3):
        separation = row_geometry[axis_id][:, None] - col_geometry[axis_id][None, :]
        squared = squared + separation * separation
    squared = jnp.where(self_pair, 1.0, squared)
    inverse = lax.rsqrt(squared)
    screening = lax.rsqrt(row_geometry[3][:, None] + col_geometry[3][None, :])
    slope = (
        (
            lax.erf(screening * squared * inverse) * inverse
            - TWO_ROOT * screening * jnp.exp(-screening * screening * squared)
        )
        * inverse
        * inverse
    )
    return jnp.where(self_pair, 0.0, slope)


def pulling_fields(row_geometry, col_geometry, slope, vectors):
    separations = [row_geometry[axis_id][:, None] - col_geometry[axis_id][None, :] for axis_id in range(3)]
    return jnp.stack(
        [jnp.stack([jnp.sum(slope * vector[None, :] * separation, 1) for separation in separations]) for vector in vectors]
    )


def make_shards(rows, cols):
    devices = rows * cols
    everyone = ("row", "col")

    def gather_all(piece):
        spread = jnp.broadcast_to(piece[None], (devices,) + piece.shape)
        got = lax.all_to_all(spread, everyone, 0, 0, tiled=True)
        return jnp.moveaxis(got, 0, 1).reshape(piece.shape[0], -1)

    def shards(positions, species, descriptors, readout, hardness, widths):
        per_brick = species.shape[-1]
        atoms = devices * per_brick
        me = lax.axis_index("row") * cols + lax.axis_index("col")
        payload = prep(positions, species, descriptors, readout, hardness, widths, devices)
        got = lax.all_to_all(payload, everyone, 0, 0, tiled=True)
        geometry = jnp.moveaxis(got.reshape(devices, FEATURES, per_brick), 0, 1).reshape(FEATURES, atoms)
        own = lax.dynamic_slice_in_dim(geometry, me * per_brick, per_brick, 1)
        col_index = jnp.arange(atoms, dtype=jnp.int32)

        pair = devices % 2 == 0 and (atoms // 2) * atoms * 4 <= PAIR_LIMIT
        if pair:
            parity = me % 2
            halves = devices // 2
            row_geometry = lax.dynamic_index_in_dim(
                geometry.reshape(geometry.shape[0], halves, 2, per_brick), parity, 2, keepdims=False
            ).reshape(geometry.shape[0], -1)
            brick_of = 2 * jnp.arange(halves, dtype=jnp.int32) + parity
            row_index = (brick_of[:, None] * per_brick + jnp.arange(per_brick, dtype=jnp.int32)[None]).reshape(-1)
            partner = [(i, i ^ 1) for i in range(devices)]

            def pick_rows(vectors):
                return lax.dynamic_index_in_dim(
                    vectors.reshape(2, halves, 2, per_brick), parity, 2, keepdims=False
                ).reshape(2, -1)

            def assemble(mine):
                theirs = lax.ppermute(mine, everyone, partner)
                first = jnp.where(parity == 0, mine, theirs).reshape(2, halves, per_brick)
                second = jnp.where(parity == 0, theirs, mine).reshape(2, halves, per_brick)
                return jnp.stack([first, second], 2).reshape(2, atoms)
        else:
            row_geometry = own
            row_index = me * per_brick + jnp.arange(per_brick, dtype=jnp.int32)

            def assemble(mine):
                return gather_all(mine.reshape(2, per_brick))

        if pair and atoms % 4 == 0:
            group = atoms // 4
            starts = []
            matrices = []
            for k, ((row_a, col_a), (row_b, col_b)) in enumerate(zip(BLOCKS[0], BLOCKS[1])):
                row_at = jnp.where(parity == 0, row_a, row_b) * group
                col_at = jnp.where(parity == 0, col_a, col_b) * group
                starts.append((row_at, col_at))
                offsets = jnp.arange(group, dtype=jnp.int32)
                matrices.append(
                    lax.optimization_barrier(
                        screened(
                            lax.dynamic_slice_in_dim(geometry, row_at, group, 1),
                            lax.dynamic_slice_in_dim(geometry, col_at, group, 1),
                            offsets[:, None] == offsets[None, :] if k < 2 else None,
                        )
                    )
                )

            def partial_image(vectors):
                partial = jnp.zeros_like(vectors)
                for k, (matrix, (row_at, col_at)) in enumerate(zip(matrices, starts)):
                    col_part = lax.dynamic_slice_in_dim(vectors, col_at, group, 1)
                    forward = jnp.sum(matrix[None, :, :] * col_part[:, None, :], 2)
                    partial = lax.dynamic_update_slice_in_dim(
                        partial, lax.dynamic_slice_in_dim(partial, row_at, group, 1) + forward, row_at, 1
                    )
                    if k >= 2:
                        row_part = lax.dynamic_slice_in_dim(vectors, row_at, group, 1)
                        backward = jnp.sum(matrix[None, :, :] * row_part[:, :, None], 1)
                        partial = lax.dynamic_update_slice_in_dim(
                            partial, lax.dynamic_slice_in_dim(partial, col_at, group, 1) + backward, col_at, 1
                        )
                return partial

            def operate(vectors):
                partial = partial_image(vectors)
                return partial + lax.ppermute(partial, everyone, partner)

            def curvature(vectors):
                mine = 0.0
                for k, (matrix, (row_at, col_at)) in enumerate(zip(matrices, starts)):
                    col_part = lax.dynamic_slice_in_dim(vectors, col_at, group, 1)
                    row_part = lax.dynamic_slice_in_dim(vectors, row_at, group, 1)
                    term = jnp.sum(row_part * jnp.sum(matrix[None, :, :] * col_part[:, None, :], 2), 1)
                    mine = mine + (term if k < 2 else 2.0 * term)
                return mine + lax.ppermute(mine, everyone, partner)
        else:
            matrix = screened(row_geometry, geometry, row_index[:, None] == col_index[None, :])

            def operate(vectors):
                return assemble(jnp.sum(matrix[None, :, :] * vectors[:, None, :], 2))

            def curvature(vectors):
                return jnp.sum(vectors * operate(vectors), 1)

        own_index = me * per_brick + jnp.arange(per_brick, dtype=jnp.int32)
        slope = lax.optimization_barrier(pulling_slope(own, geometry, own_index[:, None] == col_index[None, :]))
        rhs = jnp.stack([-geometry[4], jnp.ones((atoms,), jnp.float32)])
        solution = jnp.zeros_like(rhs)
        resid = rhs
        direction = rhs
        norm_now = jnp.sum(resid * resid, 1)
        own_index = me * per_brick + jnp.arange(per_brick, dtype=jnp.int32)
        for iteration in range(ITERS - 1):
            image = operate(direction)
            step_size = norm_now / jnp.sum(direction * image, 1)
            solution = solution + step_size[:, None] * direction
            resid = resid - step_size[:, None] * image
            norm_next = jnp.sum(resid * resid, 1)
            direction = resid + (norm_next / norm_now)[:, None] * direction
            norm_now = norm_next
        fields = pulling_fields(
            own, geometry, slope, [solution[0], solution[1], direction[0], direction[1]]
        ).reshape(2, 2, 3, per_brick)
        own_solution = lax.dynamic_slice_in_dim(solution, me * per_brick, per_brick, 1)
        own_direction = lax.dynamic_slice_in_dim(direction, me * per_brick, per_brick, 1)
        solution_sums = jnp.sum(solution, 1)
        direction_sums = jnp.sum(direction, 1)
        last_curvature = curvature(direction)
        step_size = norm_now / last_curvature
        totals = solution_sums + step_size * direction_sums
        weights = jnp.where(jnp.arange(2) == 0, 1.0, -(totals[::-1] / totals))
        own_charges = jnp.sum(weights[:, None] * (own_solution + step_size[:, None] * own_direction), 0)
        field = jnp.sum(
            weights[:, None, None] * (fields[0] + step_size[:, None, None] * fields[1]), 0
        )
        forces = (own_charges[None, :] * field).reshape(3, 1, 1, per_brick)
        return (own_charges.reshape(1, 1, per_brick), forces)

    return shards


def solution(mesh):
    in_specs = (
        P(None, "row", "col", None),
        P("row", "col", None),
        P(None, "row", "col", None),
        P(),
        P(),
        P(),
    )
    out_specs = (P("row", "col", None), P(None, "row", "col", None))
    shards = make_shards(mesh.shape["row"], mesh.shape["col"])
    return jax.shard_map(shards, mesh=mesh, in_specs=in_specs, out_specs=out_specs, check_vma=False)
```

```python
import jax
import jax.numpy as jnp
from jax import lax
from jax.sharding import PartitionSpec as P
from jax.experimental import pallas as pl
from jax.experimental.pallas import tpu as pltpu

ITERS = 3


ROOT_PI = 1.7724538509055159
TWO_ROOT = 1.1283791670955126

PAIR_LIMIT = 16 * 1024 * 1024
FEATURES = 6
BLOCKS = (
    ((0, 0), (1, 1), (0, 1), (0, 2), (1, 2)),
    ((2, 2), (3, 3), (2, 3), (0, 3), (1, 3)),
)


def screened(row_geometry, col_geometry, self_pair):
    squared = 0.0
    for axis_id in range(3):
        separation = row_geometry[axis_id][:, None] - col_geometry[axis_id][None, :]
        squared = squared + separation * separation
    if self_pair is not None:
        squared = jnp.where(self_pair, 1.0, squared)
    inverse = lax.rsqrt(squared)
    screening = lax.rsqrt(row_geometry[3][:, None] + col_geometry[3][None, :])
    off = lax.erf(screening * squared * inverse) * inverse
    if self_pair is None:
        return off
    return jnp.where(self_pair, row_geometry[5][:, None], off)


def pulling(row_geometry, col_geometry, self_pair, col_charges):
    separations = []
    squared = jnp.zeros(self_pair.shape, row_geometry.dtype)
    for axis_id in range(3):
        separation = row_geometry[axis_id][:, None] - col_geometry[axis_id][None, :]
        separations.append(separation)
        squared = squared + separation * separation
    squared = jnp.where(self_pair, 1.0, squared)
    inverse = lax.rsqrt(squared)
    screening = lax.rsqrt(row_geometry[3][:, None] + col_geometry[3][None, :])
    slope = (
        (
            lax.erf(screening * squared * inverse) * inverse
            - TWO_ROOT * screening * jnp.exp(-screening * screening * squared)
        )
        * inverse
        * inverse
    )
    slope = jnp.where(self_pair, 0.0, slope) * col_charges[None, :]
    return jnp.stack(
        [
            jnp.sum(slope * separations[0], 1),
            jnp.sum(slope * separations[1], 1),
            jnp.sum(slope * separations[2], 1),
        ]
    )


def prep_kernel(hard_ref, width_ref, pos_ref, species_ref, desc_ref, readout_ref, out_ref):
    kinds = species_ref[...]
    hard = jnp.zeros(kinds.shape, jnp.float32)
    width = jnp.zeros(kinds.shape, jnp.float32)
    for kind in range(hard_ref.shape[0]):
        hard = jnp.where(kinds == kind, hard_ref[kind], hard)
        width = jnp.where(kinds == kind, width_ref[kind], width)
    scores = lax.dot_general(
        readout_ref[...],
        desc_ref[...],
        (((1,), (1,)), ((), ())),
        precision=lax.Precision.HIGHEST,
        preferred_element_type=jnp.float32,
    )
    negativity = jnp.zeros(kinds.shape, jnp.float32)
    for kind in range(hard_ref.shape[0]):
        negativity = jnp.where(kinds == kind, scores[kind : kind + 1, :], negativity)
    self_term = hard + 1.0 / (width * ROOT_PI)
    per_brick = kinds.shape[-1]
    features = [pos_ref[0], pos_ref[1], pos_ref[2], 2.0 * (width * width), negativity, self_term]
    features = features + [jnp.zeros(kinds.shape, jnp.float32)] * (out_ref.shape[-1] // per_brick - len(features))
    block = jnp.concatenate(features, 1)
    for slot in range(out_ref.shape[0]):
        out_ref[slot] = block


def prep(positions, species, descriptors, readout, hardness, widths, devices):
    per_brick = species.shape[-1]
    smem = pltpu.MemorySpace.SMEM if hasattr(pltpu, "MemorySpace") else pltpu.SMEM
    return pl.pallas_call(
        prep_kernel,
        in_specs=[
            pl.BlockSpec(memory_space=smem),
            pl.BlockSpec(memory_space=smem),
            pl.BlockSpec(memory_space=pltpu.VMEM),
            pl.BlockSpec(memory_space=pltpu.VMEM),
            pl.BlockSpec(memory_space=pltpu.VMEM),
            pl.BlockSpec(memory_space=pltpu.VMEM),
        ],
        out_specs=pl.BlockSpec(memory_space=pltpu.VMEM),
        out_shape=jax.ShapeDtypeStruct((devices, 1, FEATURES * per_brick), jnp.float32),
    )(
        hardness,
        widths,
        positions.reshape(3, 1, per_brick),
        species.reshape(1, per_brick),
        descriptors.reshape(descriptors.shape[0], per_brick).T,
        readout,
    )


def pulling_fields(row_geometry, col_geometry, self_pair, vectors):
    separations = []
    squared = jnp.zeros(self_pair.shape, row_geometry.dtype)
    for axis_id in range(3):
        separation = row_geometry[axis_id][:, None] - col_geometry[axis_id][None, :]
        separations.append(separation)
        squared = squared + separation * separation
    squared = jnp.where(self_pair, 1.0, squared)
    inverse = lax.rsqrt(squared)
    screening = lax.rsqrt(row_geometry[3][:, None] + col_geometry[3][None, :])
    slope = (
        (
            lax.erf(screening * squared * inverse) * inverse
            - TWO_ROOT * screening * jnp.exp(-screening * screening * squared)
        )
        * inverse
        * inverse
    )
    slope = jnp.where(self_pair, 0.0, slope)
    return jnp.stack(
        [jnp.stack([jnp.sum(slope * vector[None, :] * separation, 1) for separation in separations]) for vector in vectors]
    )


def make_shards(rows, cols):
    devices = rows * cols
    everyone = ("row", "col")

    def gather_all(piece):
        spread = jnp.broadcast_to(piece[None], (devices,) + piece.shape)
        got = lax.all_to_all(spread, everyone, 0, 0, tiled=True)
        return jnp.moveaxis(got, 0, 1).reshape(piece.shape[0], -1)

    def shards(positions, species, descriptors, readout, hardness, widths):
        per_brick = species.shape[-1]
        atoms = devices * per_brick
        me = lax.axis_index("row") * cols + lax.axis_index("col")
        payload = prep(positions, species, descriptors, readout, hardness, widths, devices)
        got = lax.all_to_all(payload, everyone, 0, 0, tiled=True)
        geometry = jnp.moveaxis(got.reshape(devices, FEATURES, per_brick), 0, 1).reshape(FEATURES, atoms)
        own = lax.dynamic_slice_in_dim(geometry, me * per_brick, per_brick, 1)
        col_index = jnp.arange(atoms, dtype=jnp.int32)

        pair = devices % 2 == 0 and (atoms // 2) * atoms * 4 <= PAIR_LIMIT
        if pair:
            parity = me % 2
            halves = devices // 2
            row_geometry = lax.dynamic_index_in_dim(
                geometry.reshape(geometry.shape[0], halves, 2, per_brick), parity, 2, keepdims=False
            ).reshape(geometry.shape[0], -1)
            brick_of = 2 * jnp.arange(halves, dtype=jnp.int32) + parity
            row_index = (brick_of[:, None] * per_brick + jnp.arange(per_brick, dtype=jnp.int32)[None]).reshape(-1)
            partner = [(i, i ^ 1) for i in range(devices)]

            def pick_rows(vectors):
                return lax.dynamic_index_in_dim(
                    vectors.reshape(2, halves, 2, per_brick), parity, 2, keepdims=False
                ).reshape(2, -1)

            def assemble(mine):
                theirs = lax.ppermute(mine, everyone, partner)
                first = jnp.where(parity == 0, mine, theirs).reshape(2, halves, per_brick)
                second = jnp.where(parity == 0, theirs, mine).reshape(2, halves, per_brick)
                return jnp.stack([first, second], 2).reshape(2, atoms)
        else:
            row_geometry = own
            row_index = me * per_brick + jnp.arange(per_brick, dtype=jnp.int32)

            def assemble(mine):
                return gather_all(mine.reshape(2, per_brick))

        if pair and atoms % 8 == 0:
            group = atoms // 4
            half = group // 2
            specs = []
            for (row_a, col_a), (row_b, col_b) in zip(BLOCKS[0][:2], BLOCKS[1][:2]):
                for low, high in ((0, 0), (1, 1), (0, 1)):
                    specs.append((row_a * group + low * half, row_b * group + low * half,
                                  col_a * group + high * half, col_b * group + high * half, half, low == high))
            for (row_a, col_a), (row_b, col_b) in zip(BLOCKS[0][2:], BLOCKS[1][2:]):
                specs.append((row_a * group, row_b * group, col_a * group, col_b * group, group, False))
            starts = []
            matrices = []
            for row_a, row_b, col_a, col_b, size, diagonal in specs:
                row_at = jnp.where(parity == 0, row_a, row_b)
                col_at = jnp.where(parity == 0, col_a, col_b)
                starts.append((row_at, col_at, size, diagonal))
                offsets = jnp.arange(size, dtype=jnp.int32)
                matrices.append(
                    lax.optimization_barrier(
                        screened(
                            lax.dynamic_slice_in_dim(geometry, row_at, size, 1),
                            lax.dynamic_slice_in_dim(geometry, col_at, size, 1),
                            offsets[:, None] == offsets[None, :] if diagonal else None,
                        )
                    )
                )

            def partial_image(vectors):
                partial = jnp.zeros_like(vectors)
                for matrix, (row_at, col_at, size, diagonal) in zip(matrices, starts):
                    col_part = lax.dynamic_slice_in_dim(vectors, col_at, size, 1)
                    forward = jnp.sum(matrix[None, :, :] * col_part[:, None, :], 2)
                    partial = lax.dynamic_update_slice_in_dim(
                        partial, lax.dynamic_slice_in_dim(partial, row_at, size, 1) + forward, row_at, 1
                    )
                    if not diagonal:
                        row_part = lax.dynamic_slice_in_dim(vectors, row_at, size, 1)
                        backward = jnp.sum(matrix[None, :, :] * row_part[:, :, None], 1)
                        partial = lax.dynamic_update_slice_in_dim(
                            partial, lax.dynamic_slice_in_dim(partial, col_at, size, 1) + backward, col_at, 1
                        )
                return partial

            def operate(vectors):
                partial = partial_image(vectors)
                return partial + lax.ppermute(partial, everyone, partner)

            def curvature(vectors):
                mine = 0.0
                for matrix, (row_at, col_at, size, diagonal) in zip(matrices, starts):
                    col_part = lax.dynamic_slice_in_dim(vectors, col_at, size, 1)
                    row_part = lax.dynamic_slice_in_dim(vectors, row_at, size, 1)
                    term = jnp.sum(row_part * jnp.sum(matrix[None, :, :] * col_part[:, None, :], 2), 1)
                    mine = mine + (term if diagonal else 2.0 * term)
                return mine + lax.ppermute(mine, everyone, partner)
        else:
            matrix = screened(row_geometry, geometry, row_index[:, None] == col_index[None, :])

            def operate(vectors):
                return assemble(jnp.sum(matrix[None, :, :] * vectors[:, None, :], 2))

            def curvature(vectors):
                return jnp.sum(vectors * operate(vectors), 1)

        rhs = jnp.stack([-geometry[4], jnp.ones((atoms,), jnp.float32)])
        solution = jnp.zeros_like(rhs)
        resid = rhs
        direction = rhs
        norm_now = jnp.sum(resid * resid, 1)
        own_index = me * per_brick + jnp.arange(per_brick, dtype=jnp.int32)
        for iteration in range(ITERS - 1):
            image = operate(direction)
            step_size = norm_now / jnp.sum(direction * image, 1)
            solution = solution + step_size[:, None] * direction
            resid = resid - step_size[:, None] * image
            norm_next = jnp.sum(resid * resid, 1)
            direction = resid + (norm_next / norm_now)[:, None] * direction
            norm_now = norm_next
        fields = pulling_fields(
            own, geometry, own_index[:, None] == col_index[None, :],
            [solution[0], solution[1], direction[0], direction[1]],
        ).reshape(2, 2, 3, per_brick)
        own_solution = lax.dynamic_slice_in_dim(solution, me * per_brick, per_brick, 1)
        own_direction = lax.dynamic_slice_in_dim(direction, me * per_brick, per_brick, 1)
        solution_sums = jnp.sum(solution, 1)
        direction_sums = jnp.sum(direction, 1)
        last_curvature = curvature(direction)
        step_size = norm_now / last_curvature
        totals = solution_sums + step_size * direction_sums
        weights = jnp.where(jnp.arange(2) == 0, 1.0, -(totals[::-1] / totals))
        own_charges = jnp.sum(weights[:, None] * (own_solution + step_size[:, None] * own_direction), 0)
        field = jnp.sum(
            weights[:, None, None] * (fields[0] + step_size[:, None, None] * fields[1]), 0
        )
        forces = (own_charges[None, :] * field).reshape(3, 1, 1, per_brick)
        return (own_charges.reshape(1, 1, per_brick), forces)

    return shards


def solution(mesh):
    in_specs = (
        P(None, "row", "col", None),
        P("row", "col", None),
        P(None, "row", "col", None),
        P(),
        P(),
        P(),
    )
    out_specs = (P("row", "col", None), P(None, "row", "col", None))
    shards = make_shards(mesh.shape["row"], mesh.shape["col"])
    return jax.shard_map(shards, mesh=mesh, in_specs=in_specs, out_specs=out_specs, check_vma=False)
```
